512 devices in a mesh: gx: 32 (over x, z), gy: 16 (over y, core).
Axes of the slice: x: 4, y: 8, z: 8, core: 2. Of those that a mesh axis runs over, the one named last changes fastest.
Arguments:
- start_disp: float32 [6, 3, 128, 128, 128], P(None, None, 'gx', 'gy'), may hold values from -6 to 6
- bone_mask: int32 [128, 128, 128], P('gx', 'gy'), may hold values from 0 to 1, as said below
- density: float32 [128, 128, 128], P('gx', 'gy'), may hold values from 0.3 to 1
- load_nodes: int32 [32, 16, 6, 32], P('gx', 'gy'), may hold values from 0 to 31
- load_forces: float32 [32, 16, 6, 3, 32], P('gx', 'gy'), may hold values from -12 to 12
Outputs:
- displacement: float32 [6, 3, 128, 128, 128], P(None, None, 'gx', 'gy')
- new_density: float32 [128, 128, 128], P('gx', 'gy')
The draws below stay inside these ranges and needn't reach their ends.
Inputs may be any that keep to these rules, and one draw needn't show every extreme that they name: `bone_mask`: 1 marks a bone voxel.
All inputs are finite; a program needn't handle non-finite values.
Results may differ from the reference program's by a relative error of at most 0.0001.
Values sent between devices are 32-bit elements; how exact they have to be, the bound alone decides.
No kernel may reach another device: no remote copies, remote signals or barrier semaphores. Data moves between devices by JAX's collectives and lax.ppermute only.
A program may use at most 64 MiB of HBM per device.

```python
import jax
import jax.numpy as jnp
import numpy as np
from jax import lax

CX = 4
CY = 8
CASES = 6
NLOAD = 32
ITERS = 1
NX = 128
NY = 128
NZ = 128
N_GX = 32
N_GY = 16


def draw_bone_mask(key, part):
    dice_rolls = jax.random.randint(key, (NX, NY, NZ), 0, 1000, dtype=jnp.int32)
    row_x = jnp.arange(NX, dtype=jnp.int32)[:, None, None]
    row_y = jnp.arange(NY, dtype=jnp.int32)[None, :, None]
    threshold = 60 + 120 * row_x // NX + 120 * row_y // NY
    return (dice_rolls < threshold).astype(jnp.int32)


def set_ends(result, stream_key, least, largest):
    dims = result.shape
    spot = [jax.random.randint(jax.random.fold_in(stream_key, axis), (), 0, dims[axis]) for axis in range(len(dims))]
    result = result.at[tuple(spot)].set(least)
    longest = dims.index(max(dims))
    spot[longest] = (spot[longest] + 1) % dims[longest]
    return result.at[tuple(spot)].set(largest)


def block_scale(stream_key, dims, cuts, least, high):
    loudness, own = 1.0, jax.random.fold_in(stream_key, 6)
    for position, blocks in cuts:
        draws = jnp.exp(jax.random.uniform(jax.random.fold_in(own, position), (blocks,), jnp.float32, least / len(cuts), high / len(cuts)))
        loudness = loudness * jnp.repeat(draws, dims[position] // blocks).reshape([-1 if axis == position else 1 for axis in range(len(dims))])
    return loudness


def bell_draw(key, dims, spread, limit, shards=(), held_as=jnp.bfloat16):
    array = jax.random.normal(key, dims, jnp.float32) * spread
    if len(shards) > 0:
        array = block_scale(key, dims, shards, -0.22, 0.18) * array
    return jnp.clip(array, min=-limit, max=limit).astype(held_as)


def setup_inputs(seed: int = 0) -> dict:
    seeds = jax.random.split(jax.random.key(seed), 6)
    start_disp = bell_draw(seeds[0], (CASES, 3, NX, NY, NZ), 1.0, 6.0, ((2, 32), (3, 16)), jnp.float32)
    bone_mask = draw_bone_mask(jax.random.fold_in(seeds[5], 71), 0)
    density = jnp.clip(0.3 + 0.7 * jax.random.uniform(seeds[2], (NX, NY, NZ), jnp.float32) ** block_scale(seeds[2], (NX, NY, NZ), ((0, 32), (1, 16)), -0.2, 0.2), 0.3, 1.0)
    load_nodes = set_ends(jax.random.randint(seeds[3], (N_GX, N_GY, CASES, NLOAD), 0, CX * CY), jax.random.fold_in(seeds[3], 1), 0, (CX * CY) - 1).astype(jnp.int32)
    load_forces = bell_draw(seeds[4], (N_GX, N_GY, CASES, 3, NLOAD), 2.0, 12.0, ((0, 32), (1, 16)), jnp.float32)
    return {"start_disp": start_disp, "bone_mask": bone_mask, "density": density, "load_nodes": load_nodes, "load_forces": load_forces}


spring = 0.1
poisson = 0.3
blur_sigma = 2.0
density_cap = 1.0
mean_eps = 1e-06
highest = lax.Precision.HIGHEST

def hex_stiffness():
    lame_first = poisson / ((1.0 + poisson) * (1.0 - 2.0 * poisson))
    shear_mod = 1.0 / (2.0 * (1.0 + poisson))
    elastic = np.zeros((6, 6))
    elastic[:3, :3] = lame_first
    for axis_id in range(3):
        elastic[axis_id, axis_id] = lame_first + 2.0 * shear_mod
        elastic[axis_id + 3, axis_id + 3] = shear_mod
    points = [0.5 - 0.5 / np.sqrt(3.0), 0.5 + 0.5 / np.sqrt(3.0)]
    stiffness = np.zeros((24, 24))
    for point_x in points:
        for point_y in points:
            for point_z in points:
                coords = (point_x, point_y, point_z)
                strain = np.zeros((6, 24))
                for corner in range(8):
                    offsets = (corner // 4, corner // 2 % 2, corner % 2)
                    shapes = [coords[axis_id] if offsets[axis_id] == 1 else 1.0 - coords[axis_id] for axis_id in range(3)]
                    slopes = [1.0 if offsets[axis_id] == 1 else -1.0 for axis_id in range(3)]
                    grad_x = slopes[0] * shapes[1] * shapes[2]
                    grad_y = shapes[0] * slopes[1] * shapes[2]
                    grad_z = shapes[0] * shapes[1] * slopes[2]
                    column = 3 * corner
                    strain[0, column] = grad_x
                    strain[1, column + 1] = grad_y
                    strain[2, column + 2] = grad_z
                    strain[3, column] = grad_y
                    strain[3, column + 1] = grad_x
                    strain[4, column + 1] = grad_z
                    strain[4, column + 2] = grad_y
                    strain[5, column] = grad_z
                    strain[5, column + 2] = grad_x
                stiffness += 0.125 * strain.T @ elastic @ strain
    return stiffness

def blur_weights():
    offsets = np.arange(9) - 4.0
    unscaled = np.exp(-offsets * offsets / (2.0 * blur_sigma * blur_sigma))
    return [float(entry) for entry in unscaled / unscaled.sum()]

def blur_valid(values, axis_id, extent):
    weights = blur_weights()
    summed = weights[0] * lax.slice_in_dim(values, 0, extent, axis=axis_id)
    for tap_index in range(1, 9):
        summed = summed + weights[tap_index] * lax.slice_in_dim(values, tap_index, tap_index + extent, axis=axis_id)
    return summed

def element_disp(node_field):
    size_x = node_field.shape[1] - 1
    size_y = node_field.shape[2] - 1
    size_z = node_field.shape[3] - 1
    corners = []
    for corner in range(8):
        off_x, off_y, off_z = (corner // 4, corner // 2 % 2, corner % 2)
        corners.append(node_field[:, off_x:off_x + size_x, off_y:off_y + size_y, off_z:off_z + size_z])
    return jnp.stack(corners).reshape(24, size_x, size_y, size_z)

def element_forces(node_field, modulus, stiffness):
    local_disp = element_disp(node_field)
    local_force = jnp.einsum('ij,jabc->iabc', stiffness, local_disp, precision=highest) * modulus
    local_force = local_force.reshape((8, 3) + modulus.shape)
    summed = jnp.zeros_like(node_field)
    for corner in range(8):
        off_x, off_y, off_z = (corner // 4, corner // 2 % 2, corner % 2)
        summed = summed + jnp.pad(local_force[corner], ((0, 0), (off_x, 1 - off_x), (off_y, 1 - off_y), (off_z, 1 - off_z)))
    return summed

def element_energy(node_field, stiffness):
    local_disp = element_disp(node_field)
    local_force = jnp.einsum('ij,jabc->iabc', stiffness, local_disp, precision=highest)
    return lax.optimization_barrier(jnp.sum(local_disp * local_force, axis=0))

def apply_operator(field, modulus, stiffness):
    padded = jnp.pad(field, ((0, 0), (0, 0), (0, 1), (0, 1), (0, 1)))
    forces = lax.map(lambda case_field: element_forces(case_field, modulus, stiffness), padded)
    return forces[:, :, :-1, :-1, :-1] + spring * field

def local_gram(left_field, right_field):
    return jnp.einsum('iabcd,jabcd->ij', left_field, right_field, precision=highest)

def mix_cases(field, coeffs):
    return jnp.einsum('kabcd,kj->jabcd', field, coeffs, precision=highest)

def solve_spd(matrix, rhs_matrix):
    factor = jnp.linalg.cholesky(matrix)
    matrix_order = matrix.shape[0]
    forward = []
    for row_index in range(matrix_order):
        partial_sum = rhs_matrix[row_index]
        for col_index in range(row_index):
            partial_sum = partial_sum - factor[row_index, col_index] * forward[col_index]
        forward.append(partial_sum / factor[row_index, row_index])
    backward = [None] * matrix_order
    for row_index in reversed(range(matrix_order)):
        partial_sum = forward[row_index]
        for col_index in range(row_index + 1, matrix_order):
            partial_sum = partial_sum - factor[col_index, row_index] * backward[col_index]
        backward[row_index] = partial_sum / factor[row_index, row_index]
    return jnp.stack(backward)

def top_loads(load_nodes, load_forces):
    slot_ids = jnp.arange(CX * CY, dtype=jnp.int32)
    matches = (load_nodes[..., None] == slot_ids).astype(jnp.float32)
    top_plane = jnp.einsum('abcls,abckl->abcks', matches, load_forces, precision=highest)
    top_plane = top_plane.reshape(N_GX, N_GY, CASES, 3, CX, CY)
    return top_plane.transpose(2, 3, 0, 4, 1, 5).reshape(CASES, 3, N_GX * CX, N_GY * CY)

def reference(start_disp, bone_mask, density, load_nodes, load_forces):
    stiffness = jnp.asarray(hex_stiffness(), jnp.float32)
    modulus = bone_mask.astype(jnp.float32) * density * density
    top_plane = top_loads(load_nodes, load_forces)
    applied = apply_operator(start_disp, modulus, stiffness)
    residual = jnp.concatenate([-applied[..., :-1], (top_plane - applied[..., -1])[..., None]], axis=4)
    solution = start_disp
    direction = residual
    norm_now = local_gram(residual, residual)
    for step_index in range(ITERS):
        applied = apply_operator(direction, modulus, stiffness)
        step_alpha = solve_spd(local_gram(direction, applied), norm_now)
        solution = solution + mix_cases(direction, step_alpha)
        residual = residual - mix_cases(applied, step_alpha)
        if step_index + 1 < ITERS:
            norm_next = local_gram(residual, residual)
            step_beta = solve_spd(norm_now, norm_next)
            direction = residual + mix_cases(direction, step_beta)
            norm_now = norm_next
    padded = jnp.pad(solution, ((0, 0), (0, 0), (0, 1), (0, 1), (0, 1)))
    energy = lax.optimization_barrier(jnp.sum(lax.map(lambda case_field: element_energy(case_field, stiffness), padded), axis=0))
    stimulus = modulus * energy
    smooth = blur_valid(jnp.pad(stimulus, ((4, 4), (0, 0), (0, 0))), 0, stimulus.shape[0])
    smooth = blur_valid(jnp.pad(smooth, ((0, 0), (4, 4), (0, 0))), 1, stimulus.shape[1])
    smooth = blur_valid(jnp.pad(smooth, ((0, 0), (0, 0), (4, 4))), 2, stimulus.shape[2])
    mean_stim = jnp.sum(smooth) / (NX * NY * NZ)
    new_density = jnp.minimum(density * (0.5 + 0.5 * smooth / (mean_stim + mean_eps)), density_cap)
    return (solution, new_density)
```

```python
import jax
import jax.numpy as jnp
import numpy as np
from jax import lax
from jax.sharding import PartitionSpec as P

spring = 0.1
poisson = 0.3
blur_sigma = 2.0
density_cap = 1.0
mean_eps = 1e-06
highest = lax.Precision.HIGHEST


def from_behind(block, axis, distance):
    devices = range(lax.axis_size(axis))
    route = [(i - distance, i) for i in devices if i - distance in devices]
    return lax.ppermute(block, axis, route)


def with_halo(cells, sides, width):
    for axis, dim in sides:
        count = lax.axis_size(axis)
        ends = count - 1
        head = lax.slice_in_dim(cells, 0, width, axis=dim)
        tail = lax.slice_in_dim(cells, cells.shape[dim] - width, cells.shape[dim], axis=dim)
        cells = jnp.concatenate(
            [
                lax.ppermute(tail, axis, [(i, (i + 1) % count) for i in range(ends)]),
                cells,
                lax.ppermute(head, axis, [((i + 1) % count, i) for i in range(ends)]),
            ],
            axis=dim,
        )
    return cells


def hex_stiffness():
    lame_first = poisson / ((1.0 + poisson) * (1.0 - 2.0 * poisson))
    shear_mod = 1.0 / (2.0 * (1.0 + poisson))
    elastic = np.zeros((6, 6))
    elastic[:3, :3] = lame_first
    for axis_id in range(3):
        elastic[axis_id, axis_id] = lame_first + 2.0 * shear_mod
        elastic[axis_id + 3, axis_id + 3] = shear_mod
    points = [0.5 - 0.5 / np.sqrt(3.0), 0.5 + 0.5 / np.sqrt(3.0)]
    stiffness = np.zeros((24, 24))
    for point_x in points:
        for point_y in points:
            for point_z in points:
                coords = (point_x, point_y, point_z)
                strain = np.zeros((6, 24))
                for corner in range(8):
                    offsets = (corner // 4, corner // 2 % 2, corner % 2)
                    shapes = [
                        coords[axis_id] if offsets[axis_id] == 1 else 1.0 - coords[axis_id]
                        for axis_id in range(3)
                    ]
                    slopes = [1.0 if offsets[axis_id] == 1 else -1.0 for axis_id in range(3)]
                    grad_x = slopes[0] * shapes[1] * shapes[2]
                    grad_y = shapes[0] * slopes[1] * shapes[2]
                    grad_z = shapes[0] * shapes[1] * slopes[2]
                    column = 3 * corner
                    strain[0, column] = grad_x
                    strain[1, column + 1] = grad_y
                    strain[2, column + 2] = grad_z
                    strain[3, column] = grad_y
                    strain[3, column + 1] = grad_x
                    strain[4, column + 1] = grad_z
                    strain[4, column + 2] = grad_y
                    strain[5, column] = grad_z
                    strain[5, column + 2] = grad_x
                stiffness += 0.125 * strain.T @ elastic @ strain
    return stiffness


def blur_weights():
    offsets = np.arange(9) - 4.0
    unscaled = np.exp(-offsets * offsets / (2.0 * blur_sigma * blur_sigma))
    return [float(entry) for entry in unscaled / unscaled.sum()]


def blur_valid(values, axis_id, extent):
    weights = blur_weights()
    summed = weights[0] * lax.slice_in_dim(values, 0, extent, axis=axis_id)
    for tap_index in range(1, 9):
        summed = summed + weights[tap_index] * lax.slice_in_dim(
            values, tap_index, tap_index + extent, axis=axis_id
        )
    return summed


def element_disp(node_field):
    size_x = node_field.shape[1] - 1
    size_y = node_field.shape[2] - 1
    size_z = node_field.shape[3] - 1
    corners = []
    for corner in range(8):
        off_x, off_y, off_z = (corner // 4, corner // 2 % 2, corner % 2)
        corners.append(
            node_field[:, off_x : off_x + size_x, off_y : off_y + size_y, off_z : off_z + size_z]
        )
    return jnp.stack(corners).reshape(24, size_x, size_y, size_z)


def cases_disp(node_field):
    size_x = node_field.shape[2] - 1
    size_y = node_field.shape[3] - 1
    size_z = node_field.shape[4] - 1
    corners = []
    for corner in range(8):
        off_x, off_y, off_z = (corner // 4, corner // 2 % 2, corner % 2)
        corners.append(
            node_field[:, :, off_x : off_x + size_x, off_y : off_y + size_y, off_z : off_z + size_z]
        )
    return jnp.stack(corners, axis=1).reshape(
        (node_field.shape[0], 24, size_x, size_y, size_z)
    )


def element_forces(node_field, modulus, stiffness):
    local_disp = cases_disp(node_field)
    local_force = jnp.einsum("ij,cjabd->ciabd", stiffness, local_disp, precision=highest) * modulus
    local_force = local_force.reshape((node_field.shape[0], 8, 3) + modulus.shape)
    summed = jnp.zeros_like(node_field)
    for corner in range(8):
        off_x, off_y, off_z = (corner // 4, corner // 2 % 2, corner % 2)
        summed = summed + jnp.pad(
            local_force[:, corner],
            ((0, 0), (0, 0), (off_x, 1 - off_x), (off_y, 1 - off_y), (off_z, 1 - off_z)),
        )
    return summed


def element_energy(node_field, stiffness):
    local_disp = cases_disp(node_field)
    local_force = jnp.einsum("ij,cjabd->ciabd", stiffness, local_disp, precision=highest)
    return jnp.sum(local_disp * local_force, axis=(0, 1))


def local_gram(left_field, right_field):
    return jnp.einsum("iabcd,jabcd->ij", left_field, right_field, precision=highest)


def tree_sum(value):
    for axis in ("gy", "gx"):
        count = lax.axis_size(axis)
        if count & (count - 1):
            value = lax.psum(value, axis)
            continue
        step = 1
        while step < count:
            value = value + lax.ppermute(value, axis, [(i, i ^ step) for i in range(count)])
            step *= 2
    return value


def mix_cases(field, coeffs):
    return jnp.einsum("kabcd,kj->jabcd", field, coeffs, precision=highest)


def solve_spd(matrix, rhs_matrix):
    factor = jnp.linalg.cholesky(matrix)
    forward = lax.linalg.triangular_solve(factor, rhs_matrix, left_side=True, lower=True)
    return lax.linalg.triangular_solve(
        factor, forward, left_side=True, lower=True, transpose_a=True
    )


def solve_spd_rows(matrix, rhs_matrix):
    factor = jnp.linalg.cholesky(matrix)
    matrix_order = matrix.shape[0]
    forward = []
    for row_index in range(matrix_order):
        partial_sum = rhs_matrix[row_index]
        for col_index in range(row_index):
            partial_sum = partial_sum - factor[row_index, col_index] * forward[col_index]
        forward.append(partial_sum / factor[row_index, row_index])
    backward = [None] * matrix_order
    for row_index in reversed(range(matrix_order)):
        partial_sum = forward[row_index]
        for col_index in range(row_index + 1, matrix_order):
            partial_sum = partial_sum - factor[col_index, row_index] * backward[col_index]
        backward[row_index] = partial_sum / factor[row_index, row_index]
    return jnp.stack(backward)


def pad_upper_z(field):
    return jnp.pad(field, ((0, 0), (0, 0), (0, 0), (0, 0), (0, 1)))


def gather_upper(field):
    from_x = from_behind(field[:, :, :1], "gx", -1)
    widened = jnp.concatenate([field, from_x], axis=2)
    from_y = from_behind(widened[:, :, :, :1], "gy", -1)
    return jnp.concatenate([widened, from_y], axis=3)


def return_lower(forces):
    size_x = forces.shape[2] - 1
    size_y = forces.shape[3] - 1
    to_y = from_behind(forces[:, :, :, size_y:], "gy", 1)
    kept = forces[:, :, :, :size_y]
    kept = jnp.concatenate([kept[:, :, :, :1] + to_y, kept[:, :, :, 1:]], axis=3)
    to_x = from_behind(kept[:, :, size_x:], "gx", 1)
    kept = kept[:, :, :size_x]
    return jnp.concatenate([kept[:, :, :1] + to_x, kept[:, :, 1:]], axis=2)


def on_device(start_disp, bone_mask, density, load_nodes, load_forces):
    stiffness = jnp.asarray(hex_stiffness(), jnp.float32)
    modulus = bone_mask.astype(jnp.float32) * density * density
    case_count = start_disp.shape[0]
    size_x = start_disp.shape[2]
    size_y = start_disp.shape[3]
    size_z = start_disp.shape[4]

    def apply_operator(field):
        node_field = pad_upper_z(gather_upper(field))
        forces = element_forces(node_field, modulus, stiffness)
        return return_lower(forces[..., :-1]) + spring * field, node_field

    slot_ids = jnp.arange(size_x * size_y, dtype=jnp.int32)
    matches = (load_nodes[0, 0][:, :, None] == slot_ids).astype(jnp.float32)
    top_plane = jnp.einsum("cls,ckl->cks", matches, load_forces[0, 0], precision=highest).reshape(
        case_count, 3, size_x, size_y
    )
    applied, start_nodes = apply_operator(start_disp)
    residual = jnp.concatenate(
        [-applied[..., :-1], (top_plane - applied[..., -1])[..., None]], axis=4
    )
    applied, residual_nodes = apply_operator(residual)
    grams = tree_sum(
        jnp.stack([local_gram(residual, residual), local_gram(residual, applied)])
    )
    norm_now = grams[0]
    step_alpha = solve_spd(grams[1], norm_now)
    solution = start_disp + mix_cases(residual, step_alpha)
    node_field = start_nodes + mix_cases(residual_nodes, step_alpha)
    energy = element_energy(node_field, stiffness)
    stimulus = modulus * energy
    smooth = blur_valid(with_halo(stimulus, (("gx", 0),), 4), 0, size_x)
    smooth = blur_valid(with_halo(smooth, (("gy", 1),), 4), 1, size_y)
    smooth = blur_valid(jnp.pad(smooth, ((0, 0), (0, 0), (4, 4))), 2, size_z)
    summed = tree_sum(jnp.sum(smooth))
    mean_stim = summed / (size_x * size_y * size_z * lax.axis_size("gx") * lax.axis_size("gy"))
    new_density = jnp.minimum(density * (0.5 + 0.5 * smooth / (mean_stim + mean_eps)), density_cap)
    return (solution, new_density)


def solution(mesh):
    return jax.shard_map(
        on_device,
        mesh=mesh,
        in_specs=(
            P(None, None, "gx", "gy", None),
            P("gx", "gy", None),
            P("gx", "gy", None),
            P("gx", "gy", None, None),
            P("gx", "gy", None, None, None),
        ),
        out_specs=(P(None, None, "gx", "gy", None), P("gx", "gy", None)),
        check_vma=False,
    )
```

```python
import jax
import jax.numpy as jnp
import numpy as np
from jax import lax
from jax.sharding import PartitionSpec as P

spring = 0.1
poisson = 0.3
blur_sigma = 2.0
density_cap = 1.0
mean_eps = 1e-06
highest = lax.Precision.HIGHEST


def from_behind(block, axis, distance):
    devices = range(lax.axis_size(axis))
    route = [(i - distance, i) for i in devices if i - distance in devices]
    return lax.ppermute(block, axis, route)


def with_halo(cells, sides, width):
    for axis, dim in sides:
        count = lax.axis_size(axis)
        ends = count - 1
        head = lax.slice_in_dim(cells, 0, width, axis=dim)
        tail = lax.slice_in_dim(cells, cells.shape[dim] - width, cells.shape[dim], axis=dim)
        cells = jnp.concatenate(
            [
                lax.ppermute(tail, axis, [(i, (i + 1) % count) for i in range(ends)]),
                cells,
                lax.ppermute(head, axis, [((i + 1) % count, i) for i in range(ends)]),
            ],
            axis=dim,
        )
    return cells


def hex_stiffness():
    lame_first = poisson / ((1.0 + poisson) * (1.0 - 2.0 * poisson))
    shear_mod = 1.0 / (2.0 * (1.0 + poisson))
    elastic = np.zeros((6, 6))
    elastic[:3, :3] = lame_first
    for axis_id in range(3):
        elastic[axis_id, axis_id] = lame_first + 2.0 * shear_mod
        elastic[axis_id + 3, axis_id + 3] = shear_mod
    points = [0.5 - 0.5 / np.sqrt(3.0), 0.5 + 0.5 / np.sqrt(3.0)]
    stiffness = np.zeros((24, 24))
    for point_x in points:
        for point_y in points:
            for point_z in points:
                coords = (point_x, point_y, point_z)
                strain = np.zeros((6, 24))
                for corner in range(8):
                    offsets = (corner // 4, corner // 2 % 2, corner % 2)
                    shapes = [
                        coords[axis_id] if offsets[axis_id] == 1 else 1.0 - coords[axis_id]
                        for axis_id in range(3)
                    ]
                    slopes = [1.0 if offsets[axis_id] == 1 else -1.0 for axis_id in range(3)]
                    grad_x = slopes[0] * shapes[1] * shapes[2]
                    grad_y = shapes[0] * slopes[1] * shapes[2]
                    grad_z = shapes[0] * shapes[1] * slopes[2]
                    column = 3 * corner
                    strain[0, column] = grad_x
                    strain[1, column + 1] = grad_y
                    strain[2, column + 2] = grad_z
                    strain[3, column] = grad_y
                    strain[3, column + 1] = grad_x
                    strain[4, column + 1] = grad_z
                    strain[4, column + 2] = grad_y
                    strain[5, column] = grad_z
                    strain[5, column + 2] = grad_x
                stiffness += 0.125 * strain.T @ elastic @ strain
    return stiffness


def blur_weights():
    offsets = np.arange(9) - 4.0
    unscaled = np.exp(-offsets * offsets / (2.0 * blur_sigma * blur_sigma))
    return [float(entry) for entry in unscaled / unscaled.sum()]


def blur_valid(values, axis_id, extent):
    weights = blur_weights()
    summed = weights[0] * lax.slice_in_dim(values, 0, extent, axis=axis_id)
    for tap_index in range(1, 9):
        summed = summed + weights[tap_index] * lax.slice_in_dim(
            values, tap_index, tap_index + extent, axis=axis_id
        )
    return summed


def element_disp(node_field):
    size_x = node_field.shape[1] - 1
    size_y = node_field.shape[2] - 1
    size_z = node_field.shape[3] - 1
    corners = []
    for corner in range(8):
        off_x, off_y, off_z = (corner // 4, corner // 2 % 2, corner % 2)
        corners.append(
            node_field[:, off_x : off_x + size_x, off_y : off_y + size_y, off_z : off_z + size_z]
        )
    return jnp.stack(corners).reshape(24, size_x, size_y, size_z)


def cases_disp(node_field):
    size_x = node_field.shape[2] - 1
    size_y = node_field.shape[3] - 1
    size_z = node_field.shape[4] - 1
    corners = []
    for corner in range(8):
        off_x, off_y, off_z = (corner // 4, corner // 2 % 2, corner % 2)
        corners.append(
            node_field[:, :, off_x : off_x + size_x, off_y : off_y + size_y, off_z : off_z + size_z]
        )
    return jnp.stack(corners, axis=1).reshape(
        (node_field.shape[0], 24, size_x, size_y, size_z)
    )


def element_forces(node_field, modulus, stiffness):
    local_disp = cases_disp(node_field)
    local_force = jnp.einsum("ij,cjabd->ciabd", stiffness, local_disp, precision=highest) * modulus
    local_force = local_force.reshape((node_field.shape[0], 8, 3) + modulus.shape)
    summed = jnp.zeros_like(node_field)
    for corner in range(8):
        off_x, off_y, off_z = (corner // 4, corner // 2 % 2, corner % 2)
        summed = summed + jnp.pad(
            local_force[:, corner],
            ((0, 0), (0, 0), (off_x, 1 - off_x), (off_y, 1 - off_y), (off_z, 1 - off_z)),
        )
    return summed


def element_energy(node_field, stiffness):
    local_disp = cases_disp(node_field)
    local_force = jnp.einsum("ij,cjabd->ciabd", stiffness, local_disp, precision=highest)
    return jnp.sum(local_disp * local_force, axis=(0, 1))


def local_gram(left_field, right_field):
    return jnp.einsum("iabcd,jabcd->ij", left_field, right_field, precision=highest)


def tree_sum(value):
    for axis in ("gy", "gx"):
        count = lax.axis_size(axis)
        if count & (count - 1):
            value = lax.psum(value, axis)
            continue
        step = 1
        while step < count:
            value = value + lax.ppermute(value, axis, [(i, i ^ step) for i in range(count)])
            step *= 2
    return value


def mix_cases(field, coeffs):
    return jnp.einsum("kabcd,kj->jabcd", field, coeffs, precision=highest)


def solve_spd(matrix, rhs_matrix):
    factor = jnp.linalg.cholesky(matrix)
    forward = lax.linalg.triangular_solve(factor, rhs_matrix, left_side=True, lower=True)
    return lax.linalg.triangular_solve(
        factor, forward, left_side=True, lower=True, transpose_a=True
    )


def solve_spd_rows(matrix, rhs_matrix):
    factor = jnp.linalg.cholesky(matrix)
    matrix_order = matrix.shape[0]
    forward = []
    for row_index in range(matrix_order):
        partial_sum = rhs_matrix[row_index]
        for col_index in range(row_index):
            partial_sum = partial_sum - factor[row_index, col_index] * forward[col_index]
        forward.append(partial_sum / factor[row_index, row_index])
    backward = [None] * matrix_order
    for row_index in reversed(range(matrix_order)):
        partial_sum = forward[row_index]
        for col_index in range(row_index + 1, matrix_order):
            partial_sum = partial_sum - factor[col_index, row_index] * backward[col_index]
        backward[row_index] = partial_sum / factor[row_index, row_index]
    return jnp.stack(backward)


def pad_upper_z(field):
    return jnp.pad(field, ((0, 0), (0, 0), (0, 0), (0, 0), (0, 1)))


def gather_upper(field):
    from_x = from_behind(field[:, :, :1], "gx", -1)
    widened = jnp.concatenate([field, from_x], axis=2)
    from_y = from_behind(widened[:, :, :, :1], "gy", -1)
    return jnp.concatenate([widened, from_y], axis=3)


def return_lower(forces):
    size_x = forces.shape[2] - 1
    size_y = forces.shape[3] - 1
    to_y = from_behind(forces[:, :, :, size_y:], "gy", 1)
    kept = forces[:, :, :, :size_y]
    kept = jnp.concatenate([kept[:, :, :, :1] + to_y, kept[:, :, :, 1:]], axis=3)
    to_x = from_behind(kept[:, :, size_x:], "gx", 1)
    kept = kept[:, :, :size_x]
    return jnp.concatenate([kept[:, :, :1] + to_x, kept[:, :, 1:]], axis=2)


def on_device(start_disp, bone_mask, density, load_nodes, load_forces):
    stiffness = jnp.asarray(hex_stiffness(), jnp.float32)
    modulus = bone_mask.astype(jnp.float32) * density * density
    case_count = start_disp.shape[0]
    size_x = start_disp.shape[2]
    size_y = start_disp.shape[3]
    size_z = start_disp.shape[4]

    def apply_operator(field):
        node_field = pad_upper_z(gather_upper(field))
        forces = element_forces(node_field, modulus, stiffness)
        return return_lower(forces[..., :-1]) + spring * field, node_field

    slot_ids = jnp.arange(size_x * size_y, dtype=jnp.int32)
    matches = (load_nodes[0, 0][:, :, None] == slot_ids).astype(jnp.float32)
    top_plane = jnp.einsum("cls,ckl->cks", matches, load_forces[0, 0], precision=highest).reshape(
        case_count, 3, size_x, size_y
    )
    applied, start_nodes = apply_operator(start_disp)
    residual = jnp.concatenate(
        [-applied[..., :-1], (top_plane - applied[..., -1])[..., None]], axis=4
    )
    applied, residual_nodes = apply_operator(residual)
    blur_mass = modulus
    for dim, axis in ((0, "gx"), (1, "gy"), (2, None)):
        extent = modulus.shape[dim]
        places = lax.broadcasted_iota(jnp.int32, modulus.shape, dim)
        if axis is not None:
            places = places + lax.axis_index(axis) * extent
            extent = extent * lax.axis_size(axis)
        kept = jnp.zeros(modulus.shape, jnp.float32)
        for tap_index, weight in enumerate(blur_weights()):
            inside = (places + 4 - tap_index >= 0) & (places + 4 - tap_index < extent)
            kept = kept + jnp.where(inside, weight, 0.0)
        blur_mass = blur_mass * kept
    start_elems = cases_disp(start_nodes)
    start_loads = jnp.einsum("ij,cjabd->ciabd", stiffness, start_elems, precision=highest)
    residual_elems = cases_disp(residual_nodes)
    residual_loads = jnp.einsum(
        "ij,cjabd->ciabd", stiffness, residual_elems, precision=highest
    )
    start_energy = jnp.sum(start_elems * start_loads * blur_mass, axis=(1, 2, 3, 4))
    cross_energy = jnp.einsum(
        "iqabd,jqabd->ij", residual_elems, start_loads * blur_mass, precision=highest
    )
    residual_energy = jnp.einsum(
        "iqabd,jqabd->ij", residual_elems, residual_loads * blur_mass, precision=highest
    )
    grams = tree_sum(
        jnp.stack(
            [
                local_gram(residual, residual),
                local_gram(residual, applied),
                cross_energy,
                residual_energy,
                jnp.diag(start_energy),
            ]
        )
    )
    norm_now = grams[0]
    step_alpha = solve_spd(grams[1], norm_now)
    summed = (
        jnp.sum(grams[4])
        + 2.0 * jnp.sum(step_alpha * grams[2])
        + jnp.sum(step_alpha[:, None, :] * grams[3][:, :, None] * step_alpha[None, :, :])
    )
    solution = start_disp + mix_cases(residual, step_alpha)
    node_field = start_nodes + mix_cases(residual_nodes, step_alpha)
    energy = element_energy(node_field, stiffness)
    stimulus = modulus * energy
    smooth = blur_valid(with_halo(stimulus, (("gx", 0),), 4), 0, size_x)
    smooth = blur_valid(with_halo(smooth, (("gy", 1),), 4), 1, size_y)
    smooth = blur_valid(jnp.pad(smooth, ((0, 0), (0, 0), (4, 4))), 2, size_z)
    mean_stim = summed / (size_x * size_y * size_z * lax.axis_size("gx") * lax.axis_size("gy"))
    new_density = jnp.minimum(density * (0.5 + 0.5 * smooth / (mean_stim + mean_eps)), density_cap)
    return (solution, new_density)


def solution(mesh):
    return jax.shard_map(
        on_device,
        mesh=mesh,
        in_specs=(
            P(None, None, "gx", "gy", None),
            P("gx", "gy", None),
            P("gx", "gy", None),
            P("gx", "gy", None, None),
            P("gx", "gy", None, None, None),
        ),
        out_specs=(P(None, None, "gx", "gy", None), P("gx", "gy", None)),
        check_vma=False,
    )
```

```python
import jax
import jax.numpy as jnp
import numpy as np
from jax import lax
from jax.sharding import PartitionSpec as P

spring = 0.1
poisson = 0.3
blur_sigma = 2.0
density_cap = 1.0
mean_eps = 1e-06
highest = lax.Precision.HIGHEST


def from_behind(block, axis, distance):
    devices = range(lax.axis_size(axis))
    route = [(i - distance, i) for i in devices if i - distance in devices]
    return lax.ppermute(block, axis, route)


def with_halo(cells, sides, width):
    for axis, dim in sides:
        count = lax.axis_size(axis)
        ends = count - 1
        head = lax.slice_in_dim(cells, 0, width, axis=dim)
        tail = lax.slice_in_dim(cells, cells.shape[dim] - width, cells.shape[dim], axis=dim)
        cells = jnp.concatenate(
            [
                lax.ppermute(tail, axis, [(i, (i + 1) % count) for i in range(ends)]),
                cells,
                lax.ppermute(head, axis, [((i + 1) % count, i) for i in range(ends)]),
            ],
            axis=dim,
        )
    return cells


def hex_stiffness():
    lame_first = poisson / ((1.0 + poisson) * (1.0 - 2.0 * poisson))
    shear_mod = 1.0 / (2.0 * (1.0 + poisson))
    elastic = np.zeros((6, 6))
    elastic[:3, :3] = lame_first
    for axis_id in range(3):
        elastic[axis_id, axis_id] = lame_first + 2.0 * shear_mod
        elastic[axis_id + 3, axis_id + 3] = shear_mod
    points = [0.5 - 0.5 / np.sqrt(3.0), 0.5 + 0.5 / np.sqrt(3.0)]
    stiffness = np.zeros((24, 24))
    for point_x in points:
        for point_y in points:
            for point_z in points:
                coords = (point_x, point_y, point_z)
                strain = np.zeros((6, 24))
                for corner in range(8):
                    offsets = (corner // 4, corner // 2 % 2, corner % 2)
                    shapes = [
                        coords[axis_id] if offsets[axis_id] == 1 else 1.0 - coords[axis_id]
                        for axis_id in range(3)
                    ]
                    slopes = [1.0 if offsets[axis_id] == 1 else -1.0 for axis_id in range(3)]
                    grad_x = slopes[0] * shapes[1] * shapes[2]
                    grad_y = shapes[0] * slopes[1] * shapes[2]
                    grad_z = shapes[0] * shapes[1] * slopes[2]
                    column = 3 * corner
                    strain[0, column] = grad_x
                    strain[1, column + 1] = grad_y
                    strain[2, column + 2] = grad_z
                    strain[3, column] = grad_y
                    strain[3, column + 1] = grad_x
                    strain[4, column + 1] = grad_z
                    strain[4, column + 2] = grad_y
                    strain[5, column] = grad_z
                    strain[5, column + 2] = grad_x
                stiffness += 0.125 * strain.T @ elastic @ strain
    return stiffness


def blur_weights():
    offsets = np.arange(9) - 4.0
    unscaled = np.exp(-offsets * offsets / (2.0 * blur_sigma * blur_sigma))
    return [float(entry) for entry in unscaled / unscaled.sum()]


def blur_valid(values, axis_id, extent):
    weights = blur_weights()
    summed = weights[0] * lax.slice_in_dim(values, 0, extent, axis=axis_id)
    for tap_index in range(1, 9):
        summed = summed + weights[tap_index] * lax.slice_in_dim(
            values, tap_index, tap_index + extent, axis=axis_id
        )
    return summed


def element_disp(node_field):
    size_x = node_field.shape[1] - 1
    size_y = node_field.shape[2] - 1
    size_z = node_field.shape[3] - 1
    corners = []
    for corner in range(8):
        off_x, off_y, off_z = (corner // 4, corner // 2 % 2, corner % 2)
        corners.append(
            node_field[:, off_x : off_x + size_x, off_y : off_y + size_y, off_z : off_z + size_z]
        )
    return jnp.stack(corners).reshape(24, size_x, size_y, size_z)


def cases_disp(node_field):
    size_x = node_field.shape[2] - 1
    size_y = node_field.shape[3] - 1
    size_z = node_field.shape[4] - 1
    corners = []
    for corner in range(8):
        off_x, off_y, off_z = (corner // 4, corner // 2 % 2, corner % 2)
        corners.append(
            node_field[:, :, off_x : off_x + size_x, off_y : off_y + size_y, off_z : off_z + size_z]
        )
    return jnp.stack(corners, axis=1).reshape(
        (node_field.shape[0], 24, size_x, size_y, size_z)
    )


def element_forces(node_field, modulus, stiffness):
    local_disp = cases_disp(node_field)
    local_force = jnp.einsum("ij,cjabd->ciabd", stiffness, local_disp, precision=highest) * modulus
    local_force = local_force.reshape((node_field.shape[0], 8, 3) + modulus.shape)
    summed = jnp.zeros_like(node_field)
    for corner in range(8):
        off_x, off_y, off_z = (corner // 4, corner // 2 % 2, corner % 2)
        summed = summed + jnp.pad(
            local_force[:, corner],
            ((0, 0), (0, 0), (off_x, 1 - off_x), (off_y, 1 - off_y), (off_z, 1 - off_z)),
        )
    return summed


def element_energy(node_field, stiffness):
    local_disp = cases_disp(node_field)
    local_force = jnp.einsum("ij,cjabd->ciabd", stiffness, local_disp, precision=highest)
    return jnp.sum(local_disp * local_force, axis=(0, 1))


def local_gram(left_field, right_field):
    return jnp.einsum("iabcd,jabcd->ij", left_field, right_field, precision=highest)


def tree_sum(value):
    for axis in ("gy", "gx"):
        count = lax.axis_size(axis)
        if count & (count - 1):
            value = lax.psum(value, axis)
            continue
        step = 1
        while step < count:
            value = value + lax.ppermute(value, axis, [(i, i ^ step) for i in range(count)])
            step *= 2
    return value


def mix_cases(field, coeffs):
    return jnp.einsum("kabcd,kj->jabcd", field, coeffs, precision=highest)


def solve_spd(matrix, rhs_matrix):
    factor = jnp.linalg.cholesky(matrix)
    forward = lax.linalg.triangular_solve(factor, rhs_matrix, left_side=True, lower=True)
    return lax.linalg.triangular_solve(
        factor, forward, left_side=True, lower=True, transpose_a=True
    )


def solve_spd_rows(matrix, rhs_matrix):
    factor = jnp.linalg.cholesky(matrix)
    matrix_order = matrix.shape[0]
    forward = []
    for row_index in range(matrix_order):
        partial_sum = rhs_matrix[row_index]
        for col_index in range(row_index):
            partial_sum = partial_sum - factor[row_index, col_index] * forward[col_index]
        forward.append(partial_sum / factor[row_index, row_index])
    backward = [None] * matrix_order
    for row_index in reversed(range(matrix_order)):
        partial_sum = forward[row_index]
        for col_index in range(row_index + 1, matrix_order):
            partial_sum = partial_sum - factor[col_index, row_index] * backward[col_index]
        backward[row_index] = partial_sum / factor[row_index, row_index]
    return jnp.stack(backward)


def pad_upper_z(field):
    return jnp.pad(field, ((0, 0), (0, 0), (0, 0), (0, 0), (0, 1)))


def gather_upper(field):
    from_x = from_behind(field[:, :, :1], "gx", -1)
    widened = jnp.concatenate([field, from_x], axis=2)
    from_y = from_behind(widened[:, :, :, :1], "gy", -1)
    return jnp.concatenate([widened, from_y], axis=3)


def return_lower(forces):
    size_x = forces.shape[2] - 1
    size_y = forces.shape[3] - 1
    to_y = from_behind(forces[:, :, :, size_y:], "gy", 1)
    kept = forces[:, :, :, :size_y]
    kept = jnp.concatenate([kept[:, :, :, :1] + to_y, kept[:, :, :, 1:]], axis=3)
    to_x = from_behind(kept[:, :, size_x:], "gx", 1)
    kept = kept[:, :, :size_x]
    return jnp.concatenate([kept[:, :, :1] + to_x, kept[:, :, 1:]], axis=2)


def on_device(start_disp, bone_mask, density, load_nodes, load_forces):
    stiffness = jnp.asarray(hex_stiffness(), jnp.float32)
    modulus = bone_mask.astype(jnp.float32) * density * density
    case_count = start_disp.shape[0]
    size_x = start_disp.shape[2]
    size_y = start_disp.shape[3]
    size_z = start_disp.shape[4]

    def apply_operator(field):
        node_field = pad_upper_z(gather_upper(field))
        forces = element_forces(node_field, modulus, stiffness)
        return return_lower(forces[..., :-1]) + spring * field, node_field

    slot_ids = jnp.arange(size_x * size_y, dtype=jnp.int32)
    matches = (load_nodes[0, 0][:, :, None] == slot_ids).astype(jnp.float32)
    top_plane = jnp.einsum("cls,ckl->cks", matches, load_forces[0, 0], precision=highest).reshape(
        case_count, 3, size_x, size_y
    )
    applied, start_nodes = apply_operator(start_disp)
    residual = jnp.concatenate(
        [-applied[..., :-1], (top_plane - applied[..., -1])[..., None]], axis=4
    )
    applied, residual_nodes = apply_operator(residual)
    blur_mass = modulus
    for dim, axis in ((0, "gx"), (1, "gy"), (2, None)):
        extent = modulus.shape[dim]
        count = 1 if axis is None else lax.axis_size(axis)
        places = np.arange(extent * count)
        kept = np.zeros(extent * count)
        for tap_index, weight in enumerate(blur_weights()):
            inside = (places + 4 - tap_index >= 0) & (places + 4 - tap_index < extent * count)
            kept = kept + np.where(inside, weight, 0.0)
        kept = jnp.asarray(kept, jnp.float32)
        if axis is not None:
            kept = lax.dynamic_slice_in_dim(kept, lax.axis_index(axis) * extent, extent)
        shape = [1, 1, 1]
        shape[dim] = extent
        blur_mass = blur_mass * kept.reshape(shape)
    start_elems = cases_disp(start_nodes)
    start_loads = jnp.einsum("ij,cjabd->ciabd", stiffness, start_elems, precision=highest)
    residual_elems = cases_disp(residual_nodes)
    residual_loads = jnp.einsum(
        "ij,cjabd->ciabd", stiffness, residual_elems, precision=highest
    )
    start_energy = jnp.sum(start_elems * start_loads * blur_mass, axis=(1, 2, 3, 4))
    start_weighted = start_loads * blur_mass
    residual_weighted = residual_loads * blur_mass
    cross_energy = jnp.sum(
        residual_elems[:, None] * start_weighted[None, :], axis=(2, 3, 4, 5)
    )
    residual_energy = jnp.sum(
        residual_elems[:, None] * residual_weighted[None, :], axis=(2, 3, 4, 5)
    )
    grams = tree_sum(
        jnp.stack(
            [
                local_gram(residual, residual),
                local_gram(residual, applied),
                cross_energy,
                residual_energy,
                jnp.diag(start_energy),
            ]
        )
    )
    norm_now = grams[0]
    step_alpha = solve_spd(grams[1], norm_now)
    summed = (
        jnp.sum(grams[4])
        + 2.0 * jnp.sum(step_alpha * grams[2])
        + jnp.sum(step_alpha[:, None, :] * grams[3][:, :, None] * step_alpha[None, :, :])
    )
    solution = start_disp + mix_cases(residual, step_alpha)
    node_field = start_nodes + mix_cases(residual_nodes, step_alpha)
    energy = element_energy(node_field, stiffness)
    stimulus = modulus * energy
    smooth = blur_valid(with_halo(stimulus, (("gx", 0),), 4), 0, size_x)
    smooth = blur_valid(with_halo(smooth, (("gy", 1),), 4), 1, size_y)
    smooth = blur_valid(jnp.pad(smooth, ((0, 0), (0, 0), (4, 4))), 2, size_z)
    mean_stim = summed / (size_x * size_y * size_z * lax.axis_size("gx") * lax.axis_size("gy"))
    new_density = jnp.minimum(density * (0.5 + 0.5 * smooth / (mean_stim + mean_eps)), density_cap)
    return (solution, new_density)


def solution(mesh):
    return jax.shard_map(
        on_device,
        mesh=mesh,
        in_specs=(
            P(None, None, "gx", "gy", None),
            P("gx", "gy", None),
            P("gx", "gy", None),
            P("gx", "gy", None, None),
            P("gx", "gy", None, None, None),
        ),
        out_specs=(P(None, None, "gx", "gy", None), P("gx", "gy", None)),
        check_vma=False,
    )
```

```python
import jax
import jax.numpy as jnp
import numpy as np
from jax import lax
from jax.sharding import PartitionSpec as P

spring = 0.1
poisson = 0.3
blur_sigma = 2.0
density_cap = 1.0
mean_eps = 1e-06
highest = lax.Precision.HIGHEST


def from_behind(block, axis, distance):
    devices = range(lax.axis_size(axis))
    route = [(i - distance, i) for i in devices if i - distance in devices]
    return lax.ppermute(block, axis, route)


def with_halo(cells, sides, width):
    for axis, dim in sides:
        count = lax.axis_size(axis)
        ends = count - 1
        head = lax.slice_in_dim(cells, 0, width, axis=dim)
        tail = lax.slice_in_dim(cells, cells.shape[dim] - width, cells.shape[dim], axis=dim)
        cells = jnp.concatenate(
            [
                lax.ppermute(tail, axis, [(i, (i + 1) % count) for i in range(ends)]),
                cells,
                lax.ppermute(head, axis, [((i + 1) % count, i) for i in range(ends)]),
            ],
            axis=dim,
        )
    return cells


def hex_stiffness():
    lame_first = poisson / ((1.0 + poisson) * (1.0 - 2.0 * poisson))
    shear_mod = 1.0 / (2.0 * (1.0 + poisson))
    elastic = np.zeros((6, 6))
    elastic[:3, :3] = lame_first
    for axis_id in range(3):
        elastic[axis_id, axis_id] = lame_first + 2.0 * shear_mod
        elastic[axis_id + 3, axis_id + 3] = shear_mod
    points = [0.5 - 0.5 / np.sqrt(3.0), 0.5 + 0.5 / np.sqrt(3.0)]
    stiffness = np.zeros((24, 24))
    for point_x in points:
        for point_y in points:
            for point_z in points:
                coords = (point_x, point_y, point_z)
                strain = np.zeros((6, 24))
                for corner in range(8):
                    offsets = (corner // 4, corner // 2 % 2, corner % 2)
                    shapes = [
                        coords[axis_id] if offsets[axis_id] == 1 else 1.0 - coords[axis_id]
                        for axis_id in range(3)
                    ]
                    slopes = [1.0 if offsets[axis_id] == 1 else -1.0 for axis_id in range(3)]
                    grad_x = slopes[0] * shapes[1] * shapes[2]
                    grad_y = shapes[0] * slopes[1] * shapes[2]
                    grad_z = shapes[0] * shapes[1] * slopes[2]
                    column = 3 * corner
                    strain[0, column] = grad_x
                    strain[1, column + 1] = grad_y
                    strain[2, column + 2] = grad_z
                    strain[3, column] = grad_y
                    strain[3, column + 1] = grad_x
                    strain[4, column + 1] = grad_z
                    strain[4, column + 2] = grad_y
                    strain[5, column] = grad_z
                    strain[5, column + 2] = grad_x
                stiffness += 0.125 * strain.T @ elastic @ strain
    return stiffness


def blur_weights():
    offsets = np.arange(9) - 4.0
    unscaled = np.exp(-offsets * offsets / (2.0 * blur_sigma * blur_sigma))
    return [float(entry) for entry in unscaled / unscaled.sum()]


def blur_valid(values, axis_id, extent):
    weights = blur_weights()
    summed = weights[0] * lax.slice_in_dim(values, 0, extent, axis=axis_id)
    for tap_index in range(1, 9):
        summed = summed + weights[tap_index] * lax.slice_in_dim(
            values, tap_index, tap_index + extent, axis=axis_id
        )
    return summed


def element_disp(node_field):
    size_x = node_field.shape[1] - 1
    size_y = node_field.shape[2] - 1
    size_z = node_field.shape[3] - 1
    corners = []
    for corner in range(8):
        off_x, off_y, off_z = (corner // 4, corner // 2 % 2, corner % 2)
        corners.append(
            node_field[:, off_x : off_x + size_x, off_y : off_y + size_y, off_z : off_z + size_z]
        )
    return jnp.stack(corners).reshape(24, size_x, size_y, size_z)


def cases_disp(node_field):
    size_x = node_field.shape[2] - 1
    size_y = node_field.shape[3] - 1
    size_z = node_field.shape[4] - 1
    corners = []
    for corner in range(8):
        off_x, off_y, off_z = (corner // 4, corner // 2 % 2, corner % 2)
        corners.append(
            node_field[:, :, off_x : off_x + size_x, off_y : off_y + size_y, off_z : off_z + size_z]
        )
    return jnp.stack(corners, axis=1).reshape(
        (node_field.shape[0], 24, size_x, size_y, size_z)
    )


def element_forces(node_field, modulus, stiffness):
    local_disp = cases_disp(node_field)
    local_force = jnp.einsum("ij,cjabd->ciabd", stiffness, local_disp, precision=highest) * modulus
    local_force = local_force.reshape((node_field.shape[0], 8, 3) + modulus.shape)
    summed = jnp.zeros_like(node_field)
    for corner in range(8):
        off_x, off_y, off_z = (corner // 4, corner // 2 % 2, corner % 2)
        summed = summed + jnp.pad(
            local_force[:, corner],
            ((0, 0), (0, 0), (off_x, 1 - off_x), (off_y, 1 - off_y), (off_z, 1 - off_z)),
        )
    return summed


def element_energy(node_field, stiffness):
    local_disp = cases_disp(node_field)
    local_force = jnp.einsum("ij,cjabd->ciabd", stiffness, local_disp, precision=highest)
    return jnp.sum(local_disp * local_force, axis=(0, 1))


def local_gram(left_field, right_field):
    return jnp.einsum("iabcd,jabcd->ij", left_field, right_field, precision=highest)


def tree_sum(value):
    for axis in ("gy", "gx"):
        count = lax.axis_size(axis)
        if count & (count - 1):
            value = lax.psum(value, axis)
            continue
        step = 1
        while step < count:
            value = value + lax.ppermute(value, axis, [(i, i ^ step) for i in range(count)])
            step *= 2
    return value


def mix_cases(field, coeffs):
    return jnp.einsum("kabcd,kj->jabcd", field, coeffs, precision=highest)


def solve_spd(matrix, rhs_matrix):
    factor = jnp.linalg.cholesky(matrix)
    forward = lax.linalg.triangular_solve(factor, rhs_matrix, left_side=True, lower=True)
    return lax.linalg.triangular_solve(
        factor, forward, left_side=True, lower=True, transpose_a=True
    )


def solve_spd_rows(matrix, rhs_matrix):
    factor = jnp.linalg.cholesky(matrix)
    matrix_order = matrix.shape[0]
    forward = []
    for row_index in range(matrix_order):
        partial_sum = rhs_matrix[row_index]
        for col_index in range(row_index):
            partial_sum = partial_sum - factor[row_index, col_index] * forward[col_index]
        forward.append(partial_sum / factor[row_index, row_index])
    backward = [None] * matrix_order
    for row_index in reversed(range(matrix_order)):
        partial_sum = forward[row_index]
        for col_index in range(row_index + 1, matrix_order):
            partial_sum = partial_sum - factor[col_index, row_index] * backward[col_index]
        backward[row_index] = partial_sum / factor[row_index, row_index]
    return jnp.stack(backward)


def pad_upper_z(field):
    return jnp.pad(field, ((0, 0), (0, 0), (0, 0), (0, 0), (0, 1)))


def gather_upper(field):
    from_x = from_behind(field[:, :, :1], "gx", -1)
    widened = jnp.concatenate([field, from_x], axis=2)
    from_y = from_behind(widened[:, :, :, :1], "gy", -1)
    return jnp.concatenate([widened, from_y], axis=3)


def return_lower(forces):
    size_x = forces.shape[2] - 1
    size_y = forces.shape[3] - 1
    to_y = from_behind(forces[:, :, :, size_y:], "gy", 1)
    kept = forces[:, :, :, :size_y]
    kept = jnp.concatenate([kept[:, :, :, :1] + to_y, kept[:, :, :, 1:]], axis=3)
    to_x = from_behind(kept[:, :, size_x:], "gx", 1)
    kept = kept[:, :, :size_x]
    return jnp.concatenate([kept[:, :, :1] + to_x, kept[:, :, 1:]], axis=2)


def halo_both(cells, axis, dim, width):
    count = lax.axis_size(axis)
    head = lax.slice_in_dim(cells, 0, width, axis=dim)
    tail = lax.slice_in_dim(cells, cells.shape[dim] - width, cells.shape[dim], axis=dim)
    below = lax.ppermute(tail, axis, [(i, i + 1) for i in range(count - 1)])
    above = lax.ppermute(head, axis, [(i + 1, i) for i in range(count - 1)])
    return jnp.concatenate([below, cells, above], axis=dim)


def inside_mask(axis, extent, width, total):
    places = np.arange(extent + 2 * width) - width
    own = jnp.asarray(places, jnp.int32) + lax.axis_index(axis) * extent
    return ((own >= 0) & (own < total)).astype(jnp.float32)


def node_forces(node_field, modulus, stiffness):
    local_disp = cases_disp(node_field)
    local_load = jnp.einsum("ij,cjabd->ciabd", stiffness, local_disp, precision=highest)
    local_force = (local_load * modulus).reshape((node_field.shape[0], 8, 3) + modulus.shape)
    summed = jnp.zeros_like(node_field)
    for corner in range(8):
        off_x, off_y, off_z = (corner // 4, corner // 2 % 2, corner % 2)
        summed = summed + jnp.pad(
            local_force[:, corner],
            ((0, 0), (0, 0), (off_x, 1 - off_x), (off_y, 1 - off_y), (off_z, 1 - off_z)),
        )
    return summed[..., :-1], local_disp, local_load


def on_device(start_disp, bone_mask, density, load_nodes, load_forces):
    stiffness = jnp.asarray(hex_stiffness(), jnp.float32)
    modulus = bone_mask.astype(jnp.float32) * density * density
    case_count = start_disp.shape[0]
    size_x = start_disp.shape[2]
    size_y = start_disp.shape[3]
    size_z = start_disp.shape[4]
    count_x = lax.axis_size("gx")
    count_y = lax.axis_size("gy")
    fields = case_count * 3

    slot_ids = jnp.arange(size_x * size_y, dtype=jnp.int32)
    matches = (load_nodes[0, 0][:, :, None] == slot_ids).astype(jnp.float32)
    top_plane = jnp.einsum("cls,ckl->cks", matches, load_forces[0, 0], precision=highest).reshape(
        fields, size_x, size_y
    )
    packed_loads = jnp.pad(top_plane.transpose(1, 2, 0), ((0, 0), (0, 0), (0, size_z - fields)))
    packed = jnp.concatenate(
        [start_disp.reshape(fields, size_x, size_y, size_z), modulus[None], packed_loads[None]],
        axis=0,
    )
    packed = halo_both(halo_both(packed, "gx", 1, 2), "gy", 2, 2)
    wide_start = packed[:fields].reshape(case_count, 3, size_x + 4, size_y + 4, size_z)
    wide_modulus = packed[fields]
    wide_loads = packed[fields + 1, 1:-1, 1:-1, :fields].transpose(2, 0, 1)
    wide_loads = wide_loads.reshape(case_count, 3, size_x + 2, size_y + 2)

    start_nodes = pad_upper_z(wide_start)
    forces, start_elems, start_loads = node_forces(
        start_nodes, wide_modulus[:-1, :-1], stiffness
    )
    applied = forces[:, :, 1:-1, 1:-1] + spring * wide_start[:, :, 1:-1, 1:-1]
    keep = (
        inside_mask("gx", size_x, 1, size_x * count_x)[:, None, None]
        * inside_mask("gy", size_y, 1, size_y * count_y)[None, :, None]
    )
    residual_wide = (
        jnp.concatenate(
            [-applied[..., :-1], (wide_loads - applied[..., -1])[..., None]], axis=4
        )
        * keep
    )

    residual_nodes = pad_upper_z(residual_wide)
    forces, residual_elems, residual_loads = node_forces(
        residual_nodes, wide_modulus[1:-2, 1:-2], stiffness
    )
    residual = residual_wide[:, :, 1:-1, 1:-1]
    applied = forces[:, :, 1:-1, 1:-1] + spring * residual

    blur_mass = modulus
    for dim, axis in ((0, "gx"), (1, "gy"), (2, None)):
        extent = modulus.shape[dim]
        count = 1 if axis is None else lax.axis_size(axis)
        places = np.arange(extent * count)
        kept = np.zeros(extent * count)
        for tap_index, weight in enumerate(blur_weights()):
            inside = (places + 4 - tap_index >= 0) & (places + 4 - tap_index < extent * count)
            kept = kept + np.where(inside, weight, 0.0)
        kept = jnp.asarray(kept, jnp.float32)
        if axis is not None:
            kept = lax.dynamic_slice_in_dim(kept, lax.axis_index(axis) * extent, extent)
        shape = [1, 1, 1]
        shape[dim] = extent
        blur_mass = blur_mass * kept.reshape(shape)
    start_elems = start_elems[:, :, 2:-1, 2:-1]
    start_loads = start_loads[:, :, 2:-1, 2:-1]
    residual_elems = residual_elems[:, :, 1:, 1:]
    residual_loads = residual_loads[:, :, 1:, 1:]
    start_energy = jnp.sum(start_elems * start_loads * blur_mass, axis=(1, 2, 3, 4))
    start_weighted = start_loads * blur_mass
    residual_weighted = residual_loads * blur_mass
    cross_energy = jnp.sum(
        residual_elems[:, None] * start_weighted[None, :], axis=(2, 3, 4, 5)
    )
    residual_energy = jnp.sum(
        residual_elems[:, None] * residual_weighted[None, :], axis=(2, 3, 4, 5)
    )
    grams = tree_sum(
        jnp.stack(
            [
                local_gram(residual, residual),
                local_gram(residual, applied),
                cross_energy,
                residual_energy,
                jnp.diag(start_energy),
            ]
        )
    )
    norm_now = grams[0]
    step_alpha = solve_spd(grams[1], norm_now)
    summed = (
        jnp.sum(grams[4])
        + 2.0 * jnp.sum(step_alpha * grams[2])
        + jnp.sum(step_alpha[:, None, :] * grams[3][:, :, None] * step_alpha[None, :, :])
    )
    solution = start_disp + mix_cases(residual, step_alpha)
    node_field = start_nodes[:, :, 2:-1, 2:-1] + mix_cases(
        residual_nodes[:, :, 1:, 1:], step_alpha
    )
    energy = element_energy(node_field, stiffness)
    stimulus = modulus * energy
    smooth = blur_valid(with_halo(stimulus, (("gx", 0),), 4), 0, size_x)
    smooth = blur_valid(with_halo(smooth, (("gy", 1),), 4), 1, size_y)
    smooth = blur_valid(jnp.pad(smooth, ((0, 0), (0, 0), (4, 4))), 2, size_z)
    mean_stim = summed / (size_x * size_y * size_z * count_x * count_y)
    new_density = jnp.minimum(density * (0.5 + 0.5 * smooth / (mean_stim + mean_eps)), density_cap)
    return (solution, new_density)


def solution(mesh):
    return jax.shard_map(
        on_device,
        mesh=mesh,
        in_specs=(
            P(None, None, "gx", "gy", None),
            P("gx", "gy", None),
            P("gx", "gy", None),
            P("gx", "gy", None, None),
            P("gx", "gy", None, None, None),
        ),
        out_specs=(P(None, None, "gx", "gy", None), P("gx", "gy", None)),
        check_vma=False,
    )
```

```python
import jax
import jax.numpy as jnp
import numpy as np
from jax import lax
from jax.sharding import PartitionSpec as P

spring = 0.1
poisson = 0.3
blur_sigma = 2.0
density_cap = 1.0
mean_eps = 1e-06
highest = lax.Precision.HIGHEST


def from_behind(block, axis, distance):
    devices = range(lax.axis_size(axis))
    route = [(i - distance, i) for i in devices if i - distance in devices]
    return lax.ppermute(block, axis, route)


def with_halo(cells, sides, width):
    for axis, dim in sides:
        count = lax.axis_size(axis)
        ends = count - 1
        head = lax.slice_in_dim(cells, 0, width, axis=dim)
        tail = lax.slice_in_dim(cells, cells.shape[dim] - width, cells.shape[dim], axis=dim)
        cells = jnp.concatenate(
            [
                lax.ppermute(tail, axis, [(i, (i + 1) % count) for i in range(ends)]),
                cells,
                lax.ppermute(head, axis, [((i + 1) % count, i) for i in range(ends)]),
            ],
            axis=dim,
        )
    return cells


def hex_stiffness():
    lame_first = poisson / ((1.0 + poisson) * (1.0 - 2.0 * poisson))
    shear_mod = 1.0 / (2.0 * (1.0 + poisson))
    elastic = np.zeros((6, 6))
    elastic[:3, :3] = lame_first
    for axis_id in range(3):
        elastic[axis_id, axis_id] = lame_first + 2.0 * shear_mod
        elastic[axis_id + 3, axis_id + 3] = shear_mod
    points = [0.5 - 0.5 / np.sqrt(3.0), 0.5 + 0.5 / np.sqrt(3.0)]
    stiffness = np.zeros((24, 24))
    for point_x in points:
        for point_y in points:
            for point_z in points:
                coords = (point_x, point_y, point_z)
                strain = np.zeros((6, 24))
                for corner in range(8):
                    offsets = (corner // 4, corner // 2 % 2, corner % 2)
                    shapes = [
                        coords[axis_id] if offsets[axis_id] == 1 else 1.0 - coords[axis_id]
                        for axis_id in range(3)
                    ]
                    slopes = [1.0 if offsets[axis_id] == 1 else -1.0 for axis_id in range(3)]
                    grad_x = slopes[0] * shapes[1] * shapes[2]
                    grad_y = shapes[0] * slopes[1] * shapes[2]
                    grad_z = shapes[0] * shapes[1] * slopes[2]
                    column = 3 * corner
                    strain[0, column] = grad_x
                    strain[1, column + 1] = grad_y
                    strain[2, column + 2] = grad_z
                    strain[3, column] = grad_y
                    strain[3, column + 1] = grad_x
                    strain[4, column + 1] = grad_z
                    strain[4, column + 2] = grad_y
                    strain[5, column] = grad_z
                    strain[5, column + 2] = grad_x
                stiffness += 0.125 * strain.T @ elastic @ strain
    return stiffness


def blur_weights():
    offsets = np.arange(9) - 4.0
    unscaled = np.exp(-offsets * offsets / (2.0 * blur_sigma * blur_sigma))
    return [float(entry) for entry in unscaled / unscaled.sum()]


def blur_valid(values, axis_id, extent):
    weights = blur_weights()
    summed = weights[0] * lax.slice_in_dim(values, 0, extent, axis=axis_id)
    for tap_index in range(1, 9):
        summed = summed + weights[tap_index] * lax.slice_in_dim(
            values, tap_index, tap_index + extent, axis=axis_id
        )
    return summed


def element_disp(node_field):
    size_x = node_field.shape[1] - 1
    size_y = node_field.shape[2] - 1
    size_z = node_field.shape[3] - 1
    corners = []
    for corner in range(8):
        off_x, off_y, off_z = (corner // 4, corner // 2 % 2, corner % 2)
        corners.append(
            node_field[:, off_x : off_x + size_x, off_y : off_y + size_y, off_z : off_z + size_z]
        )
    return jnp.stack(corners).reshape(24, size_x, size_y, size_z)


def cases_disp(node_field):
    size_x = node_field.shape[2] - 1
    size_y = node_field.shape[3] - 1
    size_z = node_field.shape[4] - 1
    corners = []
    for corner in range(8):
        off_x, off_y, off_z = (corner // 4, corner // 2 % 2, corner % 2)
        corners.append(
            node_field[:, :, off_x : off_x + size_x, off_y : off_y + size_y, off_z : off_z + size_z]
        )
    return jnp.stack(corners, axis=1).reshape(
        (node_field.shape[0], 24, size_x, size_y, size_z)
    )


def element_forces(node_field, modulus, stiffness):
    local_disp = cases_disp(node_field)
    local_force = jnp.einsum("ij,cjabd->ciabd", stiffness, local_disp, precision=highest) * modulus
    local_force = local_force.reshape((node_field.shape[0], 8, 3) + modulus.shape)
    summed = jnp.zeros_like(node_field)
    for corner in range(8):
        off_x, off_y, off_z = (corner // 4, corner // 2 % 2, corner % 2)
        summed = summed + jnp.pad(
            local_force[:, corner],
            ((0, 0), (0, 0), (off_x, 1 - off_x), (off_y, 1 - off_y), (off_z, 1 - off_z)),
        )
    return summed


def element_energy(node_field, stiffness):
    local_disp = cases_disp(node_field)
    local_force = jnp.einsum("ij,cjabd->ciabd", stiffness, local_disp, precision=highest)
    return jnp.sum(local_disp * local_force, axis=(0, 1))


def local_gram(left_field, right_field):
    return jnp.einsum("iabcd,jabcd->ij", left_field, right_field, precision=highest)


def tree_sum(value):
    for axis in ("gy", "gx"):
        count = lax.axis_size(axis)
        copies = jnp.broadcast_to(value[None], (count,) + value.shape)
        value = jnp.sum(lax.all_to_all(copies, axis, 0, 0, tiled=False), axis=0)
    return value


def mix_cases(field, coeffs):
    return jnp.einsum("kabcd,kj->jabcd", field, coeffs, precision=highest)


def solve_spd(matrix, rhs_matrix):
    factor = jnp.linalg.cholesky(matrix)
    forward = lax.linalg.triangular_solve(factor, rhs_matrix, left_side=True, lower=True)
    return lax.linalg.triangular_solve(
        factor, forward, left_side=True, lower=True, transpose_a=True
    )


def solve_spd_rows(matrix, rhs_matrix):
    factor = jnp.linalg.cholesky(matrix)
    matrix_order = matrix.shape[0]
    forward = []
    for row_index in range(matrix_order):
        partial_sum = rhs_matrix[row_index]
        for col_index in range(row_index):
            partial_sum = partial_sum - factor[row_index, col_index] * forward[col_index]
        forward.append(partial_sum / factor[row_index, row_index])
    backward = [None] * matrix_order
    for row_index in reversed(range(matrix_order)):
        partial_sum = forward[row_index]
        for col_index in range(row_index + 1, matrix_order):
            partial_sum = partial_sum - factor[col_index, row_index] * backward[col_index]
        backward[row_index] = partial_sum / factor[row_index, row_index]
    return jnp.stack(backward)


def pad_upper_z(field):
    return jnp.pad(field, ((0, 0), (0, 0), (0, 0), (0, 0), (0, 1)))


def gather_upper(field):
    from_x = from_behind(field[:, :, :1], "gx", -1)
    widened = jnp.concatenate([field, from_x], axis=2)
    from_y = from_behind(widened[:, :, :, :1], "gy", -1)
    return jnp.concatenate([widened, from_y], axis=3)


def return_lower(forces):
    size_x = forces.shape[2] - 1
    size_y = forces.shape[3] - 1
    to_y = from_behind(forces[:, :, :, size_y:], "gy", 1)
    kept = forces[:, :, :, :size_y]
    kept = jnp.concatenate([kept[:, :, :, :1] + to_y, kept[:, :, :, 1:]], axis=3)
    to_x = from_behind(kept[:, :, size_x:], "gx", 1)
    kept = kept[:, :, :size_x]
    return jnp.concatenate([kept[:, :, :1] + to_x, kept[:, :, 1:]], axis=2)


def halo_both(cells, axis, dim, width):
    count = lax.axis_size(axis)
    head = lax.slice_in_dim(cells, 0, width, axis=dim)
    tail = lax.slice_in_dim(cells, cells.shape[dim] - width, cells.shape[dim], axis=dim)
    below = lax.ppermute(tail, axis, [(i, i + 1) for i in range(count - 1)])
    above = lax.ppermute(head, axis, [(i + 1, i) for i in range(count - 1)])
    return jnp.concatenate([below, cells, above], axis=dim)


def inside_mask(axis, extent, width, total):
    places = np.arange(extent + 2 * width) - width
    own = jnp.asarray(places, jnp.int32) + lax.axis_index(axis) * extent
    return ((own >= 0) & (own < total)).astype(jnp.float32)


def node_forces(node_field, modulus, stiffness):
    local_disp = cases_disp(node_field)
    local_load = jnp.einsum("ij,cjabd->ciabd", stiffness, local_disp, precision=highest)
    local_force = (local_load * modulus).reshape((node_field.shape[0], 8, 3) + modulus.shape)
    summed = jnp.zeros_like(node_field)
    for corner in range(8):
        off_x, off_y, off_z = (corner // 4, corner // 2 % 2, corner % 2)
        summed = summed + jnp.pad(
            local_force[:, corner],
            ((0, 0), (0, 0), (off_x, 1 - off_x), (off_y, 1 - off_y), (off_z, 1 - off_z)),
        )
    return summed[..., :-1], local_disp, local_load


def on_device(start_disp, bone_mask, density, load_nodes, load_forces):
    stiffness = jnp.asarray(hex_stiffness(), jnp.float32)
    modulus = bone_mask.astype(jnp.float32) * density * density
    case_count = start_disp.shape[0]
    size_x = start_disp.shape[2]
    size_y = start_disp.shape[3]
    size_z = start_disp.shape[4]
    count_x = lax.axis_size("gx")
    count_y = lax.axis_size("gy")
    fields = case_count * 3

    slot_ids = jnp.arange(size_x * size_y, dtype=jnp.int32)
    matches = (load_nodes[0, 0][:, :, None] == slot_ids).astype(jnp.float32)
    top_plane = jnp.einsum("cls,ckl->cks", matches, load_forces[0, 0], precision=highest).reshape(
        fields, size_x, size_y
    )
    packed_loads = jnp.pad(top_plane.transpose(1, 2, 0), ((0, 0), (0, 0), (0, size_z - fields)))
    packed = jnp.concatenate(
        [start_disp.reshape(fields, size_x, size_y, size_z), modulus[None], packed_loads[None]],
        axis=0,
    )
    packed = halo_both(halo_both(packed, "gx", 1, 2), "gy", 2, 2)
    wide_start = packed[:fields].reshape(case_count, 3, size_x + 4, size_y + 4, size_z)
    wide_modulus = packed[fields]
    wide_loads = packed[fields + 1, 1:-1, 1:-1, :fields].transpose(2, 0, 1)
    wide_loads = wide_loads.reshape(case_count, 3, size_x + 2, size_y + 2)

    start_nodes = pad_upper_z(wide_start)
    forces, start_elems, start_loads = node_forces(
        start_nodes, wide_modulus[:-1, :-1], stiffness
    )
    applied = forces[:, :, 1:-1, 1:-1] + spring * wide_start[:, :, 1:-1, 1:-1]
    keep = (
        inside_mask("gx", size_x, 1, size_x * count_x)[:, None, None]
        * inside_mask("gy", size_y, 1, size_y * count_y)[None, :, None]
    )
    residual_wide = (
        jnp.concatenate(
            [-applied[..., :-1], (wide_loads - applied[..., -1])[..., None]], axis=4
        )
        * keep
    )

    residual_nodes = pad_upper_z(residual_wide)
    forces, residual_elems, residual_loads = node_forces(
        residual_nodes, wide_modulus[1:-2, 1:-2], stiffness
    )
    residual = residual_wide[:, :, 1:-1, 1:-1]
    applied = forces[:, :, 1:-1, 1:-1] + spring * residual

    blur_mass = modulus
    for dim, axis in ((0, "gx"), (1, "gy"), (2, None)):
        extent = modulus.shape[dim]
        count = 1 if axis is None else lax.axis_size(axis)
        places = np.arange(extent * count)
        kept = np.zeros(extent * count)
        for tap_index, weight in enumerate(blur_weights()):
            inside = (places + 4 - tap_index >= 0) & (places + 4 - tap_index < extent * count)
            kept = kept + np.where(inside, weight, 0.0)
        kept = jnp.asarray(kept, jnp.float32)
        if axis is not None:
            kept = lax.dynamic_slice_in_dim(kept, lax.axis_index(axis) * extent, extent)
        shape = [1, 1, 1]
        shape[dim] = extent
        blur_mass = blur_mass * kept.reshape(shape)
    start_elems = start_elems[:, :, 2:-1, 2:-1]
    start_loads = start_loads[:, :, 2:-1, 2:-1]
    residual_elems = residual_elems[:, :, 1:, 1:]
    residual_loads = residual_loads[:, :, 1:, 1:]
    start_energy = jnp.sum(start_elems * start_loads * blur_mass, axis=(1, 2, 3, 4))
    start_weighted = start_loads * blur_mass
    residual_weighted = residual_loads * blur_mass
    cross_energy = jnp.sum(
        residual_elems[:, None] * start_weighted[None, :], axis=(2, 3, 4, 5)
    )
    residual_energy = jnp.sum(
        residual_elems[:, None] * residual_weighted[None, :], axis=(2, 3, 4, 5)
    )
    grams = tree_sum(
        jnp.stack(
            [
                local_gram(residual, residual),
                local_gram(residual, applied),
                cross_energy,
                residual_energy,
                jnp.diag(start_energy),
            ]
        )
    )
    norm_now = grams[0]
    step_alpha = solve_spd(grams[1], norm_now)
    summed = (
        jnp.sum(grams[4])
        + 2.0 * jnp.sum(step_alpha * grams[2])
        + jnp.sum(step_alpha[:, None, :] * grams[3][:, :, None] * step_alpha[None, :, :])
    )
    solution = start_disp + mix_cases(residual, step_alpha)
    node_field = start_nodes[:, :, 2:-1, 2:-1] + mix_cases(
        residual_nodes[:, :, 1:, 1:], step_alpha
    )
    energy = element_energy(node_field, stiffness)
    stimulus = modulus * energy
    smooth = blur_valid(with_halo(stimulus, (("gx", 0),), 4), 0, size_x)
    smooth = blur_valid(with_halo(smooth, (("gy", 1),), 4), 1, size_y)
    smooth = blur_valid(jnp.pad(smooth, ((0, 0), (0, 0), (4, 4))), 2, size_z)
    mean_stim = summed / (size_x * size_y * size_z * count_x * count_y)
    new_density = jnp.minimum(density * (0.5 + 0.5 * smooth / (mean_stim + mean_eps)), density_cap)
    return (solution, new_density)


def solution(mesh):
    return jax.shard_map(
        on_device,
        mesh=mesh,
        in_specs=(
            P(None, None, "gx", "gy", None),
            P("gx", "gy", None),
            P("gx", "gy", None),
            P("gx", "gy", None, None),
            P("gx", "gy", None, None, None),
        ),
        out_specs=(P(None, None, "gx", "gy", None), P("gx", "gy", None)),
        check_vma=False,
    )
```

```python
import jax
import jax.numpy as jnp
import numpy as np
from jax import lax
from jax.sharding import PartitionSpec as P

spring = 0.1
poisson = 0.3
blur_sigma = 2.0
density_cap = 1.0
mean_eps = 1e-06
highest = lax.Precision.HIGHEST


def from_behind(block, axis, distance):
    devices = range(lax.axis_size(axis))
    route = [(i - distance, i) for i in devices if i - distance in devices]
    return lax.ppermute(block, axis, route)


def with_halo(cells, sides, width):
    for axis, dim in sides:
        count = lax.axis_size(axis)
        ends = count - 1
        head = lax.slice_in_dim(cells, 0, width, axis=dim)
        tail = lax.slice_in_dim(cells, cells.shape[dim] - width, cells.shape[dim], axis=dim)
        cells = jnp.concatenate(
            [
                lax.ppermute(tail, axis, [(i, (i + 1) % count) for i in range(ends)]),
                cells,
                lax.ppermute(head, axis, [((i + 1) % count, i) for i in range(ends)]),
            ],
            axis=dim,
        )
    return cells


def hex_stiffness():
    lame_first = poisson / ((1.0 + poisson) * (1.0 - 2.0 * poisson))
    shear_mod = 1.0 / (2.0 * (1.0 + poisson))
    elastic = np.zeros((6, 6))
    elastic[:3, :3] = lame_first
    for axis_id in range(3):
        elastic[axis_id, axis_id] = lame_first + 2.0 * shear_mod
        elastic[axis_id + 3, axis_id + 3] = shear_mod
    points = [0.5 - 0.5 / np.sqrt(3.0), 0.5 + 0.5 / np.sqrt(3.0)]
    stiffness = np.zeros((24, 24))
    for point_x in points:
        for point_y in points:
            for point_z in points:
                coords = (point_x, point_y, point_z)
                strain = np.zeros((6, 24))
                for corner in range(8):
                    offsets = (corner // 4, corner // 2 % 2, corner % 2)
                    shapes = [
                        coords[axis_id] if offsets[axis_id] == 1 else 1.0 - coords[axis_id]
                        for axis_id in range(3)
                    ]
                    slopes = [1.0 if offsets[axis_id] == 1 else -1.0 for axis_id in range(3)]
                    grad_x = slopes[0] * shapes[1] * shapes[2]
                    grad_y = shapes[0] * slopes[1] * shapes[2]
                    grad_z = shapes[0] * shapes[1] * slopes[2]
                    column = 3 * corner
                    strain[0, column] = grad_x
                    strain[1, column + 1] = grad_y
                    strain[2, column + 2] = grad_z
                    strain[3, column] = grad_y
                    strain[3, column + 1] = grad_x
                    strain[4, column + 1] = grad_z
                    strain[4, column + 2] = grad_y
                    strain[5, column] = grad_z
                    strain[5, column + 2] = grad_x
                stiffness += 0.125 * strain.T @ elastic @ strain
    return stiffness


def blur_weights():
    offsets = np.arange(9) - 4.0
    unscaled = np.exp(-offsets * offsets / (2.0 * blur_sigma * blur_sigma))
    return [float(entry) for entry in unscaled / unscaled.sum()]


def blur_valid(values, axis_id, extent):
    weights = blur_weights()
    summed = weights[0] * lax.slice_in_dim(values, 0, extent, axis=axis_id)
    for tap_index in range(1, 9):
        summed = summed + weights[tap_index] * lax.slice_in_dim(
            values, tap_index, tap_index + extent, axis=axis_id
        )
    return summed


def element_disp(node_field):
    size_x = node_field.shape[1] - 1
    size_y = node_field.shape[2] - 1
    size_z = node_field.shape[3] - 1
    corners = []
    for corner in range(8):
        off_x, off_y, off_z = (corner // 4, corner // 2 % 2, corner % 2)
        corners.append(
            node_field[:, off_x : off_x + size_x, off_y : off_y + size_y, off_z : off_z + size_z]
        )
    return jnp.stack(corners).reshape(24, size_x, size_y, size_z)


def cases_disp(node_field):
    size_x = node_field.shape[2] - 1
    size_y = node_field.shape[3] - 1
    size_z = node_field.shape[4] - 1
    corners = []
    for corner in range(8):
        off_x, off_y, off_z = (corner // 4, corner // 2 % 2, corner % 2)
        corners.append(
            node_field[:, :, off_x : off_x + size_x, off_y : off_y + size_y, off_z : off_z + size_z]
        )
    return jnp.stack(corners, axis=1).reshape(
        (node_field.shape[0], 24, size_x, size_y, size_z)
    )


def element_forces(node_field, modulus, stiffness):
    local_disp = cases_disp(node_field)
    local_force = jnp.einsum("ij,cjabd->ciabd", stiffness, local_disp, precision=highest) * modulus
    local_force = local_force.reshape((node_field.shape[0], 8, 3) + modulus.shape)
    summed = jnp.zeros_like(node_field)
    for corner in range(8):
        off_x, off_y, off_z = (corner // 4, corner // 2 % 2, corner % 2)
        summed = summed + jnp.pad(
            local_force[:, corner],
            ((0, 0), (0, 0), (off_x, 1 - off_x), (off_y, 1 - off_y), (off_z, 1 - off_z)),
        )
    return summed


def element_energy(node_field, stiffness):
    local_disp = cases_disp(node_field)
    local_force = jnp.einsum("ij,cjabd->ciabd", stiffness, local_disp, precision=highest)
    return jnp.sum(local_disp * local_force, axis=(0, 1))


def local_gram(left_field, right_field):
    return jnp.einsum("iabcd,jabcd->ij", left_field, right_field, precision=highest)


def tree_sum(value):
    for axis in ("gy", "gx"):
        count = lax.axis_size(axis)
        copies = jnp.broadcast_to(value[None], (count,) + value.shape)
        value = jnp.sum(lax.all_to_all(copies, axis, 0, 0, tiled=False), axis=0)
    return value


def mix_cases(field, coeffs):
    return jnp.einsum("kabcd,kj->jabcd", field, coeffs, precision=highest)


def solve_spd(matrix, rhs_matrix):
    factor = jnp.linalg.cholesky(matrix)
    forward = lax.linalg.triangular_solve(factor, rhs_matrix, left_side=True, lower=True)
    return lax.linalg.triangular_solve(
        factor, forward, left_side=True, lower=True, transpose_a=True
    )


def solve_spd_rows(matrix, rhs_matrix):
    factor = jnp.linalg.cholesky(matrix)
    matrix_order = matrix.shape[0]
    forward = []
    for row_index in range(matrix_order):
        partial_sum = rhs_matrix[row_index]
        for col_index in range(row_index):
            partial_sum = partial_sum - factor[row_index, col_index] * forward[col_index]
        forward.append(partial_sum / factor[row_index, row_index])
    backward = [None] * matrix_order
    for row_index in reversed(range(matrix_order)):
        partial_sum = forward[row_index]
        for col_index in range(row_index + 1, matrix_order):
            partial_sum = partial_sum - factor[col_index, row_index] * backward[col_index]
        backward[row_index] = partial_sum / factor[row_index, row_index]
    return jnp.stack(backward)


def pad_upper_z(field):
    return jnp.pad(field, ((0, 0), (0, 0), (0, 0), (0, 0), (0, 1)))


def gather_upper(field):
    from_x = from_behind(field[:, :, :1], "gx", -1)
    widened = jnp.concatenate([field, from_x], axis=2)
    from_y = from_behind(widened[:, :, :, :1], "gy", -1)
    return jnp.concatenate([widened, from_y], axis=3)


def return_lower(forces):
    size_x = forces.shape[2] - 1
    size_y = forces.shape[3] - 1
    to_y = from_behind(forces[:, :, :, size_y:], "gy", 1)
    kept = forces[:, :, :, :size_y]
    kept = jnp.concatenate([kept[:, :, :, :1] + to_y, kept[:, :, :, 1:]], axis=3)
    to_x = from_behind(kept[:, :, size_x:], "gx", 1)
    kept = kept[:, :, :size_x]
    return jnp.concatenate([kept[:, :, :1] + to_x, kept[:, :, 1:]], axis=2)


def halo_both(cells, axis, dim, width):
    count = lax.axis_size(axis)
    head = lax.slice_in_dim(cells, 0, width, axis=dim)
    tail = lax.slice_in_dim(cells, cells.shape[dim] - width, cells.shape[dim], axis=dim)
    below = lax.ppermute(tail, axis, [(i, i + 1) for i in range(count - 1)])
    above = lax.ppermute(head, axis, [(i + 1, i) for i in range(count - 1)])
    return jnp.concatenate([below, cells, above], axis=dim)


def inside_mask(axis, extent, width, total):
    places = np.arange(extent + 2 * width) - width
    own = jnp.asarray(places, jnp.int32) + lax.axis_index(axis) * extent
    return ((own >= 0) & (own < total)).astype(jnp.float32)


def node_forces(node_field, modulus, stiffness):
    local_disp = cases_disp(node_field)
    local_load = jnp.einsum("ij,cjabd->ciabd", stiffness, local_disp, precision=highest)
    local_force = (local_load * modulus).reshape((node_field.shape[0], 8, 3) + modulus.shape)
    summed = jnp.zeros_like(node_field)
    for corner in range(8):
        off_x, off_y, off_z = (corner // 4, corner // 2 % 2, corner % 2)
        summed = summed + jnp.pad(
            local_force[:, corner],
            ((0, 0), (0, 0), (off_x, 1 - off_x), (off_y, 1 - off_y), (off_z, 1 - off_z)),
        )
    return summed[..., :-1], local_disp, local_load


def on_device(start_disp, bone_mask, density, load_nodes, load_forces):
    stiffness = jnp.asarray(hex_stiffness(), jnp.float32)
    modulus = bone_mask.astype(jnp.float32) * density * density
    case_count = start_disp.shape[0]
    size_x = start_disp.shape[2]
    size_y = start_disp.shape[3]
    size_z = start_disp.shape[4]
    count_x = lax.axis_size("gx")
    count_y = lax.axis_size("gy")
    fields = case_count * 3

    slot_ids = jnp.arange(size_x * size_y, dtype=jnp.int32)
    matches = (load_nodes[0, 0][:, :, None] == slot_ids).astype(jnp.float32)
    top_plane = jnp.einsum("cls,ckl->cks", matches, load_forces[0, 0], precision=highest).reshape(
        fields, size_x, size_y
    )
    packed_loads = jnp.pad(top_plane.transpose(1, 2, 0), ((0, 0), (0, 0), (0, size_z - fields)))
    packed = jnp.concatenate(
        [start_disp.reshape(fields, size_x, size_y, size_z), modulus[None], packed_loads[None]],
        axis=0,
    )
    packed = halo_both(halo_both(packed, "gx", 1, 2), "gy", 2, 2)
    wide_start = packed[:fields].reshape(case_count, 3, size_x + 4, size_y + 4, size_z)
    wide_modulus = packed[fields]
    wide_loads = packed[fields + 1, 1:-1, 1:-1, :fields].transpose(2, 0, 1)
    wide_loads = wide_loads.reshape(case_count, 3, size_x + 2, size_y + 2)

    start_nodes = pad_upper_z(wide_start)
    forces, start_elems, start_loads = node_forces(
        start_nodes, wide_modulus[:-1, :-1], stiffness
    )
    applied = forces[:, :, 1:-1, 1:-1] + spring * wide_start[:, :, 1:-1, 1:-1]
    keep = (
        inside_mask("gx", size_x, 1, size_x * count_x)[:, None, None]
        * inside_mask("gy", size_y, 1, size_y * count_y)[None, :, None]
    )
    residual_wide = (
        jnp.concatenate(
            [-applied[..., :-1], (wide_loads - applied[..., -1])[..., None]], axis=4
        )
        * keep
    )

    residual_nodes = pad_upper_z(residual_wide)
    forces, residual_elems, residual_loads = node_forces(
        residual_nodes, wide_modulus[1:-2, 1:-2], stiffness
    )
    residual = residual_wide[:, :, 1:-1, 1:-1]
    applied = forces[:, :, 1:-1, 1:-1] + spring * residual

    blur_mass = modulus
    for dim, axis in ((0, "gx"), (1, "gy"), (2, None)):
        extent = modulus.shape[dim]
        count = 1 if axis is None else lax.axis_size(axis)
        places = lax.iota(jnp.int32, extent)
        if axis is not None:
            places = places + lax.axis_index(axis) * extent
        kept = jnp.zeros((extent,), jnp.float32)
        for tap_index, weight in enumerate(blur_weights()):
            shifted = places + 4 - tap_index
            kept = kept + jnp.where((shifted >= 0) & (shifted < extent * count), weight, 0.0)
        shape = [1, 1, 1]
        shape[dim] = extent
        blur_mass = blur_mass * kept.reshape(shape)
    start_elems = start_elems[:, :, 2:-1, 2:-1]
    start_loads = start_loads[:, :, 2:-1, 2:-1]
    residual_elems = residual_elems[:, :, 1:, 1:]
    residual_loads = residual_loads[:, :, 1:, 1:]
    start_energy = jnp.sum(start_elems * start_loads * blur_mass, axis=(1, 2, 3, 4))
    start_weighted = start_loads * blur_mass
    residual_weighted = residual_loads * blur_mass
    cross_energy = jnp.sum(
        residual_elems[:, None] * start_weighted[None, :], axis=(2, 3, 4, 5)
    )
    residual_energy = jnp.sum(
        residual_elems[:, None] * residual_weighted[None, :], axis=(2, 3, 4, 5)
    )
    grams = tree_sum(
        jnp.stack(
            [
                local_gram(residual, residual),
                local_gram(residual, applied),
                cross_energy,
                residual_energy,
                jnp.diag(start_energy),
            ]
        )
    )
    norm_now = grams[0]
    step_alpha = solve_spd(grams[1], norm_now)
    summed = (
        jnp.sum(grams[4])
        + 2.0 * jnp.sum(step_alpha * grams[2])
        + jnp.sum(step_alpha[:, None, :] * grams[3][:, :, None] * step_alpha[None, :, :])
    )
    solution = start_disp + mix_cases(residual, step_alpha)
    final_elems = start_elems + jnp.sum(
        residual_elems[:, None] * step_alpha[:, :, None, None, None, None], axis=0
    )
    final_loads = start_loads + jnp.sum(
        residual_loads[:, None] * step_alpha[:, :, None, None, None, None], axis=0
    )
    energy = jnp.sum(final_elems * final_loads, axis=(0, 1))
    stimulus = modulus * energy
    smooth = blur_valid(with_halo(stimulus, (("gx", 0),), 4), 0, size_x)
    smooth = blur_valid(with_halo(smooth, (("gy", 1),), 4), 1, size_y)
    smooth = blur_valid(jnp.pad(smooth, ((0, 0), (0, 0), (4, 4))), 2, size_z)
    mean_stim = summed / (size_x * size_y * size_z * count_x * count_y)
    new_density = jnp.minimum(density * (0.5 + 0.5 * smooth / (mean_stim + mean_eps)), density_cap)
    return (solution, new_density)


def solution(mesh):
    return jax.shard_map(
        on_device,
        mesh=mesh,
        in_specs=(
            P(None, None, "gx", "gy", None),
            P("gx", "gy", None),
            P("gx", "gy", None),
            P("gx", "gy", None, None),
            P("gx", "gy", None, None, None),
        ),
        out_specs=(P(None, None, "gx", "gy", None), P("gx", "gy", None)),
        check_vma=False,
    )
```

```python
import jax
import jax.numpy as jnp
import numpy as np
from jax import lax
from jax.sharding import PartitionSpec as P

spring = 0.1
poisson = 0.3
blur_sigma = 2.0
density_cap = 1.0
mean_eps = 1e-06
highest = lax.Precision.HIGHEST


def from_behind(block, axis, distance):
    devices = range(lax.axis_size(axis))
    route = [(i - distance, i) for i in devices if i - distance in devices]
    return lax.ppermute(block, axis, route)


def with_halo(cells, sides, width):
    for axis, dim in sides:
        count = lax.axis_size(axis)
        ends = count - 1
        head = lax.slice_in_dim(cells, 0, width, axis=dim)
        tail = lax.slice_in_dim(cells, cells.shape[dim] - width, cells.shape[dim], axis=dim)
        cells = jnp.concatenate(
            [
                lax.ppermute(tail, axis, [(i, (i + 1) % count) for i in range(ends)]),
                cells,
                lax.ppermute(head, axis, [((i + 1) % count, i) for i in range(ends)]),
            ],
            axis=dim,
        )
    return cells


def hex_stiffness():
    lame_first = poisson / ((1.0 + poisson) * (1.0 - 2.0 * poisson))
    shear_mod = 1.0 / (2.0 * (1.0 + poisson))
    elastic = np.zeros((6, 6))
    elastic[:3, :3] = lame_first
    for axis_id in range(3):
        elastic[axis_id, axis_id] = lame_first + 2.0 * shear_mod
        elastic[axis_id + 3, axis_id + 3] = shear_mod
    points = [0.5 - 0.5 / np.sqrt(3.0), 0.5 + 0.5 / np.sqrt(3.0)]
    stiffness = np.zeros((24, 24))
    for point_x in points:
        for point_y in points:
            for point_z in points:
                coords = (point_x, point_y, point_z)
                strain = np.zeros((6, 24))
                for corner in range(8):
                    offsets = (corner // 4, corner // 2 % 2, corner % 2)
                    shapes = [
                        coords[axis_id] if offsets[axis_id] == 1 else 1.0 - coords[axis_id]
                        for axis_id in range(3)
                    ]
                    slopes = [1.0 if offsets[axis_id] == 1 else -1.0 for axis_id in range(3)]
                    grad_x = slopes[0] * shapes[1] * shapes[2]
                    grad_y = shapes[0] * slopes[1] * shapes[2]
                    grad_z = shapes[0] * shapes[1] * slopes[2]
                    column = 3 * corner
                    strain[0, column] = grad_x
                    strain[1, column + 1] = grad_y
                    strain[2, column + 2] = grad_z
                    strain[3, column] = grad_y
                    strain[3, column + 1] = grad_x
                    strain[4, column + 1] = grad_z
                    strain[4, column + 2] = grad_y
                    strain[5, column] = grad_z
                    strain[5, column + 2] = grad_x
                stiffness += 0.125 * strain.T @ elastic @ strain
    return stiffness


def blur_weights():
    offsets = np.arange(9) - 4.0
    unscaled = np.exp(-offsets * offsets / (2.0 * blur_sigma * blur_sigma))
    return [float(entry) for entry in unscaled / unscaled.sum()]


def blur_valid(values, axis_id, extent):
    weights = blur_weights()
    summed = weights[0] * lax.slice_in_dim(values, 0, extent, axis=axis_id)
    for tap_index in range(1, 9):
        summed = summed + weights[tap_index] * lax.slice_in_dim(
            values, tap_index, tap_index + extent, axis=axis_id
        )
    return summed


def element_disp(node_field):
    size_x = node_field.shape[1] - 1
    size_y = node_field.shape[2] - 1
    size_z = node_field.shape[3] - 1
    corners = []
    for corner in range(8):
        off_x, off_y, off_z = (corner // 4, corner // 2 % 2, corner % 2)
        corners.append(
            node_field[:, off_x : off_x + size_x, off_y : off_y + size_y, off_z : off_z + size_z]
        )
    return jnp.stack(corners).reshape(24, size_x, size_y, size_z)


def cases_disp(node_field):
    size_x = node_field.shape[2] - 1
    size_y = node_field.shape[3] - 1
    size_z = node_field.shape[4] - 1
    corners = []
    for corner in range(8):
        off_x, off_y, off_z = (corner // 4, corner // 2 % 2, corner % 2)
        corners.append(
            node_field[:, :, off_x : off_x + size_x, off_y : off_y + size_y, off_z : off_z + size_z]
        )
    return jnp.stack(corners, axis=1).reshape(
        (node_field.shape[0], 24, size_x, size_y, size_z)
    )


def element_forces(node_field, modulus, stiffness):
    local_disp = cases_disp(node_field)
    local_force = jnp.einsum("ij,cjabd->ciabd", stiffness, local_disp, precision=highest) * modulus
    local_force = local_force.reshape((node_field.shape[0], 8, 3) + modulus.shape)
    summed = jnp.zeros_like(node_field)
    for corner in range(8):
        off_x, off_y, off_z = (corner // 4, corner // 2 % 2, corner % 2)
        summed = summed + jnp.pad(
            local_force[:, corner],
            ((0, 0), (0, 0), (off_x, 1 - off_x), (off_y, 1 - off_y), (off_z, 1 - off_z)),
        )
    return summed


def element_energy(node_field, stiffness):
    local_disp = cases_disp(node_field)
    local_force = jnp.einsum("ij,cjabd->ciabd", stiffness, local_disp, precision=highest)
    return jnp.sum(local_disp * local_force, axis=(0, 1))


def local_gram(left_field, right_field):
    return jnp.einsum("iabcd,jabcd->ij", left_field, right_field, precision=highest)


def tree_sum(value):
    for axis in ("gy", "gx"):
        count = lax.axis_size(axis)
        copies = jnp.broadcast_to(value[None], (count,) + value.shape)
        value = jnp.sum(lax.all_to_all(copies, axis, 0, 0, tiled=False), axis=0)
    return value


def mix_cases(field, coeffs):
    return jnp.einsum("kabcd,kj->jabcd", field, coeffs, precision=highest)


def solve_spd(matrix, rhs_matrix):
    factor = jnp.linalg.cholesky(matrix)
    forward = lax.linalg.triangular_solve(factor, rhs_matrix, left_side=True, lower=True)
    return lax.linalg.triangular_solve(
        factor, forward, left_side=True, lower=True, transpose_a=True
    )


def solve_spd_rows(matrix, rhs_matrix):
    factor = jnp.linalg.cholesky(matrix)
    matrix_order = matrix.shape[0]
    forward = []
    for row_index in range(matrix_order):
        partial_sum = rhs_matrix[row_index]
        for col_index in range(row_index):
            partial_sum = partial_sum - factor[row_index, col_index] * forward[col_index]
        forward.append(partial_sum / factor[row_index, row_index])
    backward = [None] * matrix_order
    for row_index in reversed(range(matrix_order)):
        partial_sum = forward[row_index]
        for col_index in range(row_index + 1, matrix_order):
            partial_sum = partial_sum - factor[col_index, row_index] * backward[col_index]
        backward[row_index] = partial_sum / factor[row_index, row_index]
    return jnp.stack(backward)


def pad_upper_z(field):
    return jnp.pad(field, ((0, 0), (0, 0), (0, 0), (0, 0), (0, 1)))


def gather_upper(field):
    from_x = from_behind(field[:, :, :1], "gx", -1)
    widened = jnp.concatenate([field, from_x], axis=2)
    from_y = from_behind(widened[:, :, :, :1], "gy", -1)
    return jnp.concatenate([widened, from_y], axis=3)


def return_lower(forces):
    size_x = forces.shape[2] - 1
    size_y = forces.shape[3] - 1
    to_y = from_behind(forces[:, :, :, size_y:], "gy", 1)
    kept = forces[:, :, :, :size_y]
    kept = jnp.concatenate([kept[:, :, :, :1] + to_y, kept[:, :, :, 1:]], axis=3)
    to_x = from_behind(kept[:, :, size_x:], "gx", 1)
    kept = kept[:, :, :size_x]
    return jnp.concatenate([kept[:, :, :1] + to_x, kept[:, :, 1:]], axis=2)


def corner_modes(node_field):
    found = {(): node_field}
    for dim in (2, 3, 4):
        grown = {}
        for key, cells in found.items():
            low = lax.slice_in_dim(cells, 0, cells.shape[dim] - 1, axis=dim)
            high = lax.slice_in_dim(cells, 1, cells.shape[dim], axis=dim)
            grown[key + (0,)] = high + low
            grown[key + (1,)] = high - low
        found = grown
    return [found[(mode // 4, mode // 2 % 2, mode % 2)] for mode in range(8)]


def mode_stiffness():
    step = np.array([[1.0, 1.0], [-1.0, 1.0]])
    change = np.kron(np.kron(np.kron(step, step), step), np.eye(3))
    return change @ hex_stiffness() @ change.T / 64.0


def mode_loads(modes, table):
    loads = []
    for mode in range(8):
        parts = []
        for comp in range(3):
            total = None
            for other in range(3):
                source = mode ^ (4 >> comp) ^ (4 >> other)
                weight = float(table[3 * mode + comp, 3 * source + other])
                if abs(weight) < 1e-12:
                    continue
                term = weight * modes[source][:, other]
                total = term if total is None else total + term
            parts.append(jnp.zeros_like(modes[mode][:, comp]) if total is None else total)
        loads.append(jnp.stack(parts, axis=1))
    return loads


def modes_to_nodes(loads):
    found = {(mode // 4, mode // 2 % 2, mode % 2): loads[mode] for mode in range(8)}
    for dim in (4, 3, 2):
        merged = {}
        for key in {k[:-1] for k in found}:
            total = found[key + (0,)]
            change = found[key + (1,)]
            widths = [(0, 0)] * total.ndim
            low = list(widths)
            low[dim] = (0, 1)
            high = list(widths)
            high[dim] = (1, 0)
            merged[key] = jnp.pad(total - change, low) + jnp.pad(total + change, high)
        found = merged
    return found[()]


def halo_both(cells, axis, dim, width):
    count = lax.axis_size(axis)
    head = lax.slice_in_dim(cells, 0, width, axis=dim)
    tail = lax.slice_in_dim(cells, cells.shape[dim] - width, cells.shape[dim], axis=dim)
    below = lax.ppermute(tail, axis, [(i, i + 1) for i in range(count - 1)])
    above = lax.ppermute(head, axis, [(i + 1, i) for i in range(count - 1)])
    return jnp.concatenate([below, cells, above], axis=dim)


def inside_mask(axis, extent, width, total):
    places = np.arange(extent + 2 * width) - width
    own = jnp.asarray(places, jnp.int32) + lax.axis_index(axis) * extent
    return ((own >= 0) & (own < total)).astype(jnp.float32)


def node_forces(node_field, modulus, table):
    modes = corner_modes(node_field)
    loads = mode_loads(modes, table)
    summed = modes_to_nodes([part * modulus for part in loads])
    return summed[..., :-1], jnp.stack(modes, axis=1), jnp.stack(loads, axis=1)


def on_device(start_disp, bone_mask, density, load_nodes, load_forces):
    stiffness = mode_stiffness()
    modulus = bone_mask.astype(jnp.float32) * density * density
    case_count = start_disp.shape[0]
    size_x = start_disp.shape[2]
    size_y = start_disp.shape[3]
    size_z = start_disp.shape[4]
    count_x = lax.axis_size("gx")
    count_y = lax.axis_size("gy")
    fields = case_count * 3

    slot_ids = jnp.arange(size_x * size_y, dtype=jnp.int32)
    matches = (load_nodes[0, 0][:, :, None] == slot_ids).astype(jnp.float32)
    top_plane = jnp.einsum("cls,ckl->cks", matches, load_forces[0, 0], precision=highest).reshape(
        fields, size_x, size_y
    )
    packed_loads = jnp.pad(top_plane.transpose(1, 2, 0), ((0, 0), (0, 0), (0, size_z - fields)))
    packed = jnp.concatenate(
        [start_disp.reshape(fields, size_x, size_y, size_z), modulus[None], packed_loads[None]],
        axis=0,
    )
    packed = halo_both(halo_both(packed, "gx", 1, 2), "gy", 2, 2)
    wide_start = packed[:fields].reshape(case_count, 3, size_x + 4, size_y + 4, size_z)
    wide_modulus = packed[fields]
    wide_loads = packed[fields + 1, 1:-1, 1:-1, :fields].transpose(2, 0, 1)
    wide_loads = wide_loads.reshape(case_count, 3, size_x + 2, size_y + 2)

    start_nodes = pad_upper_z(wide_start)
    forces, start_elems, start_loads = node_forces(
        start_nodes, wide_modulus[:-1, :-1], stiffness
    )
    applied = forces[:, :, 1:-1, 1:-1] + spring * wide_start[:, :, 1:-1, 1:-1]
    keep = (
        inside_mask("gx", size_x, 1, size_x * count_x)[:, None, None]
        * inside_mask("gy", size_y, 1, size_y * count_y)[None, :, None]
    )
    residual_wide = (
        jnp.concatenate(
            [-applied[..., :-1], (wide_loads - applied[..., -1])[..., None]], axis=4
        )
        * keep
    )

    residual_nodes = pad_upper_z(residual_wide)
    forces, residual_elems, residual_loads = node_forces(
        residual_nodes, wide_modulus[1:-2, 1:-2], stiffness
    )
    residual = residual_wide[:, :, 1:-1, 1:-1]
    applied = forces[:, :, 1:-1, 1:-1] + spring * residual

    blur_mass = modulus
    for dim, axis in ((0, "gx"), (1, "gy"), (2, None)):
        extent = modulus.shape[dim]
        count = 1 if axis is None else lax.axis_size(axis)
        places = np.arange(extent * count)
        kept = np.zeros(extent * count)
        for tap_index, weight in enumerate(blur_weights()):
            inside = (places + 4 - tap_index >= 0) & (places + 4 - tap_index < extent * count)
            kept = kept + np.where(inside, weight, 0.0)
        kept = jnp.asarray(kept, jnp.float32)
        if axis is not None:
            kept = lax.dynamic_slice_in_dim(kept, lax.axis_index(axis) * extent, extent)
        shape = [1, 1, 1]
        shape[dim] = extent
        blur_mass = blur_mass * kept.reshape(shape)
    start_elems = start_elems[:, :, :, 2:-1, 2:-1]
    start_loads = start_loads[:, :, :, 2:-1, 2:-1]
    residual_elems = residual_elems[:, :, :, 1:, 1:]
    residual_loads = residual_loads[:, :, :, 1:, 1:]
    start_energy = jnp.sum(start_elems * start_loads * blur_mass, axis=(1, 2, 3, 4, 5))
    start_weighted = start_loads * blur_mass
    residual_weighted = residual_loads * blur_mass
    cross_energy = jnp.sum(
        residual_elems[:, None] * start_weighted[None, :], axis=(2, 3, 4, 5, 6)
    )
    residual_energy = jnp.sum(
        residual_elems[:, None] * residual_weighted[None, :], axis=(2, 3, 4, 5, 6)
    )
    grams = tree_sum(
        jnp.stack(
            [
                local_gram(residual, residual),
                local_gram(residual, applied),
                cross_energy,
                residual_energy,
                jnp.diag(start_energy),
            ]
        )
    )
    norm_now = grams[0]
    step_alpha = solve_spd(grams[1], norm_now)
    summed = (
        jnp.sum(grams[4])
        + 2.0 * jnp.sum(step_alpha * grams[2])
        + jnp.sum(step_alpha[:, None, :] * grams[3][:, :, None] * step_alpha[None, :, :])
    )
    solution = start_disp + mix_cases(residual, step_alpha)
    node_field = start_nodes[:, :, 2:-1, 2:-1] + mix_cases(
        residual_nodes[:, :, 1:, 1:], step_alpha
    )
    final_modes = corner_modes(node_field)
    final_loads = mode_loads(final_modes, stiffness)
    energy = sum(
        jnp.sum(part * load, axis=(0, 1)) for part, load in zip(final_modes, final_loads)
    )
    stimulus = modulus * energy
    smooth = blur_valid(with_halo(stimulus, (("gx", 0),), 4), 0, size_x)
    smooth = blur_valid(with_halo(smooth, (("gy", 1),), 4), 1, size_y)
    smooth = blur_valid(jnp.pad(smooth, ((0, 0), (0, 0), (4, 4))), 2, size_z)
    mean_stim = summed / (size_x * size_y * size_z * count_x * count_y)
    new_density = jnp.minimum(density * (0.5 + 0.5 * smooth / (mean_stim + mean_eps)), density_cap)
    return (solution, new_density)


def solution(mesh):
    return jax.shard_map(
        on_device,
        mesh=mesh,
        in_specs=(
            P(None, None, "gx", "gy", None),
            P("gx", "gy", None),
            P("gx", "gy", None),
            P("gx", "gy", None, None),
            P("gx", "gy", None, None, None),
        ),
        out_specs=(P(None, None, "gx", "gy", None), P("gx", "gy", None)),
        check_vma=False,
    )
```

```python
import jax
import jax.numpy as jnp
import numpy as np
from jax import lax
from jax.sharding import PartitionSpec as P

spring = 0.1
poisson = 0.3
blur_sigma = 2.0
density_cap = 1.0
mean_eps = 1e-06
highest = lax.Precision.HIGHEST


def from_behind(block, axis, distance):
    devices = range(lax.axis_size(axis))
    route = [(i - distance, i) for i in devices if i - distance in devices]
    return lax.ppermute(block, axis, route)


def with_halo(cells, sides, width):
    for axis, dim in sides:
        count = lax.axis_size(axis)
        ends = count - 1
        head = lax.slice_in_dim(cells, 0, width, axis=dim)
        tail = lax.slice_in_dim(cells, cells.shape[dim] - width, cells.shape[dim], axis=dim)
        cells = jnp.concatenate(
            [
                lax.ppermute(tail, axis, [(i, (i + 1) % count) for i in range(ends)]),
                cells,
                lax.ppermute(head, axis, [((i + 1) % count, i) for i in range(ends)]),
            ],
            axis=dim,
        )
    return cells


def hex_stiffness():
    lame_first = poisson / ((1.0 + poisson) * (1.0 - 2.0 * poisson))
    shear_mod = 1.0 / (2.0 * (1.0 + poisson))
    elastic = np.zeros((6, 6))
    elastic[:3, :3] = lame_first
    for axis_id in range(3):
        elastic[axis_id, axis_id] = lame_first + 2.0 * shear_mod
        elastic[axis_id + 3, axis_id + 3] = shear_mod
    points = [0.5 - 0.5 / np.sqrt(3.0), 0.5 + 0.5 / np.sqrt(3.0)]
    stiffness = np.zeros((24, 24))
    for point_x in points:
        for point_y in points:
            for point_z in points:
                coords = (point_x, point_y, point_z)
                strain = np.zeros((6, 24))
                for corner in range(8):
                    offsets = (corner // 4, corner // 2 % 2, corner % 2)
                    shapes = [
                        coords[axis_id] if offsets[axis_id] == 1 else 1.0 - coords[axis_id]
                        for axis_id in range(3)
                    ]
                    slopes = [1.0 if offsets[axis_id] == 1 else -1.0 for axis_id in range(3)]
                    grad_x = slopes[0] * shapes[1] * shapes[2]
                    grad_y = shapes[0] * slopes[1] * shapes[2]
                    grad_z = shapes[0] * shapes[1] * slopes[2]
                    column = 3 * corner
                    strain[0, column] = grad_x
                    strain[1, column + 1] = grad_y
                    strain[2, column + 2] = grad_z
                    strain[3, column] = grad_y
                    strain[3, column + 1] = grad_x
                    strain[4, column + 1] = grad_z
                    strain[4, column + 2] = grad_y
                    strain[5, column] = grad_z
                    strain[5, column + 2] = grad_x
                stiffness += 0.125 * strain.T @ elastic @ strain
    return stiffness


def blur_weights():
    offsets = np.arange(9) - 4.0
    unscaled = np.exp(-offsets * offsets / (2.0 * blur_sigma * blur_sigma))
    return [float(entry) for entry in unscaled / unscaled.sum()]


def blur_valid(values, axis_id, extent):
    weights = blur_weights()
    summed = weights[0] * lax.slice_in_dim(values, 0, extent, axis=axis_id)
    for tap_index in range(1, 9):
        summed = summed + weights[tap_index] * lax.slice_in_dim(
            values, tap_index, tap_index + extent, axis=axis_id
        )
    return summed


def element_disp(node_field):
    size_x = node_field.shape[1] - 1
    size_y = node_field.shape[2] - 1
    size_z = node_field.shape[3] - 1
    corners = []
    for corner in range(8):
        off_x, off_y, off_z = (corner // 4, corner // 2 % 2, corner % 2)
        corners.append(
            node_field[:, off_x : off_x + size_x, off_y : off_y + size_y, off_z : off_z + size_z]
        )
    return jnp.stack(corners).reshape(24, size_x, size_y, size_z)


def cases_disp(node_field):
    size_x = node_field.shape[2] - 1
    size_y = node_field.shape[3] - 1
    size_z = node_field.shape[4] - 1
    corners = []
    for corner in range(8):
        off_x, off_y, off_z = (corner // 4, corner // 2 % 2, corner % 2)
        corners.append(
            node_field[:, :, off_x : off_x + size_x, off_y : off_y + size_y, off_z : off_z + size_z]
        )
    return jnp.stack(corners, axis=1).reshape(
        (node_field.shape[0], 24, size_x, size_y, size_z)
    )


def element_forces(node_field, modulus, stiffness):
    local_disp = cases_disp(node_field)
    local_force = jnp.einsum("ij,cjabd->ciabd", stiffness, local_disp, precision=highest) * modulus
    local_force = local_force.reshape((node_field.shape[0], 8, 3) + modulus.shape)
    summed = jnp.zeros_like(node_field)
    for corner in range(8):
        off_x, off_y, off_z = (corner // 4, corner // 2 % 2, corner % 2)
        summed = summed + jnp.pad(
            local_force[:, corner],
            ((0, 0), (0, 0), (off_x, 1 - off_x), (off_y, 1 - off_y), (off_z, 1 - off_z)),
        )
    return summed


def element_energy(node_field, stiffness):
    local_disp = cases_disp(node_field)
    local_force = jnp.einsum("ij,cjabd->ciabd", stiffness, local_disp, precision=highest)
    return jnp.sum(local_disp * local_force, axis=(0, 1))


def local_gram(left_field, right_field):
    return jnp.einsum("iabcd,jabcd->ij", left_field, right_field, precision=highest)


def tree_sum(value):
    for axis in ("gy", "gx"):
        count = lax.axis_size(axis)
        copies = jnp.broadcast_to(value[None], (count,) + value.shape)
        value = jnp.sum(lax.all_to_all(copies, axis, 0, 0, tiled=False), axis=0)
    return value


def mix_cases(field, coeffs):
    return jnp.einsum("kabcd,kj->jabcd", field, coeffs, precision=highest)


def solve_spd(matrix, rhs_matrix):
    factor = jnp.linalg.cholesky(matrix)
    forward = lax.linalg.triangular_solve(factor, rhs_matrix, left_side=True, lower=True)
    return lax.linalg.triangular_solve(
        factor, forward, left_side=True, lower=True, transpose_a=True
    )


def solve_spd_rows(matrix, rhs_matrix):
    factor = jnp.linalg.cholesky(matrix)
    matrix_order = matrix.shape[0]
    forward = []
    for row_index in range(matrix_order):
        partial_sum = rhs_matrix[row_index]
        for col_index in range(row_index):
            partial_sum = partial_sum - factor[row_index, col_index] * forward[col_index]
        forward.append(partial_sum / factor[row_index, row_index])
    backward = [None] * matrix_order
    for row_index in reversed(range(matrix_order)):
        partial_sum = forward[row_index]
        for col_index in range(row_index + 1, matrix_order):
            partial_sum = partial_sum - factor[col_index, row_index] * backward[col_index]
        backward[row_index] = partial_sum / factor[row_index, row_index]
    return jnp.stack(backward)


def pad_upper_z(field):
    return jnp.pad(field, ((0, 0), (0, 0), (0, 0), (0, 0), (0, 1)))


def gather_upper(field):
    from_x = from_behind(field[:, :, :1], "gx", -1)
    widened = jnp.concatenate([field, from_x], axis=2)
    from_y = from_behind(widened[:, :, :, :1], "gy", -1)
    return jnp.concatenate([widened, from_y], axis=3)


def return_lower(forces):
    size_x = forces.shape[2] - 1
    size_y = forces.shape[3] - 1
    to_y = from_behind(forces[:, :, :, size_y:], "gy", 1)
    kept = forces[:, :, :, :size_y]
    kept = jnp.concatenate([kept[:, :, :, :1] + to_y, kept[:, :, :, 1:]], axis=3)
    to_x = from_behind(kept[:, :, size_x:], "gx", 1)
    kept = kept[:, :, :size_x]
    return jnp.concatenate([kept[:, :, :1] + to_x, kept[:, :, 1:]], axis=2)


def corner_modes(node_field):
    found = {(): node_field}
    for dim in (2, 3, 4):
        grown = {}
        for key, cells in found.items():
            low = lax.slice_in_dim(cells, 0, cells.shape[dim] - 1, axis=dim)
            high = lax.slice_in_dim(cells, 1, cells.shape[dim], axis=dim)
            grown[key + (0,)] = high + low
            grown[key + (1,)] = high - low
        found = grown
    return [found[(mode // 4, mode // 2 % 2, mode % 2)] for mode in range(8)]


def mode_stiffness():
    step = np.array([[1.0, 1.0], [-1.0, 1.0]])
    change = np.kron(np.kron(np.kron(step, step), step), np.eye(3))
    return change @ hex_stiffness() @ change.T / 64.0


def mode_loads(modes, table):
    loads = []
    for mode in range(8):
        parts = []
        for comp in range(3):
            total = None
            for other in range(3):
                source = mode ^ (4 >> comp) ^ (4 >> other)
                weight = float(table[3 * mode + comp, 3 * source + other])
                if abs(weight) < 1e-12:
                    continue
                term = weight * modes[source][:, other]
                total = term if total is None else total + term
            parts.append(jnp.zeros_like(modes[mode][:, comp]) if total is None else total)
        loads.append(jnp.stack(parts, axis=1))
    return loads


def halo_both(cells, axis, dim, width):
    count = lax.axis_size(axis)
    head = lax.slice_in_dim(cells, 0, width, axis=dim)
    tail = lax.slice_in_dim(cells, cells.shape[dim] - width, cells.shape[dim], axis=dim)
    below = lax.ppermute(tail, axis, [(i, i + 1) for i in range(count - 1)])
    above = lax.ppermute(head, axis, [(i + 1, i) for i in range(count - 1)])
    return jnp.concatenate([below, cells, above], axis=dim)


def inside_mask(axis, extent, width, total):
    places = np.arange(extent + 2 * width) - width
    own = jnp.asarray(places, jnp.int32) + lax.axis_index(axis) * extent
    return ((own >= 0) & (own < total)).astype(jnp.float32)


def node_forces(node_field, modulus, stiffness):
    local_disp = cases_disp(node_field)
    local_load = jnp.einsum("ij,cjabd->ciabd", stiffness, local_disp, precision=highest)
    local_force = (local_load * modulus).reshape((node_field.shape[0], 8, 3) + modulus.shape)
    summed = jnp.zeros_like(node_field)
    for corner in range(8):
        off_x, off_y, off_z = (corner // 4, corner // 2 % 2, corner % 2)
        summed = summed + jnp.pad(
            local_force[:, corner],
            ((0, 0), (0, 0), (off_x, 1 - off_x), (off_y, 1 - off_y), (off_z, 1 - off_z)),
        )
    return summed[..., :-1], local_disp, local_load


def on_device(start_disp, bone_mask, density, load_nodes, load_forces):
    stiffness = jnp.asarray(hex_stiffness(), jnp.float32)
    modulus = bone_mask.astype(jnp.float32) * density * density
    case_count = start_disp.shape[0]
    size_x = start_disp.shape[2]
    size_y = start_disp.shape[3]
    size_z = start_disp.shape[4]
    count_x = lax.axis_size("gx")
    count_y = lax.axis_size("gy")
    fields = case_count * 3

    slot_ids = jnp.arange(size_x * size_y, dtype=jnp.int32)
    matches = (load_nodes[0, 0][:, :, None] == slot_ids).astype(jnp.float32)
    top_plane = jnp.einsum("cls,ckl->cks", matches, load_forces[0, 0], precision=highest).reshape(
        fields, size_x, size_y
    )
    packed_loads = jnp.pad(top_plane.transpose(1, 2, 0), ((0, 0), (0, 0), (0, size_z - fields)))
    packed = jnp.concatenate(
        [start_disp.reshape(fields, size_x, size_y, size_z), modulus[None], packed_loads[None]],
        axis=0,
    )
    packed = halo_both(halo_both(packed, "gx", 1, 2), "gy", 2, 2)
    wide_start = packed[:fields].reshape(case_count, 3, size_x + 4, size_y + 4, size_z)
    wide_modulus = packed[fields]
    wide_loads = packed[fields + 1, 1:-1, 1:-1, :fields].transpose(2, 0, 1)
    wide_loads = wide_loads.reshape(case_count, 3, size_x + 2, size_y + 2)

    start_nodes = pad_upper_z(wide_start)
    forces, start_elems, start_loads = node_forces(
        start_nodes, wide_modulus[:-1, :-1], stiffness
    )
    applied = forces[:, :, 1:-1, 1:-1] + spring * wide_start[:, :, 1:-1, 1:-1]
    keep = (
        inside_mask("gx", size_x, 1, size_x * count_x)[:, None, None]
        * inside_mask("gy", size_y, 1, size_y * count_y)[None, :, None]
    )
    residual_wide = (
        jnp.concatenate(
            [-applied[..., :-1], (wide_loads - applied[..., -1])[..., None]], axis=4
        )
        * keep
    )

    residual_nodes = pad_upper_z(residual_wide)
    forces, residual_elems, residual_loads = node_forces(
        residual_nodes, wide_modulus[1:-2, 1:-2], stiffness
    )
    residual = residual_wide[:, :, 1:-1, 1:-1]
    applied = forces[:, :, 1:-1, 1:-1] + spring * residual

    blur_mass = modulus
    for dim, axis in ((0, "gx"), (1, "gy"), (2, None)):
        extent = modulus.shape[dim]
        count = 1 if axis is None else lax.axis_size(axis)
        places = lax.iota(jnp.int32, extent)
        if axis is not None:
            places = places + lax.axis_index(axis) * extent
        kept = jnp.zeros((extent,), jnp.float32)
        for tap_index, weight in enumerate(blur_weights()):
            shifted = places + 4 - tap_index
            kept = kept + jnp.where((shifted >= 0) & (shifted < extent * count), weight, 0.0)
        shape = [1, 1, 1]
        shape[dim] = extent
        blur_mass = blur_mass * kept.reshape(shape)
    start_elems = start_elems[:, :, 2:-1, 2:-1]
    start_loads = start_loads[:, :, 2:-1, 2:-1]
    residual_elems = residual_elems[:, :, 1:, 1:]
    residual_loads = residual_loads[:, :, 1:, 1:]
    start_energy = jnp.sum(start_elems * start_loads * blur_mass, axis=(1, 2, 3, 4))
    start_weighted = start_loads * blur_mass
    residual_weighted = residual_loads * blur_mass
    cross_energy = jnp.sum(
        residual_elems[:, None] * start_weighted[None, :], axis=(2, 3, 4, 5)
    )
    residual_energy = jnp.sum(
        residual_elems[:, None] * residual_weighted[None, :], axis=(2, 3, 4, 5)
    )
    grams = tree_sum(
        jnp.stack(
            [
                local_gram(residual, residual),
                local_gram(residual, applied),
                cross_energy,
                residual_energy,
                jnp.diag(start_energy),
            ]
        )
    )
    norm_now = grams[0]
    step_alpha = solve_spd(grams[1], norm_now)
    summed = (
        jnp.sum(grams[4])
        + 2.0 * jnp.sum(step_alpha * grams[2])
        + jnp.sum(step_alpha[:, None, :] * grams[3][:, :, None] * step_alpha[None, :, :])
    )
    solution = start_disp + mix_cases(residual, step_alpha)
    node_field = start_nodes[:, :, 2:-1, 2:-1] + mix_cases(
        residual_nodes[:, :, 1:, 1:], step_alpha
    )
    final_modes = corner_modes(node_field)
    final_loads = mode_loads(final_modes, mode_stiffness())
    energy = sum(
        jnp.sum(part * load, axis=(0, 1)) for part, load in zip(final_modes, final_loads)
    )
    stimulus = modulus * energy
    smooth = blur_valid(with_halo(stimulus, (("gx", 0),), 4), 0, size_x)
    smooth = blur_valid(with_halo(smooth, (("gy", 1),), 4), 1, size_y)
    smooth = blur_valid(jnp.pad(smooth, ((0, 0), (0, 0), (4, 4))), 2, size_z)
    mean_stim = summed / (size_x * size_y * size_z * count_x * count_y)
    new_density = jnp.minimum(density * (0.5 + 0.5 * smooth / (mean_stim + mean_eps)), density_cap)
    return (solution, new_density)


def solution(mesh):
    return jax.shard_map(
        on_device,
        mesh=mesh,
        in_specs=(
            P(None, None, "gx", "gy", None),
            P("gx", "gy", None),
            P("gx", "gy", None),
            P("gx", "gy", None, None),
            P("gx", "gy", None, None, None),
        ),
        out_specs=(P(None, None, "gx", "gy", None), P("gx", "gy", None)),
        check_vma=False,
    )
```

```python
import jax
import jax.numpy as jnp
import numpy as np
from jax import lax
from jax.sharding import PartitionSpec as P

spring = 0.1
poisson = 0.3
blur_sigma = 2.0
density_cap = 1.0
mean_eps = 1e-06
highest = lax.Precision.HIGHEST


def from_behind(block, axis, distance):
    devices = range(lax.axis_size(axis))
    route = [(i - distance, i) for i in devices if i - distance in devices]
    return lax.ppermute(block, axis, route)


def with_halo(cells, sides, width):
    for axis, dim in sides:
        count = lax.axis_size(axis)
        ends = count - 1
        head = lax.slice_in_dim(cells, 0, width, axis=dim)
        tail = lax.slice_in_dim(cells, cells.shape[dim] - width, cells.shape[dim], axis=dim)
        cells = jnp.concatenate(
            [
                lax.ppermute(tail, axis, [(i, (i + 1) % count) for i in range(ends)]),
                cells,
                lax.ppermute(head, axis, [((i + 1) % count, i) for i in range(ends)]),
            ],
            axis=dim,
        )
    return cells


def hex_stiffness():
    lame_first = poisson / ((1.0 + poisson) * (1.0 - 2.0 * poisson))
    shear_mod = 1.0 / (2.0 * (1.0 + poisson))
    elastic = np.zeros((6, 6))
    elastic[:3, :3] = lame_first
    for axis_id in range(3):
        elastic[axis_id, axis_id] = lame_first + 2.0 * shear_mod
        elastic[axis_id + 3, axis_id + 3] = shear_mod
    points = [0.5 - 0.5 / np.sqrt(3.0), 0.5 + 0.5 / np.sqrt(3.0)]
    stiffness = np.zeros((24, 24))
    for point_x in points:
        for point_y in points:
            for point_z in points:
                coords = (point_x, point_y, point_z)
                strain = np.zeros((6, 24))
                for corner in range(8):
                    offsets = (corner // 4, corner // 2 % 2, corner % 2)
                    shapes = [
                        coords[axis_id] if offsets[axis_id] == 1 else 1.0 - coords[axis_id]
                        for axis_id in range(3)
                    ]
                    slopes = [1.0 if offsets[axis_id] == 1 else -1.0 for axis_id in range(3)]
                    grad_x = slopes[0] * shapes[1] * shapes[2]
                    grad_y = shapes[0] * slopes[1] * shapes[2]
                    grad_z = shapes[0] * shapes[1] * slopes[2]
                    column = 3 * corner
                    strain[0, column] = grad_x
                    strain[1, column + 1] = grad_y
                    strain[2, column + 2] = grad_z
                    strain[3, column] = grad_y
                    strain[3, column + 1] = grad_x
                    strain[4, column + 1] = grad_z
                    strain[4, column + 2] = grad_y
                    strain[5, column] = grad_z
                    strain[5, column + 2] = grad_x
                stiffness += 0.125 * strain.T @ elastic @ strain
    return stiffness


def blur_weights():
    offsets = np.arange(9) - 4.0
    unscaled = np.exp(-offsets * offsets / (2.0 * blur_sigma * blur_sigma))
    return [float(entry) for entry in unscaled / unscaled.sum()]


def blur_valid(values, axis_id, extent):
    weights = blur_weights()
    summed = weights[0] * lax.slice_in_dim(values, 0, extent, axis=axis_id)
    for tap_index in range(1, 9):
        summed = summed + weights[tap_index] * lax.slice_in_dim(
            values, tap_index, tap_index + extent, axis=axis_id
        )
    return summed


def element_disp(node_field):
    size_x = node_field.shape[1] - 1
    size_y = node_field.shape[2] - 1
    size_z = node_field.shape[3] - 1
    corners = []
    for corner in range(8):
        off_x, off_y, off_z = (corner // 4, corner // 2 % 2, corner % 2)
        corners.append(
            node_field[:, off_x : off_x + size_x, off_y : off_y + size_y, off_z : off_z + size_z]
        )
    return jnp.stack(corners).reshape(24, size_x, size_y, size_z)


def cases_disp(node_field):
    size_x = node_field.shape[2] - 1
    size_y = node_field.shape[3] - 1
    size_z = node_field.shape[4] - 1
    corners = []
    for corner in range(8):
        off_x, off_y, off_z = (corner // 4, corner // 2 % 2, corner % 2)
        corners.append(
            node_field[:, :, off_x : off_x + size_x, off_y : off_y + size_y, off_z : off_z + size_z]
        )
    return jnp.stack(corners, axis=1).reshape(
        (node_field.shape[0], 24, size_x, size_y, size_z)
    )


def element_forces(node_field, modulus, stiffness):
    local_disp = cases_disp(node_field)
    local_force = jnp.einsum("ij,cjabd->ciabd", stiffness, local_disp, precision=highest) * modulus
    local_force = local_force.reshape((node_field.shape[0], 8, 3) + modulus.shape)
    summed = jnp.zeros_like(node_field)
    for corner in range(8):
        off_x, off_y, off_z = (corner // 4, corner // 2 % 2, corner % 2)
        summed = summed + jnp.pad(
            local_force[:, corner],
            ((0, 0), (0, 0), (off_x, 1 - off_x), (off_y, 1 - off_y), (off_z, 1 - off_z)),
        )
    return summed


def element_energy(node_field, stiffness):
    local_disp = cases_disp(node_field)
    local_force = jnp.einsum("ij,cjabd->ciabd", stiffness, local_disp, precision=highest)
    return jnp.sum(local_disp * local_force, axis=(0, 1))


def local_gram(left_field, right_field):
    return jnp.einsum("iabcd,jabcd->ij", left_field, right_field, precision=highest)


def tree_sum(value):
    for axis in ("gx", "gy"):
        count = lax.axis_size(axis)
        copies = jnp.broadcast_to(value[None], (count,) + value.shape)
        value = jnp.sum(lax.all_to_all(copies, axis, 0, 0, tiled=False), axis=0)
    return value


def mix_cases(field, coeffs):
    return jnp.einsum("kabcd,kj->jabcd", field, coeffs, precision=highest)


def solve_spd(matrix, rhs_matrix):
    factor = jnp.linalg.cholesky(matrix)
    forward = lax.linalg.triangular_solve(factor, rhs_matrix, left_side=True, lower=True)
    return lax.linalg.triangular_solve(
        factor, forward, left_side=True, lower=True, transpose_a=True
    )


def solve_spd_rows(matrix, rhs_matrix):
    factor = jnp.linalg.cholesky(matrix)
    matrix_order = matrix.shape[0]
    forward = []
    for row_index in range(matrix_order):
        partial_sum = rhs_matrix[row_index]
        for col_index in range(row_index):
            partial_sum = partial_sum - factor[row_index, col_index] * forward[col_index]
        forward.append(partial_sum / factor[row_index, row_index])
    backward = [None] * matrix_order
    for row_index in reversed(range(matrix_order)):
        partial_sum = forward[row_index]
        for col_index in range(row_index + 1, matrix_order):
            partial_sum = partial_sum - factor[col_index, row_index] * backward[col_index]
        backward[row_index] = partial_sum / factor[row_index, row_index]
    return jnp.stack(backward)


def pad_upper_z(field):
    return jnp.pad(field, ((0, 0), (0, 0), (0, 0), (0, 0), (0, 1)))


def gather_upper(field):
    from_x = from_behind(field[:, :, :1], "gx", -1)
    widened = jnp.concatenate([field, from_x], axis=2)
    from_y = from_behind(widened[:, :, :, :1], "gy", -1)
    return jnp.concatenate([widened, from_y], axis=3)


def return_lower(forces):
    size_x = forces.shape[2] - 1
    size_y = forces.shape[3] - 1
    to_y = from_behind(forces[:, :, :, size_y:], "gy", 1)
    kept = forces[:, :, :, :size_y]
    kept = jnp.concatenate([kept[:, :, :, :1] + to_y, kept[:, :, :, 1:]], axis=3)
    to_x = from_behind(kept[:, :, size_x:], "gx", 1)
    kept = kept[:, :, :size_x]
    return jnp.concatenate([kept[:, :, :1] + to_x, kept[:, :, 1:]], axis=2)


def corner_modes(node_field):
    found = {(): node_field}
    for dim in (2, 3, 4):
        grown = {}
        for key, cells in found.items():
            low = lax.slice_in_dim(cells, 0, cells.shape[dim] - 1, axis=dim)
            high = lax.slice_in_dim(cells, 1, cells.shape[dim], axis=dim)
            grown[key + (0,)] = high + low
            grown[key + (1,)] = high - low
        found = grown
    return [found[(mode // 4, mode // 2 % 2, mode % 2)] for mode in range(8)]


def mode_stiffness():
    step = np.array([[1.0, 1.0], [-1.0, 1.0]])
    change = np.kron(np.kron(np.kron(step, step), step), np.eye(3))
    return change @ hex_stiffness() @ change.T / 64.0


def mode_loads(modes, table):
    loads = []
    for mode in range(8):
        parts = []
        for comp in range(3):
            total = None
            for other in range(3):
                source = mode ^ (4 >> comp) ^ (4 >> other)
                weight = float(table[3 * mode + comp, 3 * source + other])
                if abs(weight) < 1e-12:
                    continue
                term = weight * modes[source][:, other]
                total = term if total is None else total + term
            parts.append(jnp.zeros_like(modes[mode][:, comp]) if total is None else total)
        loads.append(jnp.stack(parts, axis=1))
    return loads


def halo_both(cells, axis, dim, width):
    count = lax.axis_size(axis)
    head = lax.slice_in_dim(cells, 0, width, axis=dim)
    tail = lax.slice_in_dim(cells, cells.shape[dim] - width, cells.shape[dim], axis=dim)
    below = lax.ppermute(tail, axis, [(i, i + 1) for i in range(count - 1)])
    above = lax.ppermute(head, axis, [(i + 1, i) for i in range(count - 1)])
    return jnp.concatenate([below, cells, above], axis=dim)


def inside_mask(axis, extent, width, total):
    places = np.arange(extent + 2 * width) - width
    own = jnp.asarray(places, jnp.int32) + lax.axis_index(axis) * extent
    return ((own >= 0) & (own < total)).astype(jnp.float32)


def node_forces(node_field, modulus, stiffness):
    local_disp = cases_disp(node_field)
    local_load = jnp.einsum("ij,cjabd->ciabd", stiffness, local_disp, precision=highest)
    local_force = (local_load * modulus).reshape((node_field.shape[0], 8, 3) + modulus.shape)
    summed = jnp.zeros_like(node_field)
    for corner in range(8):
        off_x, off_y, off_z = (corner // 4, corner // 2 % 2, corner % 2)
        summed = summed + jnp.pad(
            local_force[:, corner],
            ((0, 0), (0, 0), (off_x, 1 - off_x), (off_y, 1 - off_y), (off_z, 1 - off_z)),
        )
    return summed[..., :-1], local_disp, local_load


def on_device(start_disp, bone_mask, density, load_nodes, load_forces):
    stiffness = jnp.asarray(hex_stiffness(), jnp.float32)
    modulus = bone_mask.astype(jnp.float32) * density * density
    case_count = start_disp.shape[0]
    size_x = start_disp.shape[2]
    size_y = start_disp.shape[3]
    size_z = start_disp.shape[4]
    count_x = lax.axis_size("gx")
    count_y = lax.axis_size("gy")
    fields = case_count * 3

    slot_ids = jnp.arange(size_x * size_y, dtype=jnp.int32)
    matches = (load_nodes[0, 0][:, :, None] == slot_ids).astype(jnp.float32)
    top_plane = jnp.einsum("cls,ckl->cks", matches, load_forces[0, 0], precision=highest).reshape(
        fields, size_x, size_y
    )
    packed_loads = jnp.pad(top_plane.transpose(1, 2, 0), ((0, 0), (0, 0), (0, size_z - fields)))
    packed = jnp.concatenate(
        [start_disp.reshape(fields, size_x, size_y, size_z), modulus[None], packed_loads[None]],
        axis=0,
    )
    packed = halo_both(halo_both(packed, "gx", 1, 2), "gy", 2, 2)
    wide_start = packed[:fields].reshape(case_count, 3, size_x + 4, size_y + 4, size_z)
    wide_modulus = packed[fields]
    wide_loads = packed[fields + 1, 1:-1, 1:-1, :fields].transpose(2, 0, 1)
    wide_loads = wide_loads.reshape(case_count, 3, size_x + 2, size_y + 2)

    start_nodes = pad_upper_z(wide_start)
    forces, start_elems, start_loads = node_forces(
        start_nodes, wide_modulus[:-1, :-1], stiffness
    )
    applied = forces[:, :, 1:-1, 1:-1] + spring * wide_start[:, :, 1:-1, 1:-1]
    keep = (
        inside_mask("gx", size_x, 1, size_x * count_x)[:, None, None]
        * inside_mask("gy", size_y, 1, size_y * count_y)[None, :, None]
    )
    residual_wide = (
        jnp.concatenate(
            [-applied[..., :-1], (wide_loads - applied[..., -1])[..., None]], axis=4
        )
        * keep
    )

    residual_nodes = pad_upper_z(residual_wide)
    forces, residual_elems, residual_loads = node_forces(
        residual_nodes, wide_modulus[1:-2, 1:-2], stiffness
    )
    residual = residual_wide[:, :, 1:-1, 1:-1]
    applied = forces[:, :, 1:-1, 1:-1] + spring * residual

    blur_mass = modulus
    for dim, axis in ((0, "gx"), (1, "gy"), (2, None)):
        extent = modulus.shape[dim]
        count = 1 if axis is None else lax.axis_size(axis)
        places = lax.iota(jnp.int32, extent)
        if axis is not None:
            places = places + lax.axis_index(axis) * extent
        kept = jnp.zeros((extent,), jnp.float32)
        for tap_index, weight in enumerate(blur_weights()):
            shifted = places + 4 - tap_index
            kept = kept + jnp.where((shifted >= 0) & (shifted < extent * count), weight, 0.0)
        shape = [1, 1, 1]
        shape[dim] = extent
        blur_mass = blur_mass * kept.reshape(shape)
    start_elems = start_elems[:, :, 2:-1, 2:-1]
    start_loads = start_loads[:, :, 2:-1, 2:-1]
    residual_elems = residual_elems[:, :, 1:, 1:]
    residual_loads = residual_loads[:, :, 1:, 1:]
    start_energy = jnp.sum(start_elems * start_loads * blur_mass, axis=(1, 2, 3, 4))
    start_weighted = start_loads * blur_mass
    residual_weighted = residual_loads * blur_mass
    cross_energy = jnp.sum(
        residual_elems[:, None] * start_weighted[None, :], axis=(2, 3, 4, 5)
    )
    residual_energy = jnp.sum(
        residual_elems[:, None] * residual_weighted[None, :], axis=(2, 3, 4, 5)
    )
    grams = tree_sum(
        jnp.stack(
            [
                local_gram(residual, residual),
                local_gram(residual, applied),
                cross_energy,
                residual_energy,
                jnp.diag(start_energy),
            ]
        )
    )
    norm_now = grams[0]
    step_alpha = solve_spd(grams[1], norm_now)
    summed = (
        jnp.sum(grams[4])
        + 2.0 * jnp.sum(step_alpha * grams[2])
        + jnp.sum(step_alpha[:, None, :] * grams[3][:, :, None] * step_alpha[None, :, :])
    )
    solution = start_disp + mix_cases(residual, step_alpha)
    node_field = start_nodes[:, :, 2:-1, 2:-1] + mix_cases(
        residual_nodes[:, :, 1:, 1:], step_alpha
    )
    final_modes = corner_modes(node_field)
    final_loads = mode_loads(final_modes, mode_stiffness())
    energy = sum(
        jnp.sum(part * load, axis=(0, 1)) for part, load in zip(final_modes, final_loads)
    )
    stimulus = modulus * energy
    smooth = blur_valid(with_halo(stimulus, (("gx", 0),), 4), 0, size_x)
    smooth = blur_valid(with_halo(smooth, (("gy", 1),), 4), 1, size_y)
    smooth = blur_valid(jnp.pad(smooth, ((0, 0), (0, 0), (4, 4))), 2, size_z)
    mean_stim = summed / (size_x * size_y * size_z * count_x * count_y)
    new_density = jnp.minimum(density * (0.5 + 0.5 * smooth / (mean_stim + mean_eps)), density_cap)
    return (solution, new_density)


def solution(mesh):
    return jax.shard_map(
        on_device,
        mesh=mesh,
        in_specs=(
            P(None, None, "gx", "gy", None),
            P("gx", "gy", None),
            P("gx", "gy", None),
            P("gx", "gy", None, None),
            P("gx", "gy", None, None, None),
        ),
        out_specs=(P(None, None, "gx", "gy", None), P("gx", "gy", None)),
        check_vma=False,
    )
```

```python
import jax
import jax.numpy as jnp
import numpy as np
from jax import lax
from jax.sharding import PartitionSpec as P

spring = 0.1
poisson = 0.3
blur_sigma = 2.0
density_cap = 1.0
mean_eps = 1e-06
highest = lax.Precision.HIGHEST


def from_behind(block, axis, distance):
    devices = range(lax.axis_size(axis))
    route = [(i - distance, i) for i in devices if i - distance in devices]
    return lax.ppermute(block, axis, route)


def with_halo(cells, sides, width):
    for axis, dim in sides:
        count = lax.axis_size(axis)
        ends = count - 1
        head = lax.slice_in_dim(cells, 0, width, axis=dim)
        tail = lax.slice_in_dim(cells, cells.shape[dim] - width, cells.shape[dim], axis=dim)
        cells = jnp.concatenate(
            [
                lax.ppermute(tail, axis, [(i, (i + 1) % count) for i in range(ends)]),
                cells,
                lax.ppermute(head, axis, [((i + 1) % count, i) for i in range(ends)]),
            ],
            axis=dim,
        )
    return cells


def hex_stiffness():
    lame_first = poisson / ((1.0 + poisson) * (1.0 - 2.0 * poisson))
    shear_mod = 1.0 / (2.0 * (1.0 + poisson))
    elastic = np.zeros((6, 6))
    elastic[:3, :3] = lame_first
    for axis_id in range(3):
        elastic[axis_id, axis_id] = lame_first + 2.0 * shear_mod
        elastic[axis_id + 3, axis_id + 3] = shear_mod
    points = [0.5 - 0.5 / np.sqrt(3.0), 0.5 + 0.5 / np.sqrt(3.0)]
    stiffness = np.zeros((24, 24))
    for point_x in points:
        for point_y in points:
            for point_z in points:
                coords = (point_x, point_y, point_z)
                strain = np.zeros((6, 24))
                for corner in range(8):
                    offsets = (corner // 4, corner // 2 % 2, corner % 2)
                    shapes = [
                        coords[axis_id] if offsets[axis_id] == 1 else 1.0 - coords[axis_id]
                        for axis_id in range(3)
                    ]
                    slopes = [1.0 if offsets[axis_id] == 1 else -1.0 for axis_id in range(3)]
                    grad_x = slopes[0] * shapes[1] * shapes[2]
                    grad_y = shapes[0] * slopes[1] * shapes[2]
                    grad_z = shapes[0] * shapes[1] * slopes[2]
                    column = 3 * corner
                    strain[0, column] = grad_x
                    strain[1, column + 1] = grad_y
                    strain[2, column + 2] = grad_z
                    strain[3, column] = grad_y
                    strain[3, column + 1] = grad_x
                    strain[4, column + 1] = grad_z
                    strain[4, column + 2] = grad_y
                    strain[5, column] = grad_z
                    strain[5, column + 2] = grad_x
                stiffness += 0.125 * strain.T @ elastic @ strain
    return stiffness


def blur_weights():
    offsets = np.arange(9) - 4.0
    unscaled = np.exp(-offsets * offsets / (2.0 * blur_sigma * blur_sigma))
    return [float(entry) for entry in unscaled / unscaled.sum()]


def blur_valid(values, axis_id, extent):
    weights = blur_weights()
    summed = weights[0] * lax.slice_in_dim(values, 0, extent, axis=axis_id)
    for tap_index in range(1, 9):
        summed = summed + weights[tap_index] * lax.slice_in_dim(
            values, tap_index, tap_index + extent, axis=axis_id
        )
    return summed


def element_disp(node_field):
    size_x = node_field.shape[1] - 1
    size_y = node_field.shape[2] - 1
    size_z = node_field.shape[3] - 1
    corners = []
    for corner in range(8):
        off_x, off_y, off_z = (corner // 4, corner // 2 % 2, corner % 2)
        corners.append(
            node_field[:, off_x : off_x + size_x, off_y : off_y + size_y, off_z : off_z + size_z]
        )
    return jnp.stack(corners).reshape(24, size_x, size_y, size_z)


def cases_disp(node_field):
    size_x = node_field.shape[2] - 1
    size_y = node_field.shape[3] - 1
    size_z = node_field.shape[4] - 1
    corners = []
    for corner in range(8):
        off_x, off_y, off_z = (corner // 4, corner // 2 % 2, corner % 2)
        corners.append(
            node_field[:, :, off_x : off_x + size_x, off_y : off_y + size_y, off_z : off_z + size_z]
        )
    return jnp.stack(corners, axis=1).reshape(
        (node_field.shape[0], 24, size_x, size_y, size_z)
    )


def element_forces(node_field, modulus, stiffness):
    local_disp = cases_disp(node_field)
    local_force = jnp.einsum("ij,cjabd->ciabd", stiffness, local_disp, precision=highest) * modulus
    local_force = local_force.reshape((node_field.shape[0], 8, 3) + modulus.shape)
    summed = jnp.zeros_like(node_field)
    for corner in range(8):
        off_x, off_y, off_z = (corner // 4, corner // 2 % 2, corner % 2)
        summed = summed + jnp.pad(
            local_force[:, corner],
            ((0, 0), (0, 0), (off_x, 1 - off_x), (off_y, 1 - off_y), (off_z, 1 - off_z)),
        )
    return summed


def element_energy(node_field, stiffness):
    local_disp = cases_disp(node_field)
    local_force = jnp.einsum("ij,cjabd->ciabd", stiffness, local_disp, precision=highest)
    return jnp.sum(local_disp * local_force, axis=(0, 1))


def local_gram(left_field, right_field):
    return jnp.einsum("iabcd,jabcd->ij", left_field, right_field, precision=highest)


def tree_sum(value):
    for axis in ("gx", "gy"):
        count = lax.axis_size(axis)
        copies = jnp.broadcast_to(value[None], (count,) + value.shape)
        value = jnp.sum(lax.all_to_all(copies, axis, 0, 0, tiled=False), axis=0)
    return value


def mix_cases(field, coeffs):
    return jnp.einsum("kabcd,kj->jabcd", field, coeffs, precision=highest)


def solve_spd(matrix, rhs_matrix):
    factor = jnp.linalg.cholesky(matrix)
    forward = lax.linalg.triangular_solve(factor, rhs_matrix, left_side=True, lower=True)
    return lax.linalg.triangular_solve(
        factor, forward, left_side=True, lower=True, transpose_a=True
    )


def solve_spd_rows(matrix, rhs_matrix):
    factor = jnp.linalg.cholesky(matrix)
    matrix_order = matrix.shape[0]
    forward = []
    for row_index in range(matrix_order):
        partial_sum = rhs_matrix[row_index]
        for col_index in range(row_index):
            partial_sum = partial_sum - factor[row_index, col_index] * forward[col_index]
        forward.append(partial_sum / factor[row_index, row_index])
    backward = [None] * matrix_order
    for row_index in reversed(range(matrix_order)):
        partial_sum = forward[row_index]
        for col_index in range(row_index + 1, matrix_order):
            partial_sum = partial_sum - factor[col_index, row_index] * backward[col_index]
        backward[row_index] = partial_sum / factor[row_index, row_index]
    return jnp.stack(backward)


def pad_upper_z(field):
    return jnp.pad(field, ((0, 0), (0, 0), (0, 0), (0, 0), (0, 1)))


def gather_upper(field):
    from_x = from_behind(field[:, :, :1], "gx", -1)
    widened = jnp.concatenate([field, from_x], axis=2)
    from_y = from_behind(widened[:, :, :, :1], "gy", -1)
    return jnp.concatenate([widened, from_y], axis=3)


def return_lower(forces):
    size_x = forces.shape[2] - 1
    size_y = forces.shape[3] - 1
    to_y = from_behind(forces[:, :, :, size_y:], "gy", 1)
    kept = forces[:, :, :, :size_y]
    kept = jnp.concatenate([kept[:, :, :, :1] + to_y, kept[:, :, :, 1:]], axis=3)
    to_x = from_behind(kept[:, :, size_x:], "gx", 1)
    kept = kept[:, :, :size_x]
    return jnp.concatenate([kept[:, :, :1] + to_x, kept[:, :, 1:]], axis=2)


def corner_modes(node_field):
    cells = node_field
    for step, dim in enumerate((2, 3, 4)):
        dim = dim + step
        low = lax.slice_in_dim(cells, 0, cells.shape[dim] - 1, axis=dim)
        high = lax.slice_in_dim(cells, 1, cells.shape[dim], axis=dim)
        cells = jnp.stack([high + low, high - low], axis=step)
    return cells


def mode_stiffness():
    step = np.array([[1.0, 1.0], [-1.0, 1.0]])
    change = np.kron(np.kron(np.kron(step, step), step), np.eye(3))
    return change @ hex_stiffness() @ change.T / 64.0


def mode_loads(modes, table):
    loads = []
    for comp in range(3):
        total = None
        for other in range(3):
            weights = np.zeros((8,))
            for mode in range(8):
                source = mode ^ (4 >> comp) ^ (4 >> other)
                weights[mode] = table[3 * mode + comp, 3 * source + other]
            weights[np.abs(weights) < 1e-12] = 0.0
            if not weights.any():
                continue
            part = modes[:, :, :, :, other]
            flips = tuple(sorted({comp, other})) if comp != other else ()
            if flips:
                part = jnp.flip(part, axis=flips)
            term = jnp.asarray(weights.reshape(2, 2, 2, 1, 1, 1, 1), jnp.float32) * part
            total = term if total is None else total + term
        loads.append(total)
    return jnp.stack(loads, axis=4)


def modes_to_nodes(loads):
    cells = loads
    for mode_axis in (2, 1, 0):
        dim = cells.ndim - (3 - mode_axis)
        total = lax.index_in_dim(cells, 0, axis=mode_axis, keepdims=False)
        change = lax.index_in_dim(cells, 1, axis=mode_axis, keepdims=False)
        dim = dim - 1
        low = [(0, 0)] * total.ndim
        low[dim] = (0, 1)
        high = [(0, 0)] * total.ndim
        high[dim] = (1, 0)
        cells = jnp.pad(total - change, low) + jnp.pad(total + change, high)
    return cells


def halo_both(cells, axis, dim, width):
    count = lax.axis_size(axis)
    head = lax.slice_in_dim(cells, 0, width, axis=dim)
    tail = lax.slice_in_dim(cells, cells.shape[dim] - width, cells.shape[dim], axis=dim)
    below = lax.ppermute(tail, axis, [(i, i + 1) for i in range(count - 1)])
    above = lax.ppermute(head, axis, [(i + 1, i) for i in range(count - 1)])
    return jnp.concatenate([below, cells, above], axis=dim)


def inside_mask(axis, extent, width, total):
    places = np.arange(extent + 2 * width) - width
    own = jnp.asarray(places, jnp.int32) + lax.axis_index(axis) * extent
    return ((own >= 0) & (own < total)).astype(jnp.float32)


def node_forces(node_field, modulus, table):
    modes = corner_modes(node_field)
    loads = mode_loads(modes, table)
    summed = modes_to_nodes(loads * modulus)
    return summed[..., :-1], modes, loads


def on_device(start_disp, bone_mask, density, load_nodes, load_forces):
    stiffness = mode_stiffness()
    modulus = bone_mask.astype(jnp.float32) * density * density
    case_count = start_disp.shape[0]
    size_x = start_disp.shape[2]
    size_y = start_disp.shape[3]
    size_z = start_disp.shape[4]
    count_x = lax.axis_size("gx")
    count_y = lax.axis_size("gy")
    fields = case_count * 3

    slot_ids = jnp.arange(size_x * size_y, dtype=jnp.int32)
    matches = (load_nodes[0, 0][:, :, None] == slot_ids).astype(jnp.float32)
    top_plane = jnp.einsum("cls,ckl->cks", matches, load_forces[0, 0], precision=highest).reshape(
        fields, size_x, size_y
    )
    packed_loads = jnp.pad(top_plane.transpose(1, 2, 0), ((0, 0), (0, 0), (0, size_z - fields)))
    packed = jnp.concatenate(
        [start_disp.reshape(fields, size_x, size_y, size_z), modulus[None], packed_loads[None]],
        axis=0,
    )
    packed = halo_both(halo_both(packed, "gx", 1, 2), "gy", 2, 2)
    wide_start = packed[:fields].reshape(case_count, 3, size_x + 4, size_y + 4, size_z)
    wide_modulus = packed[fields]
    wide_loads = packed[fields + 1, 1:-1, 1:-1, :fields].transpose(2, 0, 1)
    wide_loads = wide_loads.reshape(case_count, 3, size_x + 2, size_y + 2)

    start_nodes = pad_upper_z(wide_start)
    forces, start_elems, start_loads = node_forces(
        start_nodes, wide_modulus[:-1, :-1], stiffness
    )
    applied = forces[:, :, 1:-1, 1:-1] + spring * wide_start[:, :, 1:-1, 1:-1]
    keep = (
        inside_mask("gx", size_x, 1, size_x * count_x)[:, None, None]
        * inside_mask("gy", size_y, 1, size_y * count_y)[None, :, None]
    )
    residual_wide = (
        jnp.concatenate(
            [-applied[..., :-1], (wide_loads - applied[..., -1])[..., None]], axis=4
        )
        * keep
    )

    residual_nodes = pad_upper_z(residual_wide)
    forces, residual_elems, residual_loads = node_forces(
        residual_nodes, wide_modulus[1:-2, 1:-2], stiffness
    )
    residual = residual_wide[:, :, 1:-1, 1:-1]
    applied = forces[:, :, 1:-1, 1:-1] + spring * residual

    blur_mass = modulus
    for dim, axis in ((0, "gx"), (1, "gy"), (2, None)):
        extent = modulus.shape[dim]
        count = 1 if axis is None else lax.axis_size(axis)
        places = lax.iota(jnp.int32, extent)
        if axis is not None:
            places = places + lax.axis_index(axis) * extent
        kept = jnp.zeros((extent,), jnp.float32)
        for tap_index, weight in enumerate(blur_weights()):
            shifted = places + 4 - tap_index
            kept = kept + jnp.where((shifted >= 0) & (shifted < extent * count), weight, 0.0)
        shape = [1, 1, 1]
        shape[dim] = extent
        blur_mass = blur_mass * kept.reshape(shape)
    start_elems = start_elems[..., 2:-1, 2:-1, :]
    start_loads = start_loads[..., 2:-1, 2:-1, :]
    residual_elems = residual_elems[..., 1:, 1:, :]
    residual_loads = residual_loads[..., 1:, 1:, :]
    start_weighted = start_loads * blur_mass
    residual_weighted = residual_loads * blur_mass
    start_energy = jnp.sum(start_elems * start_weighted, axis=(0, 1, 2, 4, 5, 6, 7))
    cross_energy = jnp.sum(
        residual_elems[:, :, :, :, None] * start_weighted[:, :, :, None, :],
        axis=(0, 1, 2, 5, 6, 7, 8),
    )
    residual_energy = jnp.sum(
        residual_elems[:, :, :, :, None] * residual_weighted[:, :, :, None, :],
        axis=(0, 1, 2, 5, 6, 7, 8),
    )
    grams = tree_sum(
        jnp.stack(
            [
                local_gram(residual, residual),
                local_gram(residual, applied),
                cross_energy,
                residual_energy,
                jnp.diag(start_energy),
            ]
        )
    )
    norm_now = grams[0]
    step_alpha = solve_spd(grams[1], norm_now)
    summed = (
        jnp.sum(grams[4])
        + 2.0 * jnp.sum(step_alpha * grams[2])
        + jnp.sum(step_alpha[:, None, :] * grams[3][:, :, None] * step_alpha[None, :, :])
    )
    solution = start_disp + mix_cases(residual, step_alpha)
    node_field = start_nodes[:, :, 2:-1, 2:-1] + mix_cases(
        residual_nodes[:, :, 1:, 1:], step_alpha
    )
    final_modes = corner_modes(node_field)
    final_loads = mode_loads(final_modes, stiffness)
    energy = jnp.sum(final_modes * final_loads, axis=(0, 1, 2, 3, 4))
    stimulus = modulus * energy
    smooth = blur_valid(with_halo(stimulus, (("gx", 0),), 4), 0, size_x)
    smooth = blur_valid(with_halo(smooth, (("gy", 1),), 4), 1, size_y)
    smooth = blur_valid(jnp.pad(smooth, ((0, 0), (0, 0), (4, 4))), 2, size_z)
    mean_stim = summed / (size_x * size_y * size_z * count_x * count_y)
    new_density = jnp.minimum(density * (0.5 + 0.5 * smooth / (mean_stim + mean_eps)), density_cap)
    return (solution, new_density)


def solution(mesh):
    return jax.shard_map(
        on_device,
        mesh=mesh,
        in_specs=(
            P(None, None, "gx", "gy", None),
            P("gx", "gy", None),
            P("gx", "gy", None),
            P("gx", "gy", None, None),
            P("gx", "gy", None, None, None),
        ),
        out_specs=(P(None, None, "gx", "gy", None), P("gx", "gy", None)),
        check_vma=False,
    )
```

```python
import jax
import jax.numpy as jnp
import numpy as np
from jax import lax
from jax.sharding import PartitionSpec as P

spring = 0.1
poisson = 0.3
blur_sigma = 2.0
density_cap = 1.0
mean_eps = 1e-06
highest = lax.Precision.HIGHEST


def from_behind(block, axis, distance):
    devices = range(lax.axis_size(axis))
    route = [(i - distance, i) for i in devices if i - distance in devices]
    return lax.ppermute(block, axis, route)


def with_halo(cells, sides, width):
    for axis, dim in sides:
        count = lax.axis_size(axis)
        ends = count - 1
        head = lax.slice_in_dim(cells, 0, width, axis=dim)
        tail = lax.slice_in_dim(cells, cells.shape[dim] - width, cells.shape[dim], axis=dim)
        cells = jnp.concatenate(
            [
                lax.ppermute(tail, axis, [(i, (i + 1) % count) for i in range(ends)]),
                cells,
                lax.ppermute(head, axis, [((i + 1) % count, i) for i in range(ends)]),
            ],
            axis=dim,
        )
    return cells


def hex_stiffness():
    lame_first = poisson / ((1.0 + poisson) * (1.0 - 2.0 * poisson))
    shear_mod = 1.0 / (2.0 * (1.0 + poisson))
    elastic = np.zeros((6, 6))
    elastic[:3, :3] = lame_first
    for axis_id in range(3):
        elastic[axis_id, axis_id] = lame_first + 2.0 * shear_mod
        elastic[axis_id + 3, axis_id + 3] = shear_mod
    points = [0.5 - 0.5 / np.sqrt(3.0), 0.5 + 0.5 / np.sqrt(3.0)]
    stiffness = np.zeros((24, 24))
    for point_x in points:
        for point_y in points:
            for point_z in points:
                coords = (point_x, point_y, point_z)
                strain = np.zeros((6, 24))
                for corner in range(8):
                    offsets = (corner // 4, corner // 2 % 2, corner % 2)
                    shapes = [
                        coords[axis_id] if offsets[axis_id] == 1 else 1.0 - coords[axis_id]
                        for axis_id in range(3)
                    ]
                    slopes = [1.0 if offsets[axis_id] == 1 else -1.0 for axis_id in range(3)]
                    grad_x = slopes[0] * shapes[1] * shapes[2]
                    grad_y = shapes[0] * slopes[1] * shapes[2]
                    grad_z = shapes[0] * shapes[1] * slopes[2]
                    column = 3 * corner
                    strain[0, column] = grad_x
                    strain[1, column + 1] = grad_y
                    strain[2, column + 2] = grad_z
                    strain[3, column] = grad_y
                    strain[3, column + 1] = grad_x
                    strain[4, column + 1] = grad_z
                    strain[4, column + 2] = grad_y
                    strain[5, column] = grad_z
                    strain[5, column + 2] = grad_x
                stiffness += 0.125 * strain.T @ elastic @ strain
    return stiffness


def blur_weights():
    offsets = np.arange(9) - 4.0
    unscaled = np.exp(-offsets * offsets / (2.0 * blur_sigma * blur_sigma))
    return [float(entry) for entry in unscaled / unscaled.sum()]


def blur_valid(values, axis_id, extent):
    weights = blur_weights()
    summed = weights[0] * lax.slice_in_dim(values, 0, extent, axis=axis_id)
    for tap_index in range(1, 9):
        summed = summed + weights[tap_index] * lax.slice_in_dim(
            values, tap_index, tap_index + extent, axis=axis_id
        )
    return summed


def element_disp(node_field):
    size_x = node_field.shape[1] - 1
    size_y = node_field.shape[2] - 1
    size_z = node_field.shape[3] - 1
    corners = []
    for corner in range(8):
        off_x, off_y, off_z = (corner // 4, corner // 2 % 2, corner % 2)
        corners.append(
            node_field[:, off_x : off_x + size_x, off_y : off_y + size_y, off_z : off_z + size_z]
        )
    return jnp.stack(corners).reshape(24, size_x, size_y, size_z)


def cases_disp(node_field):
    size_x = node_field.shape[2] - 1
    size_y = node_field.shape[3] - 1
    size_z = node_field.shape[4] - 1
    corners = []
    for corner in range(8):
        off_x, off_y, off_z = (corner // 4, corner // 2 % 2, corner % 2)
        corners.append(
            node_field[:, :, off_x : off_x + size_x, off_y : off_y + size_y, off_z : off_z + size_z]
        )
    return jnp.stack(corners, axis=1).reshape(
        (node_field.shape[0], 24, size_x, size_y, size_z)
    )


def element_forces(node_field, modulus, stiffness):
    local_disp = cases_disp(node_field)
    local_force = jnp.einsum("ij,cjabd->ciabd", stiffness, local_disp, precision=highest) * modulus
    local_force = local_force.reshape((node_field.shape[0], 8, 3) + modulus.shape)
    summed = jnp.zeros_like(node_field)
    for corner in range(8):
        off_x, off_y, off_z = (corner // 4, corner // 2 % 2, corner % 2)
        summed = summed + jnp.pad(
            local_force[:, corner],
            ((0, 0), (0, 0), (off_x, 1 - off_x), (off_y, 1 - off_y), (off_z, 1 - off_z)),
        )
    return summed


def element_energy(node_field, stiffness):
    local_disp = cases_disp(node_field)
    local_force = jnp.einsum("ij,cjabd->ciabd", stiffness, local_disp, precision=highest)
    return jnp.sum(local_disp * local_force, axis=(0, 1))


def local_gram(left_field, right_field):
    return jnp.einsum("iabcd,jabcd->ij", left_field, right_field, precision=highest)


def tree_sum(value):
    for axis in ("gx", "gy"):
        count = lax.axis_size(axis)
        copies = jnp.broadcast_to(value[None], (count,) + value.shape)
        value = jnp.sum(lax.all_to_all(copies, axis, 0, 0, tiled=False), axis=0)
    return value


def mix_cases(field, coeffs):
    return jnp.sum(field[:, None] * coeffs[:, :, None, None, None, None], axis=0)


def solve_spd(matrix, rhs_matrix):
    factor = jnp.linalg.cholesky(matrix)
    forward = lax.linalg.triangular_solve(factor, rhs_matrix, left_side=True, lower=True)
    return lax.linalg.triangular_solve(
        factor, forward, left_side=True, lower=True, transpose_a=True
    )


def solve_spd_rows(matrix, rhs_matrix):
    factor = jnp.linalg.cholesky(matrix)
    matrix_order = matrix.shape[0]
    forward = []
    for row_index in range(matrix_order):
        partial_sum = rhs_matrix[row_index]
        for col_index in range(row_index):
            partial_sum = partial_sum - factor[row_index, col_index] * forward[col_index]
        forward.append(partial_sum / factor[row_index, row_index])
    backward = [None] * matrix_order
    for row_index in reversed(range(matrix_order)):
        partial_sum = forward[row_index]
        for col_index in range(row_index + 1, matrix_order):
            partial_sum = partial_sum - factor[col_index, row_index] * backward[col_index]
        backward[row_index] = partial_sum / factor[row_index, row_index]
    return jnp.stack(backward)


def pad_upper_z(field):
    return jnp.pad(field, ((0, 0), (0, 0), (0, 0), (0, 0), (0, 1)))


def gather_upper(field):
    from_x = from_behind(field[:, :, :1], "gx", -1)
    widened = jnp.concatenate([field, from_x], axis=2)
    from_y = from_behind(widened[:, :, :, :1], "gy", -1)
    return jnp.concatenate([widened, from_y], axis=3)


def return_lower(forces):
    size_x = forces.shape[2] - 1
    size_y = forces.shape[3] - 1
    to_y = from_behind(forces[:, :, :, size_y:], "gy", 1)
    kept = forces[:, :, :, :size_y]
    kept = jnp.concatenate([kept[:, :, :, :1] + to_y, kept[:, :, :, 1:]], axis=3)
    to_x = from_behind(kept[:, :, size_x:], "gx", 1)
    kept = kept[:, :, :size_x]
    return jnp.concatenate([kept[:, :, :1] + to_x, kept[:, :, 1:]], axis=2)


def corner_modes(node_field):
    found = {(): node_field}
    for dim in (2, 3, 4):
        grown = {}
        for key, cells in found.items():
            low = lax.slice_in_dim(cells, 0, cells.shape[dim] - 1, axis=dim)
            high = lax.slice_in_dim(cells, 1, cells.shape[dim], axis=dim)
            grown[key + (0,)] = high + low
            grown[key + (1,)] = high - low
        found = grown
    return [found[(mode // 4, mode // 2 % 2, mode % 2)] for mode in range(8)]


def mode_stiffness():
    step = np.array([[1.0, 1.0], [-1.0, 1.0]])
    change = np.kron(np.kron(np.kron(step, step), step), np.eye(3))
    return change @ hex_stiffness() @ change.T / 64.0


def mode_loads(modes, table):
    loads = []
    for mode in range(8):
        parts = []
        for comp in range(3):
            total = None
            for other in range(3):
                source = mode ^ (4 >> comp) ^ (4 >> other)
                weight = float(table[3 * mode + comp, 3 * source + other])
                if abs(weight) < 1e-12:
                    continue
                term = weight * modes[source][:, other]
                total = term if total is None else total + term
            parts.append(jnp.zeros_like(modes[mode][:, comp]) if total is None else total)
        loads.append(jnp.stack(parts, axis=1))
    return loads


def halo_both(cells, axis, dim, width):
    count = lax.axis_size(axis)
    head = lax.slice_in_dim(cells, 0, width, axis=dim)
    tail = lax.slice_in_dim(cells, cells.shape[dim] - width, cells.shape[dim], axis=dim)
    below = lax.ppermute(tail, axis, [(i, i + 1) for i in range(count - 1)])
    above = lax.ppermute(head, axis, [(i + 1, i) for i in range(count - 1)])
    return jnp.concatenate([below, cells, above], axis=dim)


def inside_mask(axis, extent, width, total):
    places = np.arange(extent + 2 * width) - width
    own = jnp.asarray(places, jnp.int32) + lax.axis_index(axis) * extent
    return ((own >= 0) & (own < total)).astype(jnp.float32)


def node_forces(node_field, modulus, stiffness):
    local_disp = cases_disp(node_field)
    local_load = jnp.einsum("ij,cjabd->ciabd", stiffness, local_disp, precision=highest)
    local_force = (local_load * modulus).reshape((node_field.shape[0], 8, 3) + modulus.shape)
    summed = jnp.zeros_like(node_field)
    for corner in range(8):
        off_x, off_y, off_z = (corner // 4, corner // 2 % 2, corner % 2)
        summed = summed + jnp.pad(
            local_force[:, corner],
            ((0, 0), (0, 0), (off_x, 1 - off_x), (off_y, 1 - off_y), (off_z, 1 - off_z)),
        )
    return summed[..., :-1], local_disp, local_load


def on_device(start_disp, bone_mask, density, load_nodes, load_forces):
    stiffness = jnp.asarray(hex_stiffness(), jnp.float32)
    modulus = bone_mask.astype(jnp.float32) * density * density
    case_count = start_disp.shape[0]
    size_x = start_disp.shape[2]
    size_y = start_disp.shape[3]
    size_z = start_disp.shape[4]
    count_x = lax.axis_size("gx")
    count_y = lax.axis_size("gy")
    fields = case_count * 3

    slot_ids = jnp.arange(size_x * size_y, dtype=jnp.int32)
    matches = load_nodes[0, 0][:, None, :, None] == slot_ids
    top_plane = jnp.sum(
        jnp.where(matches, load_forces[0, 0][:, :, :, None], 0.0), axis=2
    ).reshape(fields, size_x, size_y)
    packed_loads = jnp.pad(top_plane.transpose(1, 2, 0), ((0, 0), (0, 0), (0, size_z - fields)))
    parts = [start_disp.reshape(fields, size_x, size_y, size_z), modulus[None], packed_loads[None]]
    count = lax.axis_size("gx")
    head = jnp.concatenate([part[:, :2] for part in parts], axis=0)
    tail = jnp.concatenate([part[:, -2:] for part in parts], axis=0)
    below = lax.ppermute(tail, "gx", [(i, i + 1) for i in range(count - 1)])
    above = lax.ppermute(head, "gx", [(i + 1, i) for i in range(count - 1)])
    packed = jnp.concatenate(
        [below, jnp.concatenate(parts, axis=0), above], axis=1
    )
    packed = halo_both(packed, "gy", 2, 2)
    wide_start = packed[:fields].reshape(case_count, 3, size_x + 4, size_y + 4, size_z)
    wide_modulus = packed[fields]
    wide_loads = packed[fields + 1, 1:-1, 1:-1, :fields].transpose(2, 0, 1)
    wide_loads = wide_loads.reshape(case_count, 3, size_x + 2, size_y + 2)

    start_nodes = pad_upper_z(wide_start)
    forces, start_elems, start_loads = node_forces(
        start_nodes, wide_modulus[:-1, :-1], stiffness
    )
    applied = forces[:, :, 1:-1, 1:-1] + spring * wide_start[:, :, 1:-1, 1:-1]
    keep = (
        inside_mask("gx", size_x, 1, size_x * count_x)[:, None, None]
        * inside_mask("gy", size_y, 1, size_y * count_y)[None, :, None]
    )
    residual_wide = (
        jnp.concatenate(
            [-applied[..., :-1], (wide_loads - applied[..., -1])[..., None]], axis=4
        )
        * keep
    )

    residual_nodes = pad_upper_z(residual_wide)
    forces, residual_elems, residual_loads = node_forces(
        residual_nodes, wide_modulus[1:-2, 1:-2], stiffness
    )
    residual = residual_wide[:, :, 1:-1, 1:-1]
    applied = forces[:, :, 1:-1, 1:-1] + spring * residual

    blur_mass = modulus
    for dim, axis in ((0, "gx"), (1, "gy"), (2, None)):
        extent = modulus.shape[dim]
        count = 1 if axis is None else lax.axis_size(axis)
        places = lax.iota(jnp.int32, extent)
        if axis is not None:
            places = places + lax.axis_index(axis) * extent
        kept = jnp.zeros((extent,), jnp.float32)
        for tap_index, weight in enumerate(blur_weights()):
            shifted = places + 4 - tap_index
            kept = kept + jnp.where((shifted >= 0) & (shifted < extent * count), weight, 0.0)
        shape = [1, 1, 1]
        shape[dim] = extent
        blur_mass = blur_mass * kept.reshape(shape)
    start_elems = start_elems[:, :, 2:-1, 2:-1]
    start_loads = start_loads[:, :, 2:-1, 2:-1]
    residual_elems = residual_elems[:, :, 1:, 1:]
    residual_loads = residual_loads[:, :, 1:, 1:]
    start_energy = jnp.sum(start_elems * start_loads * blur_mass, axis=(1, 2, 3, 4))
    start_weighted = start_loads * blur_mass
    residual_weighted = residual_loads * blur_mass
    cross_energy = jnp.sum(
        residual_elems[:, None] * start_weighted[None, :], axis=(2, 3, 4, 5)
    )
    residual_energy = jnp.sum(
        residual_elems[:, None] * residual_weighted[None, :], axis=(2, 3, 4, 5)
    )
    grams = tree_sum(
        jnp.stack(
            [
                local_gram(residual, residual),
                local_gram(residual, applied),
                cross_energy,
                residual_energy,
                jnp.diag(start_energy),
            ]
        )
    )
    norm_now = grams[0]
    step_alpha = solve_spd(grams[1], norm_now)
    summed = (
        jnp.sum(grams[4])
        + 2.0 * jnp.sum(step_alpha * grams[2])
        + jnp.sum(step_alpha[:, None, :] * grams[3][:, :, None] * step_alpha[None, :, :])
    )
    solution = start_disp + mix_cases(residual, step_alpha)
    node_field = start_nodes[:, :, 2:-1, 2:-1] + mix_cases(
        residual_nodes[:, :, 1:, 1:], step_alpha
    )
    final_modes = corner_modes(node_field)
    final_loads = mode_loads(final_modes, mode_stiffness())
    energy = sum(
        jnp.sum(part * load, axis=(0, 1)) for part, load in zip(final_modes, final_loads)
    )
    stimulus = modulus * energy
    smooth = blur_valid(with_halo(stimulus, (("gx", 0),), 4), 0, size_x)
    smooth = blur_valid(with_halo(smooth, (("gy", 1),), 4), 1, size_y)
    smooth = blur_valid(jnp.pad(smooth, ((0, 0), (0, 0), (4, 4))), 2, size_z)
    mean_stim = summed / (size_x * size_y * size_z * count_x * count_y)
    new_density = jnp.minimum(density * (0.5 + 0.5 * smooth / (mean_stim + mean_eps)), density_cap)
    return (solution, new_density)


def solution(mesh):
    return jax.shard_map(
        on_device,
        mesh=mesh,
        in_specs=(
            P(None, None, "gx", "gy", None),
            P("gx", "gy", None),
            P("gx", "gy", None),
            P("gx", "gy", None, None),
            P("gx", "gy", None, None, None),
        ),
        out_specs=(P(None, None, "gx", "gy", None), P("gx", "gy", None)),
        check_vma=False,
    )
```

```python
import jax
import jax.numpy as jnp
import numpy as np
from jax import lax
from jax.sharding import PartitionSpec as P

spring = 0.1
poisson = 0.3
blur_sigma = 2.0
density_cap = 1.0
mean_eps = 1e-06
highest = lax.Precision.HIGHEST


def from_behind(block, axis, distance):
    devices = range(lax.axis_size(axis))
    route = [(i - distance, i) for i in devices if i - distance in devices]
    return lax.ppermute(block, axis, route)


def with_halo(cells, sides, width):
    for axis, dim in sides:
        count = lax.axis_size(axis)
        ends = count - 1
        head = lax.slice_in_dim(cells, 0, width, axis=dim)
        tail = lax.slice_in_dim(cells, cells.shape[dim] - width, cells.shape[dim], axis=dim)
        cells = jnp.concatenate(
            [
                lax.ppermute(tail, axis, [(i, (i + 1) % count) for i in range(ends)]),
                cells,
                lax.ppermute(head, axis, [((i + 1) % count, i) for i in range(ends)]),
            ],
            axis=dim,
        )
    return cells


def hex_stiffness():
    lame_first = poisson / ((1.0 + poisson) * (1.0 - 2.0 * poisson))
    shear_mod = 1.0 / (2.0 * (1.0 + poisson))
    elastic = np.zeros((6, 6))
    elastic[:3, :3] = lame_first
    for axis_id in range(3):
        elastic[axis_id, axis_id] = lame_first + 2.0 * shear_mod
        elastic[axis_id + 3, axis_id + 3] = shear_mod
    points = [0.5 - 0.5 / np.sqrt(3.0), 0.5 + 0.5 / np.sqrt(3.0)]
    stiffness = np.zeros((24, 24))
    for point_x in points:
        for point_y in points:
            for point_z in points:
                coords = (point_x, point_y, point_z)
                strain = np.zeros((6, 24))
                for corner in range(8):
                    offsets = (corner // 4, corner // 2 % 2, corner % 2)
                    shapes = [
                        coords[axis_id] if offsets[axis_id] == 1 else 1.0 - coords[axis_id]
                        for axis_id in range(3)
                    ]
                    slopes = [1.0 if offsets[axis_id] == 1 else -1.0 for axis_id in range(3)]
                    grad_x = slopes[0] * shapes[1] * shapes[2]
                    grad_y = shapes[0] * slopes[1] * shapes[2]
                    grad_z = shapes[0] * shapes[1] * slopes[2]
                    column = 3 * corner
                    strain[0, column] = grad_x
                    strain[1, column + 1] = grad_y
                    strain[2, column + 2] = grad_z
                    strain[3, column] = grad_y
                    strain[3, column + 1] = grad_x
                    strain[4, column + 1] = grad_z
                    strain[4, column + 2] = grad_y
                    strain[5, column] = grad_z
                    strain[5, column + 2] = grad_x
                stiffness += 0.125 * strain.T @ elastic @ strain
    return stiffness


def blur_weights():
    offsets = np.arange(9) - 4.0
    unscaled = np.exp(-offsets * offsets / (2.0 * blur_sigma * blur_sigma))
    return [float(entry) for entry in unscaled / unscaled.sum()]


def blur_valid(values, axis_id, extent):
    weights = blur_weights()
    summed = weights[0] * lax.slice_in_dim(values, 0, extent, axis=axis_id)
    for tap_index in range(1, 9):
        summed = summed + weights[tap_index] * lax.slice_in_dim(
            values, tap_index, tap_index + extent, axis=axis_id
        )
    return summed


def element_disp(node_field):
    size_x = node_field.shape[1] - 1
    size_y = node_field.shape[2] - 1
    size_z = node_field.shape[3] - 1
    corners = []
    for corner in range(8):
        off_x, off_y, off_z = (corner // 4, corner // 2 % 2, corner % 2)
        corners.append(
            node_field[:, off_x : off_x + size_x, off_y : off_y + size_y, off_z : off_z + size_z]
        )
    return jnp.stack(corners).reshape(24, size_x, size_y, size_z)


def cases_disp(node_field):
    size_x = node_field.shape[2] - 1
    size_y = node_field.shape[3] - 1
    size_z = node_field.shape[4] - 1
    corners = []
    for corner in range(8):
        off_x, off_y, off_z = (corner // 4, corner // 2 % 2, corner % 2)
        corners.append(
            node_field[:, :, off_x : off_x + size_x, off_y : off_y + size_y, off_z : off_z + size_z]
        )
    return jnp.stack(corners, axis=1).reshape(
        (node_field.shape[0], 24, size_x, size_y, size_z)
    )


def element_forces(node_field, modulus, stiffness):
    local_disp = cases_disp(node_field)
    local_force = jnp.einsum("ij,cjabd->ciabd", stiffness, local_disp, precision=highest) * modulus
    local_force = local_force.reshape((node_field.shape[0], 8, 3) + modulus.shape)
    summed = jnp.zeros_like(node_field)
    for corner in range(8):
        off_x, off_y, off_z = (corner // 4, corner // 2 % 2, corner % 2)
        summed = summed + jnp.pad(
            local_force[:, corner],
            ((0, 0), (0, 0), (off_x, 1 - off_x), (off_y, 1 - off_y), (off_z, 1 - off_z)),
        )
    return summed


def element_energy(node_field, stiffness):
    local_disp = cases_disp(node_field)
    local_force = jnp.einsum("ij,cjabd->ciabd", stiffness, local_disp, precision=highest)
    return jnp.sum(local_disp * local_force, axis=(0, 1))


def local_gram(left_field, right_field):
    return jnp.einsum("iabcd,jabcd->ij", left_field, right_field, precision=highest)


def tree_sum(value):
    for axis in ("gx", "gy"):
        count = lax.axis_size(axis)
        copies = jnp.broadcast_to(value[None], (count,) + value.shape)
        value = jnp.sum(lax.all_to_all(copies, axis, 0, 0, tiled=False), axis=0)
    return value


def mix_cases(field, coeffs):
    return jnp.einsum("kabcd,kj->jabcd", field, coeffs, precision=highest)


def solve_spd(matrix, rhs_matrix):
    factor = jnp.linalg.cholesky(matrix)
    forward = lax.linalg.triangular_solve(factor, rhs_matrix, left_side=True, lower=True)
    return lax.linalg.triangular_solve(
        factor, forward, left_side=True, lower=True, transpose_a=True
    )


def solve_spd_rows(matrix, rhs_matrix):
    factor = jnp.linalg.cholesky(matrix)
    matrix_order = matrix.shape[0]
    forward = []
    for row_index in range(matrix_order):
        partial_sum = rhs_matrix[row_index]
        for col_index in range(row_index):
            partial_sum = partial_sum - factor[row_index, col_index] * forward[col_index]
        forward.append(partial_sum / factor[row_index, row_index])
    backward = [None] * matrix_order
    for row_index in reversed(range(matrix_order)):
        partial_sum = forward[row_index]
        for col_index in range(row_index + 1, matrix_order):
            partial_sum = partial_sum - factor[col_index, row_index] * backward[col_index]
        backward[row_index] = partial_sum / factor[row_index, row_index]
    return jnp.stack(backward)


def pad_upper_z(field):
    return jnp.pad(field, ((0, 0), (0, 0), (0, 0), (0, 0), (0, 1)))


def gather_upper(field):
    from_x = from_behind(field[:, :, :1], "gx", -1)
    widened = jnp.concatenate([field, from_x], axis=2)
    from_y = from_behind(widened[:, :, :, :1], "gy", -1)
    return jnp.concatenate([widened, from_y], axis=3)


def return_lower(forces):
    size_x = forces.shape[2] - 1
    size_y = forces.shape[3] - 1
    to_y = from_behind(forces[:, :, :, size_y:], "gy", 1)
    kept = forces[:, :, :, :size_y]
    kept = jnp.concatenate([kept[:, :, :, :1] + to_y, kept[:, :, :, 1:]], axis=3)
    to_x = from_behind(kept[:, :, size_x:], "gx", 1)
    kept = kept[:, :, :size_x]
    return jnp.concatenate([kept[:, :, :1] + to_x, kept[:, :, 1:]], axis=2)


def corner_modes(node_field):
    found = {(): node_field}
    for dim in (2, 3, 4):
        grown = {}
        for key, cells in found.items():
            low = lax.slice_in_dim(cells, 0, cells.shape[dim] - 1, axis=dim)
            high = lax.slice_in_dim(cells, 1, cells.shape[dim], axis=dim)
            grown[key + (0,)] = high + low
            grown[key + (1,)] = high - low
        found = grown
    return [found[(mode // 4, mode // 2 % 2, mode % 2)] for mode in range(8)]


def mode_stiffness():
    step = np.array([[1.0, 1.0], [-1.0, 1.0]])
    change = np.kron(np.kron(np.kron(step, step), step), np.eye(3))
    return change @ hex_stiffness() @ change.T / 64.0


def mode_loads(modes, table):
    loads = []
    for mode in range(8):
        parts = []
        for comp in range(3):
            total = None
            for other in range(3):
                source = mode ^ (4 >> comp) ^ (4 >> other)
                weight = float(table[3 * mode + comp, 3 * source + other])
                if abs(weight) < 1e-12:
                    continue
                term = weight * modes[source][:, other]
                total = term if total is None else total + term
            parts.append(jnp.zeros_like(modes[mode][:, comp]) if total is None else total)
        loads.append(jnp.stack(parts, axis=1))
    return loads


def halo_both(cells, axis, dim, width):
    count = lax.axis_size(axis)
    head = lax.slice_in_dim(cells, 0, width, axis=dim)
    tail = lax.slice_in_dim(cells, cells.shape[dim] - width, cells.shape[dim], axis=dim)
    below = lax.ppermute(tail, axis, [(i, i + 1) for i in range(count - 1)])
    above = lax.ppermute(head, axis, [(i + 1, i) for i in range(count - 1)])
    return jnp.concatenate([below, cells, above], axis=dim)


def inside_mask(axis, extent, width, total):
    places = np.arange(extent + 2 * width) - width
    own = jnp.asarray(places, jnp.int32) + lax.axis_index(axis) * extent
    return ((own >= 0) & (own < total)).astype(jnp.float32)


def node_forces(node_field, modulus, stiffness):
    local_disp = cases_disp(node_field)
    cases = node_field.shape[0]
    blocks = jnp.asarray(np.kron(np.eye(cases), hex_stiffness()), jnp.float32)
    local_load = jnp.einsum(
        "ij,jabd->iabd", blocks, local_disp.reshape((cases * 24,) + modulus.shape),
        precision=highest,
    ).reshape(local_disp.shape)
    local_force = (local_load * modulus).reshape((node_field.shape[0], 8, 3) + modulus.shape)
    summed = jnp.zeros_like(node_field)
    for corner in range(8):
        off_x, off_y, off_z = (corner // 4, corner // 2 % 2, corner % 2)
        summed = summed + jnp.pad(
            local_force[:, corner],
            ((0, 0), (0, 0), (off_x, 1 - off_x), (off_y, 1 - off_y), (off_z, 1 - off_z)),
        )
    return summed[..., :-1], local_disp, local_load


def on_device(start_disp, bone_mask, density, load_nodes, load_forces):
    stiffness = jnp.asarray(hex_stiffness(), jnp.float32)
    modulus = bone_mask.astype(jnp.float32) * density * density
    case_count = start_disp.shape[0]
    size_x = start_disp.shape[2]
    size_y = start_disp.shape[3]
    size_z = start_disp.shape[4]
    count_x = lax.axis_size("gx")
    count_y = lax.axis_size("gy")
    fields = case_count * 3

    slot_ids = jnp.arange(size_x * size_y, dtype=jnp.int32)
    matches = (load_nodes[0, 0][:, :, None] == slot_ids).astype(jnp.float32)
    top_plane = jnp.einsum("cls,ckl->cks", matches, load_forces[0, 0], precision=highest).reshape(
        fields, size_x, size_y
    )
    packed_loads = jnp.pad(top_plane.transpose(1, 2, 0), ((0, 0), (0, 0), (0, size_z - fields)))
    packed = jnp.concatenate(
        [start_disp.reshape(fields, size_x, size_y, size_z), modulus[None], packed_loads[None]],
        axis=0,
    )
    packed = halo_both(halo_both(packed, "gx", 1, 2), "gy", 2, 2)
    wide_start = packed[:fields].reshape(case_count, 3, size_x + 4, size_y + 4, size_z)
    wide_modulus = packed[fields]
    wide_loads = packed[fields + 1, 1:-1, 1:-1, :fields].transpose(2, 0, 1)
    wide_loads = wide_loads.reshape(case_count, 3, size_x + 2, size_y + 2)

    start_nodes = pad_upper_z(wide_start)
    forces, start_elems, start_loads = node_forces(
        start_nodes, wide_modulus[:-1, :-1], stiffness
    )
    applied = forces[:, :, 1:-1, 1:-1] + spring * wide_start[:, :, 1:-1, 1:-1]
    keep = (
        inside_mask("gx", size_x, 1, size_x * count_x)[:, None, None]
        * inside_mask("gy", size_y, 1, size_y * count_y)[None, :, None]
    )
    residual_wide = (
        jnp.concatenate(
            [-applied[..., :-1], (wide_loads - applied[..., -1])[..., None]], axis=4
        )
        * keep
    )

    residual_nodes = pad_upper_z(residual_wide)
    forces, residual_elems, residual_loads = node_forces(
        residual_nodes, wide_modulus[1:-2, 1:-2], stiffness
    )
    residual = residual_wide[:, :, 1:-1, 1:-1]
    applied = forces[:, :, 1:-1, 1:-1] + spring * residual

    blur_mass = modulus
    for dim, axis in ((0, "gx"), (1, "gy"), (2, None)):
        extent = modulus.shape[dim]
        count = 1 if axis is None else lax.axis_size(axis)
        places = lax.iota(jnp.int32, extent)
        if axis is not None:
            places = places + lax.axis_index(axis) * extent
        kept = jnp.zeros((extent,), jnp.float32)
        for tap_index, weight in enumerate(blur_weights()):
            shifted = places + 4 - tap_index
            kept = kept + jnp.where((shifted >= 0) & (shifted < extent * count), weight, 0.0)
        shape = [1, 1, 1]
        shape[dim] = extent
        blur_mass = blur_mass * kept.reshape(shape)
    start_elems = start_elems[:, :, 2:-1, 2:-1]
    start_loads = start_loads[:, :, 2:-1, 2:-1]
    residual_elems = residual_elems[:, :, 1:, 1:]
    residual_loads = residual_loads[:, :, 1:, 1:]
    start_energy = jnp.sum(start_elems * start_loads * blur_mass, axis=(1, 2, 3, 4))
    start_weighted = start_loads * blur_mass
    residual_weighted = residual_loads * blur_mass
    cross_energy = jnp.sum(
        residual_elems[:, None] * start_weighted[None, :], axis=(2, 3, 4, 5)
    )
    residual_energy = jnp.sum(
        residual_elems[:, None] * residual_weighted[None, :], axis=(2, 3, 4, 5)
    )
    grams = tree_sum(
        jnp.stack(
            [
                local_gram(residual, residual),
                local_gram(residual, applied),
                cross_energy,
                residual_energy,
                jnp.diag(start_energy),
            ]
        )
    )
    norm_now = grams[0]
    step_alpha = solve_spd(grams[1], norm_now)
    summed = (
        jnp.sum(grams[4])
        + 2.0 * jnp.sum(step_alpha * grams[2])
        + jnp.sum(step_alpha[:, None, :] * grams[3][:, :, None] * step_alpha[None, :, :])
    )
    solution = start_disp + mix_cases(residual, step_alpha)
    node_field = start_nodes[:, :, 2:-1, 2:-1] + mix_cases(
        residual_nodes[:, :, 1:, 1:], step_alpha
    )
    final_modes = corner_modes(node_field)
    final_loads = mode_loads(final_modes, mode_stiffness())
    energy = sum(
        jnp.sum(part * load, axis=(0, 1)) for part, load in zip(final_modes, final_loads)
    )
    stimulus = modulus * energy
    smooth = blur_valid(with_halo(stimulus, (("gx", 0),), 4), 0, size_x)
    smooth = blur_valid(with_halo(smooth, (("gy", 1),), 4), 1, size_y)
    smooth = blur_valid(jnp.pad(smooth, ((0, 0), (0, 0), (4, 4))), 2, size_z)
    mean_stim = summed / (size_x * size_y * size_z * count_x * count_y)
    new_density = jnp.minimum(density * (0.5 + 0.5 * smooth / (mean_stim + mean_eps)), density_cap)
    return (solution, new_density)


def solution(mesh):
    return jax.shard_map(
        on_device,
        mesh=mesh,
        in_specs=(
            P(None, None, "gx", "gy", None),
            P("gx", "gy", None),
            P("gx", "gy", None),
            P("gx", "gy", None, None),
            P("gx", "gy", None, None, None),
        ),
        out_specs=(P(None, None, "gx", "gy", None), P("gx", "gy", None)),
        check_vma=False,
    )
```

```python
import jax
import jax.numpy as jnp
import numpy as np
from jax import lax
from jax.sharding import PartitionSpec as P

spring = 0.1
poisson = 0.3
blur_sigma = 2.0
density_cap = 1.0
mean_eps = 1e-06
highest = lax.Precision.HIGHEST


def from_behind(block, axis, distance):
    devices = range(lax.axis_size(axis))
    route = [(i - distance, i) for i in devices if i - distance in devices]
    return lax.ppermute(block, axis, route)


def with_halo(cells, sides, width):
    for axis, dim in sides:
        count = lax.axis_size(axis)
        ends = count - 1
        head = lax.slice_in_dim(cells, 0, width, axis=dim)
        tail = lax.slice_in_dim(cells, cells.shape[dim] - width, cells.shape[dim], axis=dim)
        cells = jnp.concatenate(
            [
                lax.ppermute(tail, axis, [(i, (i + 1) % count) for i in range(ends)]),
                cells,
                lax.ppermute(head, axis, [((i + 1) % count, i) for i in range(ends)]),
            ],
            axis=dim,
        )
    return cells


def hex_stiffness():
    lame_first = poisson / ((1.0 + poisson) * (1.0 - 2.0 * poisson))
    shear_mod = 1.0 / (2.0 * (1.0 + poisson))
    elastic = np.zeros((6, 6))
    elastic[:3, :3] = lame_first
    for axis_id in range(3):
        elastic[axis_id, axis_id] = lame_first + 2.0 * shear_mod
        elastic[axis_id + 3, axis_id + 3] = shear_mod
    points = [0.5 - 0.5 / np.sqrt(3.0), 0.5 + 0.5 / np.sqrt(3.0)]
    stiffness = np.zeros((24, 24))
    for point_x in points:
        for point_y in points:
            for point_z in points:
                coords = (point_x, point_y, point_z)
                strain = np.zeros((6, 24))
                for corner in range(8):
                    offsets = (corner // 4, corner // 2 % 2, corner % 2)
                    shapes = [
                        coords[axis_id] if offsets[axis_id] == 1 else 1.0 - coords[axis_id]
                        for axis_id in range(3)
                    ]
                    slopes = [1.0 if offsets[axis_id] == 1 else -1.0 for axis_id in range(3)]
                    grad_x = slopes[0] * shapes[1] * shapes[2]
                    grad_y = shapes[0] * slopes[1] * shapes[2]
                    grad_z = shapes[0] * shapes[1] * slopes[2]
                    column = 3 * corner
                    strain[0, column] = grad_x
                    strain[1, column + 1] = grad_y
                    strain[2, column + 2] = grad_z
                    strain[3, column] = grad_y
                    strain[3, column + 1] = grad_x
                    strain[4, column + 1] = grad_z
                    strain[4, column + 2] = grad_y
                    strain[5, column] = grad_z
                    strain[5, column + 2] = grad_x
                stiffness += 0.125 * strain.T @ elastic @ strain
    return stiffness


def blur_weights():
    offsets = np.arange(9) - 4.0
    unscaled = np.exp(-offsets * offsets / (2.0 * blur_sigma * blur_sigma))
    return [float(entry) for entry in unscaled / unscaled.sum()]


def blur_valid(values, axis_id, extent):
    weights = blur_weights()
    summed = weights[0] * lax.slice_in_dim(values, 0, extent, axis=axis_id)
    for tap_index in range(1, 9):
        summed = summed + weights[tap_index] * lax.slice_in_dim(
            values, tap_index, tap_index + extent, axis=axis_id
        )
    return summed


def element_disp(node_field):
    size_x = node_field.shape[1] - 1
    size_y = node_field.shape[2] - 1
    size_z = node_field.shape[3] - 1
    corners = []
    for corner in range(8):
        off_x, off_y, off_z = (corner // 4, corner // 2 % 2, corner % 2)
        corners.append(
            node_field[:, off_x : off_x + size_x, off_y : off_y + size_y, off_z : off_z + size_z]
        )
    return jnp.stack(corners).reshape(24, size_x, size_y, size_z)


def cases_disp(node_field):
    size_x = node_field.shape[2] - 1
    size_y = node_field.shape[3] - 1
    size_z = node_field.shape[4] - 1
    corners = []
    for corner in range(8):
        off_x, off_y, off_z = (corner // 4, corner // 2 % 2, corner % 2)
        corners.append(
            node_field[:, :, off_x : off_x + size_x, off_y : off_y + size_y, off_z : off_z + size_z]
        )
    return jnp.stack(corners, axis=1).reshape(
        (node_field.shape[0], 24, size_x, size_y, size_z)
    )


def element_forces(node_field, modulus, stiffness):
    local_disp = cases_disp(node_field)
    local_force = jnp.einsum("ij,cjabd->ciabd", stiffness, local_disp, precision=highest) * modulus
    local_force = local_force.reshape((node_field.shape[0], 8, 3) + modulus.shape)
    summed = jnp.zeros_like(node_field)
    for corner in range(8):
        off_x, off_y, off_z = (corner // 4, corner // 2 % 2, corner % 2)
        summed = summed + jnp.pad(
            local_force[:, corner],
            ((0, 0), (0, 0), (off_x, 1 - off_x), (off_y, 1 - off_y), (off_z, 1 - off_z)),
        )
    return summed


def element_energy(node_field, stiffness):
    local_disp = cases_disp(node_field)
    local_force = jnp.einsum("ij,cjabd->ciabd", stiffness, local_disp, precision=highest)
    return jnp.sum(local_disp * local_force, axis=(0, 1))


def local_gram(left_field, right_field):
    return jnp.einsum("iabcd,jabcd->ij", left_field, right_field, precision=highest)


def tree_sum(value):
    for axis in ("gx", "gy"):
        count = lax.axis_size(axis)
        copies = jnp.broadcast_to(value[None], (count,) + value.shape)
        value = jnp.sum(lax.all_to_all(copies, axis, 0, 0, tiled=False), axis=0)
    return value


def mix_cases(field, coeffs):
    return jnp.einsum("kabcd,kj->jabcd", field, coeffs, precision=highest)


def solve_spd(matrix, rhs_matrix):
    factor = jnp.linalg.cholesky(matrix)
    forward = lax.linalg.triangular_solve(factor, rhs_matrix, left_side=True, lower=True)
    return lax.linalg.triangular_solve(
        factor, forward, left_side=True, lower=True, transpose_a=True
    )


def solve_spd_rows(matrix, rhs_matrix):
    factor = jnp.linalg.cholesky(matrix)
    matrix_order = matrix.shape[0]
    forward = []
    for row_index in range(matrix_order):
        partial_sum = rhs_matrix[row_index]
        for col_index in range(row_index):
            partial_sum = partial_sum - factor[row_index, col_index] * forward[col_index]
        forward.append(partial_sum / factor[row_index, row_index])
    backward = [None] * matrix_order
    for row_index in reversed(range(matrix_order)):
        partial_sum = forward[row_index]
        for col_index in range(row_index + 1, matrix_order):
            partial_sum = partial_sum - factor[col_index, row_index] * backward[col_index]
        backward[row_index] = partial_sum / factor[row_index, row_index]
    return jnp.stack(backward)


def pad_upper_z(field):
    return jnp.pad(field, ((0, 0), (0, 0), (0, 0), (0, 0), (0, 1)))


def gather_upper(field):
    from_x = from_behind(field[:, :, :1], "gx", -1)
    widened = jnp.concatenate([field, from_x], axis=2)
    from_y = from_behind(widened[:, :, :, :1], "gy", -1)
    return jnp.concatenate([widened, from_y], axis=3)


def return_lower(forces):
    size_x = forces.shape[2] - 1
    size_y = forces.shape[3] - 1
    to_y = from_behind(forces[:, :, :, size_y:], "gy", 1)
    kept = forces[:, :, :, :size_y]
    kept = jnp.concatenate([kept[:, :, :, :1] + to_y, kept[:, :, :, 1:]], axis=3)
    to_x = from_behind(kept[:, :, size_x:], "gx", 1)
    kept = kept[:, :, :size_x]
    return jnp.concatenate([kept[:, :, :1] + to_x, kept[:, :, 1:]], axis=2)


def corner_modes(node_field):
    found = {(): node_field}
    for dim in (2, 3, 4):
        grown = {}
        for key, cells in found.items():
            low = lax.slice_in_dim(cells, 0, cells.shape[dim] - 1, axis=dim)
            high = lax.slice_in_dim(cells, 1, cells.shape[dim], axis=dim)
            grown[key + (0,)] = high + low
            grown[key + (1,)] = high - low
        found = grown
    return [found[(mode // 4, mode // 2 % 2, mode % 2)] for mode in range(8)]


def mode_stiffness():
    step = np.array([[1.0, 1.0], [-1.0, 1.0]])
    change = np.kron(np.kron(np.kron(step, step), step), np.eye(3))
    return change @ hex_stiffness() @ change.T / 64.0


def mode_loads(modes, table):
    loads = []
    for mode in range(8):
        parts = []
        for comp in range(3):
            total = None
            for other in range(3):
                source = mode ^ (4 >> comp) ^ (4 >> other)
                weight = float(table[3 * mode + comp, 3 * source + other])
                if abs(weight) < 1e-12:
                    continue
                term = weight * modes[source][:, other]
                total = term if total is None else total + term
            parts.append(jnp.zeros_like(modes[mode][:, comp]) if total is None else total)
        loads.append(jnp.stack(parts, axis=1))
    return loads


def halo_both(cells, axis, dim, width):
    count = lax.axis_size(axis)
    head = lax.slice_in_dim(cells, 0, width, axis=dim)
    tail = lax.slice_in_dim(cells, cells.shape[dim] - width, cells.shape[dim], axis=dim)
    below = lax.ppermute(tail, axis, [(i, i + 1) for i in range(count - 1)])
    above = lax.ppermute(head, axis, [(i + 1, i) for i in range(count - 1)])
    return jnp.concatenate([below, cells, above], axis=dim)


def inside_mask(axis, extent, width, total):
    places = np.arange(extent + 2 * width) - width
    own = jnp.asarray(places, jnp.int32) + lax.axis_index(axis) * extent
    return ((own >= 0) & (own < total)).astype(jnp.float32)


def node_forces(node_field, modulus, stiffness):
    local_disp = cases_disp(node_field)
    local_load = jnp.einsum("ij,cjabd->ciabd", stiffness, local_disp, precision=highest)
    local_force = (local_load * modulus).reshape((node_field.shape[0], 8, 3) + modulus.shape)
    summed = jnp.zeros_like(node_field)
    for corner in range(8):
        off_x, off_y, off_z = (corner // 4, corner // 2 % 2, corner % 2)
        summed = summed + jnp.pad(
            local_force[:, corner],
            ((0, 0), (0, 0), (off_x, 1 - off_x), (off_y, 1 - off_y), (off_z, 1 - off_z)),
        )
    return summed[..., :-1], local_disp, local_load


def on_device(start_disp, bone_mask, density, load_nodes, load_forces):
    stiffness = jnp.asarray(hex_stiffness(), jnp.float32)
    modulus = bone_mask.astype(jnp.float32) * density * density
    case_count = start_disp.shape[0]
    size_x = start_disp.shape[2]
    size_y = start_disp.shape[3]
    size_z = start_disp.shape[4]
    count_x = lax.axis_size("gx")
    count_y = lax.axis_size("gy")
    fields = case_count * 3

    slot_ids = jnp.arange(size_x * size_y, dtype=jnp.int32)
    matches = (load_nodes[0, 0][:, :, None] == slot_ids).astype(jnp.float32)
    top_plane = jnp.einsum("cls,ckl->cks", matches, load_forces[0, 0], precision=highest).reshape(
        fields, size_x, size_y
    )
    packed_loads = jnp.pad(top_plane.transpose(1, 2, 0), ((0, 0), (0, 0), (0, size_z - fields)))
    packed = jnp.concatenate(
        [start_disp.reshape(fields, size_x, size_y, size_z), modulus[None], packed_loads[None]],
        axis=0,
    )
    packed = halo_both(halo_both(packed, "gx", 1, 2), "gy", 2, 2)
    wide_start = packed[:fields].reshape(case_count, 3, size_x + 4, size_y + 4, size_z)
    wide_modulus = packed[fields]
    wide_loads = packed[fields + 1, 1:-1, 1:-1, :fields].transpose(2, 0, 1)
    wide_loads = wide_loads.reshape(case_count, 3, size_x + 2, size_y + 2)

    start_nodes = pad_upper_z(wide_start)
    forces, start_elems, start_loads = node_forces(
        start_nodes, wide_modulus[:-1, :-1], stiffness
    )
    applied = forces[:, :, 1:-1, 1:-1] + spring * wide_start[:, :, 1:-1, 1:-1]
    keep = (
        inside_mask("gx", size_x, 1, size_x * count_x)[:, None, None]
        * inside_mask("gy", size_y, 1, size_y * count_y)[None, :, None]
    )
    residual_wide = (
        jnp.concatenate(
            [-applied[..., :-1], (wide_loads - applied[..., -1])[..., None]], axis=4
        )
        * keep
    )

    residual_nodes = pad_upper_z(residual_wide)
    forces, residual_elems, residual_loads = node_forces(
        residual_nodes, wide_modulus[1:-2, 1:-2], stiffness
    )
    residual = residual_wide[:, :, 1:-1, 1:-1]
    applied = forces[:, :, 1:-1, 1:-1] + spring * residual

    blur_mass = modulus
    for dim, axis in ((0, "gx"), (1, "gy"), (2, None)):
        extent = modulus.shape[dim]
        count = 1 if axis is None else lax.axis_size(axis)
        places = lax.iota(jnp.int32, extent)
        if axis is not None:
            places = places + lax.axis_index(axis) * extent
        kept = jnp.zeros((extent,), jnp.float32)
        for tap_index, weight in enumerate(blur_weights()):
            shifted = places + 4 - tap_index
            kept = kept + jnp.where((shifted >= 0) & (shifted < extent * count), weight, 0.0)
        shape = [1, 1, 1]
        shape[dim] = extent
        blur_mass = blur_mass * kept.reshape(shape)
    start_elems = start_elems[:, :, 2:-1, 2:-1]
    start_loads = start_loads[:, :, 2:-1, 2:-1]
    residual_elems = residual_elems[:, :, 1:, 1:]
    residual_loads = residual_loads[:, :, 1:, 1:]
    start_energy = jnp.sum(start_elems * start_loads * blur_mass, axis=(1, 2, 3, 4))
    residual_scaled = residual_elems * blur_mass
    cross_energy = jnp.sum(
        residual_scaled[:, None] * start_loads[None, :], axis=(2, 3, 4, 5)
    )
    residual_energy = jnp.sum(
        residual_scaled[:, None] * residual_loads[None, :], axis=(2, 3, 4, 5)
    )
    grams = tree_sum(
        jnp.stack(
            [
                local_gram(residual, residual),
                local_gram(residual, applied),
                cross_energy,
                residual_energy,
                jnp.diag(start_energy),
            ]
        )
    )
    norm_now = grams[0]
    step_alpha = solve_spd(grams[1], norm_now)
    summed = (
        jnp.sum(grams[4])
        + 2.0 * jnp.sum(step_alpha * grams[2])
        + jnp.sum(step_alpha[:, None, :] * grams[3][:, :, None] * step_alpha[None, :, :])
    )
    solution = start_disp + mix_cases(residual, step_alpha)
    node_field = start_nodes[:, :, 2:-1, 2:-1] + mix_cases(
        residual_nodes[:, :, 1:, 1:], step_alpha
    )
    final_modes = corner_modes(node_field)
    final_loads = mode_loads(final_modes, mode_stiffness())
    energy = sum(
        jnp.sum(part * load, axis=(0, 1)) for part, load in zip(final_modes, final_loads)
    )
    stimulus = modulus * energy
    smooth = blur_valid(with_halo(stimulus, (("gx", 0),), 4), 0, size_x)
    smooth = blur_valid(with_halo(smooth, (("gy", 1),), 4), 1, size_y)
    smooth = blur_valid(jnp.pad(smooth, ((0, 0), (0, 0), (4, 4))), 2, size_z)
    mean_stim = summed / (size_x * size_y * size_z * count_x * count_y)
    new_density = jnp.minimum(density * (0.5 + 0.5 * smooth / (mean_stim + mean_eps)), density_cap)
    return (solution, new_density)


def solution(mesh):
    return jax.shard_map(
        on_device,
        mesh=mesh,
        in_specs=(
            P(None, None, "gx", "gy", None),
            P("gx", "gy", None),
            P("gx", "gy", None),
            P("gx", "gy", None, None),
            P("gx", "gy", None, None, None),
        ),
        out_specs=(P(None, None, "gx", "gy", None), P("gx", "gy", None)),
        check_vma=False,
    )
```

```python
import jax
import jax.numpy as jnp
import numpy as np
from jax import lax
from jax.sharding import PartitionSpec as P

spring = 0.1
poisson = 0.3
blur_sigma = 2.0
density_cap = 1.0
mean_eps = 1e-06
highest = lax.Precision.HIGHEST


def from_behind(block, axis, distance):
    devices = range(lax.axis_size(axis))
    route = [(i - distance, i) for i in devices if i - distance in devices]
    return lax.ppermute(block, axis, route)


def with_halo(cells, sides, width):
    for axis, dim in sides:
        count = lax.axis_size(axis)
        ends = count - 1
        head = lax.slice_in_dim(cells, 0, width, axis=dim)
        tail = lax.slice_in_dim(cells, cells.shape[dim] - width, cells.shape[dim], axis=dim)
        cells = jnp.concatenate(
            [
                lax.ppermute(tail, axis, [(i, (i + 1) % count) for i in range(ends)]),
                cells,
                lax.ppermute(head, axis, [((i + 1) % count, i) for i in range(ends)]),
            ],
            axis=dim,
        )
    return cells


def hex_stiffness():
    lame_first = poisson / ((1.0 + poisson) * (1.0 - 2.0 * poisson))
    shear_mod = 1.0 / (2.0 * (1.0 + poisson))
    elastic = np.zeros((6, 6))
    elastic[:3, :3] = lame_first
    for axis_id in range(3):
        elastic[axis_id, axis_id] = lame_first + 2.0 * shear_mod
        elastic[axis_id + 3, axis_id + 3] = shear_mod
    points = [0.5 - 0.5 / np.sqrt(3.0), 0.5 + 0.5 / np.sqrt(3.0)]
    stiffness = np.zeros((24, 24))
    for point_x in points:
        for point_y in points:
            for point_z in points:
                coords = (point_x, point_y, point_z)
                strain = np.zeros((6, 24))
                for corner in range(8):
                    offsets = (corner // 4, corner // 2 % 2, corner % 2)
                    shapes = [
                        coords[axis_id] if offsets[axis_id] == 1 else 1.0 - coords[axis_id]
                        for axis_id in range(3)
                    ]
                    slopes = [1.0 if offsets[axis_id] == 1 else -1.0 for axis_id in range(3)]
                    grad_x = slopes[0] * shapes[1] * shapes[2]
                    grad_y = shapes[0] * slopes[1] * shapes[2]
                    grad_z = shapes[0] * shapes[1] * slopes[2]
                    column = 3 * corner
                    strain[0, column] = grad_x
                    strain[1, column + 1] = grad_y
                    strain[2, column + 2] = grad_z
                    strain[3, column] = grad_y
                    strain[3, column + 1] = grad_x
                    strain[4, column + 1] = grad_z
                    strain[4, column + 2] = grad_y
                    strain[5, column] = grad_z
                    strain[5, column + 2] = grad_x
                stiffness += 0.125 * strain.T @ elastic @ strain
    return stiffness


def blur_weights():
    offsets = np.arange(9) - 4.0
    unscaled = np.exp(-offsets * offsets / (2.0 * blur_sigma * blur_sigma))
    return [float(entry) for entry in unscaled / unscaled.sum()]


def blur_valid(values, axis_id, extent):
    weights = blur_weights()
    summed = weights[0] * lax.slice_in_dim(values, 0, extent, axis=axis_id)
    for tap_index in range(1, 9):
        summed = summed + weights[tap_index] * lax.slice_in_dim(
            values, tap_index, tap_index + extent, axis=axis_id
        )
    return summed


def element_disp(node_field):
    size_x = node_field.shape[1] - 1
    size_y = node_field.shape[2] - 1
    size_z = node_field.shape[3] - 1
    corners = []
    for corner in range(8):
        off_x, off_y, off_z = (corner // 4, corner // 2 % 2, corner % 2)
        corners.append(
            node_field[:, off_x : off_x + size_x, off_y : off_y + size_y, off_z : off_z + size_z]
        )
    return jnp.stack(corners).reshape(24, size_x, size_y, size_z)


def cases_disp(node_field):
    size_x = node_field.shape[2] - 1
    size_y = node_field.shape[3] - 1
    size_z = node_field.shape[4] - 1
    corners = []
    for corner in range(8):
        off_x, off_y, off_z = (corner // 4, corner // 2 % 2, corner % 2)
        corners.append(
            node_field[:, :, off_x : off_x + size_x, off_y : off_y + size_y, off_z : off_z + size_z]
        )
    return jnp.stack(corners, axis=1).reshape(
        (node_field.shape[0], 24, size_x, size_y, size_z)
    )


def element_forces(node_field, modulus, stiffness):
    local_disp = cases_disp(node_field)
    local_force = jnp.einsum("ij,cjabd->ciabd", stiffness, local_disp, precision=highest) * modulus
    local_force = local_force.reshape((node_field.shape[0], 8, 3) + modulus.shape)
    summed = jnp.zeros_like(node_field)
    for corner in range(8):
        off_x, off_y, off_z = (corner // 4, corner // 2 % 2, corner % 2)
        summed = summed + jnp.pad(
            local_force[:, corner],
            ((0, 0), (0, 0), (off_x, 1 - off_x), (off_y, 1 - off_y), (off_z, 1 - off_z)),
        )
    return summed


def element_energy(node_field, stiffness):
    local_disp = cases_disp(node_field)
    local_force = jnp.einsum("ij,cjabd->ciabd", stiffness, local_disp, precision=highest)
    return jnp.sum(local_disp * local_force, axis=(0, 1))


def local_gram(left_field, right_field):
    return jnp.einsum("iabcd,jabcd->ij", left_field, right_field, precision=highest)


def tree_sum(value):
    for axis in ("gx", "gy"):
        count = lax.axis_size(axis)
        copies = jnp.broadcast_to(value[None], (count,) + value.shape)
        value = jnp.sum(lax.all_to_all(copies, axis, 0, 0, tiled=False), axis=0)
    return value


def mix_cases(field, coeffs):
    return jnp.einsum("kabcd,kj->jabcd", field, coeffs, precision=highest)


def solve_spd(matrix, rhs_matrix):
    factor = jnp.linalg.cholesky(matrix)
    forward = lax.linalg.triangular_solve(factor, rhs_matrix, left_side=True, lower=True)
    return lax.linalg.triangular_solve(
        factor, forward, left_side=True, lower=True, transpose_a=True
    )


def solve_spd_rows(matrix, rhs_matrix):
    factor = jnp.linalg.cholesky(matrix)
    matrix_order = matrix.shape[0]
    forward = []
    for row_index in range(matrix_order):
        partial_sum = rhs_matrix[row_index]
        for col_index in range(row_index):
            partial_sum = partial_sum - factor[row_index, col_index] * forward[col_index]
        forward.append(partial_sum / factor[row_index, row_index])
    backward = [None] * matrix_order
    for row_index in reversed(range(matrix_order)):
        partial_sum = forward[row_index]
        for col_index in range(row_index + 1, matrix_order):
            partial_sum = partial_sum - factor[col_index, row_index] * backward[col_index]
        backward[row_index] = partial_sum / factor[row_index, row_index]
    return jnp.stack(backward)


def pad_upper_z(field):
    return jnp.pad(field, ((0, 0), (0, 0), (0, 0), (0, 0), (0, 1)))


def gather_upper(field):
    from_x = from_behind(field[:, :, :1], "gx", -1)
    widened = jnp.concatenate([field, from_x], axis=2)
    from_y = from_behind(widened[:, :, :, :1], "gy", -1)
    return jnp.concatenate([widened, from_y], axis=3)


def return_lower(forces):
    size_x = forces.shape[2] - 1
    size_y = forces.shape[3] - 1
    to_y = from_behind(forces[:, :, :, size_y:], "gy", 1)
    kept = forces[:, :, :, :size_y]
    kept = jnp.concatenate([kept[:, :, :, :1] + to_y, kept[:, :, :, 1:]], axis=3)
    to_x = from_behind(kept[:, :, size_x:], "gx", 1)
    kept = kept[:, :, :size_x]
    return jnp.concatenate([kept[:, :, :1] + to_x, kept[:, :, 1:]], axis=2)


def corner_modes(node_field):
    found = {(): node_field}
    for dim in (2, 3, 4):
        grown = {}
        for key, cells in found.items():
            low = lax.slice_in_dim(cells, 0, cells.shape[dim] - 1, axis=dim)
            high = lax.slice_in_dim(cells, 1, cells.shape[dim], axis=dim)
            grown[key + (0,)] = high + low
            grown[key + (1,)] = high - low
        found = grown
    return [found[(mode // 4, mode // 2 % 2, mode % 2)] for mode in range(8)]


def mode_stiffness():
    step = np.array([[1.0, 1.0], [-1.0, 1.0]])
    change = np.kron(np.kron(np.kron(step, step), step), np.eye(3))
    return change @ hex_stiffness() @ change.T / 64.0


def mode_loads(modes, table):
    loads = []
    for mode in range(8):
        parts = []
        for comp in range(3):
            total = None
            for other in range(3):
                source = mode ^ (4 >> comp) ^ (4 >> other)
                weight = float(table[3 * mode + comp, 3 * source + other])
                if abs(weight) < 1e-12:
                    continue
                term = weight * modes[source][:, other]
                total = term if total is None else total + term
            parts.append(jnp.zeros_like(modes[mode][:, comp]) if total is None else total)
        loads.append(jnp.stack(parts, axis=1))
    return loads


def halo_both(cells, axis, dim, width):
    count = lax.axis_size(axis)
    head = lax.slice_in_dim(cells, 0, width, axis=dim)
    tail = lax.slice_in_dim(cells, cells.shape[dim] - width, cells.shape[dim], axis=dim)
    below = lax.ppermute(tail, axis, [(i, i + 1) for i in range(count - 1)])
    above = lax.ppermute(head, axis, [(i + 1, i) for i in range(count - 1)])
    return jnp.concatenate([below, cells, above], axis=dim)


def inside_mask(axis, extent, width, total):
    places = np.arange(extent + 2 * width) - width
    own = jnp.asarray(places, jnp.int32) + lax.axis_index(axis) * extent
    return ((own >= 0) & (own < total)).astype(jnp.float32)


def node_forces(node_field, modulus, stiffness):
    local_disp = cases_disp(node_field)
    local_load = jnp.einsum("ij,cjabd->ciabd", stiffness, local_disp, precision=highest)
    local_force = (local_load * modulus).reshape((node_field.shape[0], 8, 3) + modulus.shape)
    summed = jnp.zeros_like(node_field)
    for corner in range(8):
        off_x, off_y, off_z = (corner // 4, corner // 2 % 2, corner % 2)
        summed = summed + jnp.pad(
            local_force[:, corner],
            ((0, 0), (0, 0), (off_x, 1 - off_x), (off_y, 1 - off_y), (off_z, 1 - off_z)),
        )
    return summed[..., :-1], local_disp, local_load


def on_device(start_disp, bone_mask, density, load_nodes, load_forces):
    stiffness = jnp.asarray(hex_stiffness(), jnp.float32)
    modulus = bone_mask.astype(jnp.float32) * density * density
    case_count = start_disp.shape[0]
    size_x = start_disp.shape[2]
    size_y = start_disp.shape[3]
    size_z = start_disp.shape[4]
    count_x = lax.axis_size("gx")
    count_y = lax.axis_size("gy")
    fields = case_count * 3

    slot_ids = jnp.arange(size_x * size_y, dtype=jnp.int32)
    matches = load_nodes[0, 0][:, None, :, None] == slot_ids
    top_plane = jnp.sum(
        jnp.where(matches, load_forces[0, 0][:, :, :, None], 0.0), axis=2
    ).reshape(fields, size_x, size_y)
    packed_loads = jnp.pad(top_plane.transpose(1, 2, 0), ((0, 0), (0, 0), (0, size_z - fields)))
    packed = jnp.concatenate(
        [start_disp.reshape(fields, size_x, size_y, size_z), modulus[None], packed_loads[None]],
        axis=0,
    )
    packed = halo_both(halo_both(packed, "gx", 1, 2), "gy", 2, 2)
    wide_start = packed[:fields].reshape(case_count, 3, size_x + 4, size_y + 4, size_z)
    wide_modulus = packed[fields]
    wide_loads = packed[fields + 1, 1:-1, 1:-1, :fields].transpose(2, 0, 1)
    wide_loads = wide_loads.reshape(case_count, 3, size_x + 2, size_y + 2)

    start_nodes = pad_upper_z(wide_start)
    forces, start_elems, start_loads = node_forces(
        start_nodes, wide_modulus[:-1, :-1], stiffness
    )
    applied = forces[:, :, 1:-1, 1:-1] + spring * wide_start[:, :, 1:-1, 1:-1]
    keep = (
        inside_mask("gx", size_x, 1, size_x * count_x)[:, None, None]
        * inside_mask("gy", size_y, 1, size_y * count_y)[None, :, None]
    )
    residual_wide = (
        jnp.concatenate(
            [-applied[..., :-1], (wide_loads - applied[..., -1])[..., None]], axis=4
        )
        * keep
    )

    residual_nodes = pad_upper_z(residual_wide)
    forces, residual_elems, residual_loads = node_forces(
        residual_nodes, wide_modulus[1:-2, 1:-2], stiffness
    )
    residual = residual_wide[:, :, 1:-1, 1:-1]
    applied = forces[:, :, 1:-1, 1:-1] + spring * residual

    blur_mass = modulus
    for dim, axis in ((0, "gx"), (1, "gy"), (2, None)):
        extent = modulus.shape[dim]
        count = 1 if axis is None else lax.axis_size(axis)
        places = lax.iota(jnp.int32, extent)
        if axis is not None:
            places = places + lax.axis_index(axis) * extent
        kept = jnp.zeros((extent,), jnp.float32)
        for tap_index, weight in enumerate(blur_weights()):
            shifted = places + 4 - tap_index
            kept = kept + jnp.where((shifted >= 0) & (shifted < extent * count), weight, 0.0)
        shape = [1, 1, 1]
        shape[dim] = extent
        blur_mass = blur_mass * kept.reshape(shape)
    start_elems = start_elems[:, :, 2:-1, 2:-1]
    start_loads = start_loads[:, :, 2:-1, 2:-1]
    residual_elems = residual_elems[:, :, 1:, 1:]
    residual_loads = residual_loads[:, :, 1:, 1:]
    start_energy = jnp.sum(start_elems * start_loads * blur_mass, axis=(1, 2, 3, 4))
    residual_scaled = residual_elems * blur_mass
    cross_energy = jnp.sum(
        residual_scaled[:, None] * start_loads[None, :], axis=(2, 3, 4, 5)
    )
    residual_energy = jnp.sum(
        residual_scaled[:, None] * residual_loads[None, :], axis=(2, 3, 4, 5)
    )
    grams = tree_sum(
        jnp.stack(
            [
                local_gram(residual, residual),
                local_gram(residual, applied),
                cross_energy,
                residual_energy,
                jnp.diag(start_energy),
            ]
        )
    )
    norm_now = grams[0]
    step_alpha = solve_spd(grams[1], norm_now)
    summed = (
        jnp.sum(grams[4])
        + 2.0 * jnp.sum(step_alpha * grams[2])
        + jnp.sum(step_alpha[:, None, :] * grams[3][:, :, None] * step_alpha[None, :, :])
    )
    solution = start_disp + mix_cases(residual, step_alpha)
    node_field = start_nodes[:, :, 2:-1, 2:-1] + mix_cases(
        residual_nodes[:, :, 1:, 1:], step_alpha
    )
    final_modes = corner_modes(node_field)
    final_loads = mode_loads(final_modes, mode_stiffness())
    energy = sum(
        jnp.sum(part * load, axis=(0, 1)) for part, load in zip(final_modes, final_loads)
    )
    stimulus = modulus * energy
    smooth = blur_valid(with_halo(stimulus, (("gx", 0),), 4), 0, size_x)
    smooth = blur_valid(with_halo(smooth, (("gy", 1),), 4), 1, size_y)
    smooth = blur_valid(jnp.pad(smooth, ((0, 0), (0, 0), (4, 4))), 2, size_z)
    mean_stim = summed / (size_x * size_y * size_z * count_x * count_y)
    new_density = jnp.minimum(density * (0.5 + 0.5 * smooth / (mean_stim + mean_eps)), density_cap)
    return (solution, new_density)


def solution(mesh):
    return jax.shard_map(
        on_device,
        mesh=mesh,
        in_specs=(
            P(None, None, "gx", "gy", None),
            P("gx", "gy", None),
            P("gx", "gy", None),
            P("gx", "gy", None, None),
            P("gx", "gy", None, None, None),
        ),
        out_specs=(P(None, None, "gx", "gy", None), P("gx", "gy", None)),
        check_vma=False,
    )
```

```python
import jax
import jax.numpy as jnp
import numpy as np
from jax import lax
from jax.sharding import PartitionSpec as P

spring = 0.1
poisson = 0.3
blur_sigma = 2.0
density_cap = 1.0
mean_eps = 1e-06
highest = lax.Precision.HIGHEST


def from_behind(block, axis, distance):
    devices = range(lax.axis_size(axis))
    route = [(i - distance, i) for i in devices if i - distance in devices]
    return lax.ppermute(block, axis, route)


def with_halo(cells, sides, width):
    for axis, dim in sides:
        count = lax.axis_size(axis)
        ends = count - 1
        head = lax.slice_in_dim(cells, 0, width, axis=dim)
        tail = lax.slice_in_dim(cells, cells.shape[dim] - width, cells.shape[dim], axis=dim)
        cells = jnp.concatenate(
            [
                lax.ppermute(tail, axis, [(i, (i + 1) % count) for i in range(ends)]),
                cells,
                lax.ppermute(head, axis, [((i + 1) % count, i) for i in range(ends)]),
            ],
            axis=dim,
        )
    return cells


def hex_stiffness():
    lame_first = poisson / ((1.0 + poisson) * (1.0 - 2.0 * poisson))
    shear_mod = 1.0 / (2.0 * (1.0 + poisson))
    elastic = np.zeros((6, 6))
    elastic[:3, :3] = lame_first
    for axis_id in range(3):
        elastic[axis_id, axis_id] = lame_first + 2.0 * shear_mod
        elastic[axis_id + 3, axis_id + 3] = shear_mod
    points = [0.5 - 0.5 / np.sqrt(3.0), 0.5 + 0.5 / np.sqrt(3.0)]
    stiffness = np.zeros((24, 24))
    for point_x in points:
        for point_y in points:
            for point_z in points:
                coords = (point_x, point_y, point_z)
                strain = np.zeros((6, 24))
                for corner in range(8):
                    offsets = (corner // 4, corner // 2 % 2, corner % 2)
                    shapes = [
                        coords[axis_id] if offsets[axis_id] == 1 else 1.0 - coords[axis_id]
                        for axis_id in range(3)
                    ]
                    slopes = [1.0 if offsets[axis_id] == 1 else -1.0 for axis_id in range(3)]
                    grad_x = slopes[0] * shapes[1] * shapes[2]
                    grad_y = shapes[0] * slopes[1] * shapes[2]
                    grad_z = shapes[0] * shapes[1] * slopes[2]
                    column = 3 * corner
                    strain[0, column] = grad_x
                    strain[1, column + 1] = grad_y
                    strain[2, column + 2] = grad_z
                    strain[3, column] = grad_y
                    strain[3, column + 1] = grad_x
                    strain[4, column + 1] = grad_z
                    strain[4, column + 2] = grad_y
                    strain[5, column] = grad_z
                    strain[5, column + 2] = grad_x
                stiffness += 0.125 * strain.T @ elastic @ strain
    return stiffness


def blur_weights():
    offsets = np.arange(9) - 4.0
    unscaled = np.exp(-offsets * offsets / (2.0 * blur_sigma * blur_sigma))
    return [float(entry) for entry in unscaled / unscaled.sum()]


def blur_valid(values, axis_id, extent):
    weights = blur_weights()
    summed = weights[0] * lax.slice_in_dim(values, 0, extent, axis=axis_id)
    for tap_index in range(1, 9):
        summed = summed + weights[tap_index] * lax.slice_in_dim(
            values, tap_index, tap_index + extent, axis=axis_id
        )
    return summed


def element_disp(node_field):
    size_x = node_field.shape[1] - 1
    size_y = node_field.shape[2] - 1
    size_z = node_field.shape[3] - 1
    corners = []
    for corner in range(8):
        off_x, off_y, off_z = (corner // 4, corner // 2 % 2, corner % 2)
        corners.append(
            node_field[:, off_x : off_x + size_x, off_y : off_y + size_y, off_z : off_z + size_z]
        )
    return jnp.stack(corners).reshape(24, size_x, size_y, size_z)


def cases_disp(node_field):
    size_x = node_field.shape[2] - 1
    size_y = node_field.shape[3] - 1
    size_z = node_field.shape[4] - 1
    corners = []
    for corner in range(8):
        off_x, off_y, off_z = (corner // 4, corner // 2 % 2, corner % 2)
        corners.append(
            node_field[:, :, off_x : off_x + size_x, off_y : off_y + size_y, off_z : off_z + size_z]
        )
    return jnp.stack(corners, axis=1).reshape(
        (node_field.shape[0], 24, size_x, size_y, size_z)
    )


def element_forces(node_field, modulus, stiffness):
    local_disp = cases_disp(node_field)
    local_force = jnp.einsum("ij,cjabd->ciabd", stiffness, local_disp, precision=highest) * modulus
    local_force = local_force.reshape((node_field.shape[0], 8, 3) + modulus.shape)
    summed = jnp.zeros_like(node_field)
    for corner in range(8):
        off_x, off_y, off_z = (corner // 4, corner // 2 % 2, corner % 2)
        summed = summed + jnp.pad(
            local_force[:, corner],
            ((0, 0), (0, 0), (off_x, 1 - off_x), (off_y, 1 - off_y), (off_z, 1 - off_z)),
        )
    return summed


def element_energy(node_field, stiffness):
    local_disp = cases_disp(node_field)
    local_force = jnp.einsum("ij,cjabd->ciabd", stiffness, local_disp, precision=highest)
    return jnp.sum(local_disp * local_force, axis=(0, 1))


def local_gram(left_field, right_field):
    return jnp.einsum("iabcd,jabcd->ij", left_field, right_field, precision=highest)


def tree_sum(value):
    for axis in ("gx", "gy"):
        count = lax.axis_size(axis)
        copies = jnp.broadcast_to(value[None], (count,) + value.shape)
        value = jnp.sum(lax.all_to_all(copies, axis, 0, 0, tiled=False), axis=0)
    return value


def mix_cases(field, coeffs):
    return jnp.sum(field[:, None] * coeffs[:, :, None, None, None, None], axis=0)


def solve_spd(matrix, rhs_matrix):
    factor = jnp.linalg.cholesky(matrix)
    forward = lax.linalg.triangular_solve(factor, rhs_matrix, left_side=True, lower=True)
    return lax.linalg.triangular_solve(
        factor, forward, left_side=True, lower=True, transpose_a=True
    )


def solve_spd_rows(matrix, rhs_matrix):
    factor = jnp.linalg.cholesky(matrix)
    matrix_order = matrix.shape[0]
    forward = []
    for row_index in range(matrix_order):
        partial_sum = rhs_matrix[row_index]
        for col_index in range(row_index):
            partial_sum = partial_sum - factor[row_index, col_index] * forward[col_index]
        forward.append(partial_sum / factor[row_index, row_index])
    backward = [None] * matrix_order
    for row_index in reversed(range(matrix_order)):
        partial_sum = forward[row_index]
        for col_index in range(row_index + 1, matrix_order):
            partial_sum = partial_sum - factor[col_index, row_index] * backward[col_index]
        backward[row_index] = partial_sum / factor[row_index, row_index]
    return jnp.stack(backward)


def pad_upper_z(field):
    return jnp.pad(field, ((0, 0), (0, 0), (0, 0), (0, 0), (0, 1)))


def gather_upper(field):
    from_x = from_behind(field[:, :, :1], "gx", -1)
    widened = jnp.concatenate([field, from_x], axis=2)
    from_y = from_behind(widened[:, :, :, :1], "gy", -1)
    return jnp.concatenate([widened, from_y], axis=3)


def return_lower(forces):
    size_x = forces.shape[2] - 1
    size_y = forces.shape[3] - 1
    to_y = from_behind(forces[:, :, :, size_y:], "gy", 1)
    kept = forces[:, :, :, :size_y]
    kept = jnp.concatenate([kept[:, :, :, :1] + to_y, kept[:, :, :, 1:]], axis=3)
    to_x = from_behind(kept[:, :, size_x:], "gx", 1)
    kept = kept[:, :, :size_x]
    return jnp.concatenate([kept[:, :, :1] + to_x, kept[:, :, 1:]], axis=2)


def corner_modes(node_field):
    found = {(): node_field}
    for dim in (2, 3, 4):
        grown = {}
        for key, cells in found.items():
            low = lax.slice_in_dim(cells, 0, cells.shape[dim] - 1, axis=dim)
            high = lax.slice_in_dim(cells, 1, cells.shape[dim], axis=dim)
            grown[key + (0,)] = high + low
            grown[key + (1,)] = high - low
        found = grown
    return [found[(mode // 4, mode // 2 % 2, mode % 2)] for mode in range(8)]


def mode_stiffness():
    step = np.array([[1.0, 1.0], [-1.0, 1.0]])
    change = np.kron(np.kron(np.kron(step, step), step), np.eye(3))
    return change @ hex_stiffness() @ change.T / 64.0


def mode_loads(modes, table):
    loads = []
    for mode in range(8):
        parts = []
        for comp in range(3):
            total = None
            for other in range(3):
                source = mode ^ (4 >> comp) ^ (4 >> other)
                weight = float(table[3 * mode + comp, 3 * source + other])
                if abs(weight) < 1e-12:
                    continue
                term = weight * modes[source][:, other]
                total = term if total is None else total + term
            parts.append(jnp.zeros_like(modes[mode][:, comp]) if total is None else total)
        loads.append(jnp.stack(parts, axis=1))
    return loads


def halo_both(cells, axis, dim, width):
    count = lax.axis_size(axis)
    head = lax.slice_in_dim(cells, 0, width, axis=dim)
    tail = lax.slice_in_dim(cells, cells.shape[dim] - width, cells.shape[dim], axis=dim)
    below = lax.ppermute(tail, axis, [(i, i + 1) for i in range(count - 1)])
    above = lax.ppermute(head, axis, [(i + 1, i) for i in range(count - 1)])
    return jnp.concatenate([below, cells, above], axis=dim)


def inside_mask(axis, extent, width, total):
    places = np.arange(extent + 2 * width) - width
    own = jnp.asarray(places, jnp.int32) + lax.axis_index(axis) * extent
    return ((own >= 0) & (own < total)).astype(jnp.float32)


def node_forces(node_field, modulus, stiffness):
    local_disp = cases_disp(node_field)
    local_load = jnp.einsum("ij,cjabd->ciabd", stiffness, local_disp, precision=highest)
    local_force = (local_load * modulus).reshape((node_field.shape[0], 8, 3) + modulus.shape)
    summed = jnp.zeros_like(node_field)
    for corner in range(8):
        off_x, off_y, off_z = (corner // 4, corner // 2 % 2, corner % 2)
        summed = summed + jnp.pad(
            local_force[:, corner],
            ((0, 0), (0, 0), (off_x, 1 - off_x), (off_y, 1 - off_y), (off_z, 1 - off_z)),
        )
    return summed[..., :-1], local_disp, local_load


def on_device(start_disp, bone_mask, density, load_nodes, load_forces):
    stiffness = jnp.asarray(hex_stiffness(), jnp.float32)
    modulus = bone_mask.astype(jnp.float32) * density * density
    case_count = start_disp.shape[0]
    size_x = start_disp.shape[2]
    size_y = start_disp.shape[3]
    size_z = start_disp.shape[4]
    count_x = lax.axis_size("gx")
    count_y = lax.axis_size("gy")
    fields = case_count * 3

    slot_ids = jnp.arange(size_x * size_y, dtype=jnp.int32)
    matches = (load_nodes[0, 0][:, :, None] == slot_ids).astype(jnp.float32)
    top_plane = jnp.einsum("cls,ckl->cks", matches, load_forces[0, 0], precision=highest).reshape(
        fields, size_x, size_y
    )
    packed_loads = jnp.pad(top_plane.transpose(1, 2, 0), ((0, 0), (0, 0), (0, size_z - fields)))
    packed = jnp.concatenate(
        [start_disp.reshape(fields, size_x, size_y, size_z), modulus[None], packed_loads[None]],
        axis=0,
    )
    packed = halo_both(halo_both(packed, "gx", 1, 2), "gy", 2, 2)
    wide_start = packed[:fields].reshape(case_count, 3, size_x + 4, size_y + 4, size_z)
    wide_modulus = packed[fields]
    wide_loads = packed[fields + 1, 1:-1, 1:-1, :fields].transpose(2, 0, 1)
    wide_loads = wide_loads.reshape(case_count, 3, size_x + 2, size_y + 2)

    start_nodes = pad_upper_z(wide_start)
    forces, start_elems, start_loads = node_forces(
        start_nodes, wide_modulus[:-1, :-1], stiffness
    )
    applied = forces[:, :, 1:-1, 1:-1] + spring * wide_start[:, :, 1:-1, 1:-1]
    keep = (
        inside_mask("gx", size_x, 1, size_x * count_x)[:, None, None]
        * inside_mask("gy", size_y, 1, size_y * count_y)[None, :, None]
    )
    residual_wide = (
        jnp.concatenate(
            [-applied[..., :-1], (wide_loads - applied[..., -1])[..., None]], axis=4
        )
        * keep
    )

    residual_nodes = pad_upper_z(residual_wide)
    forces, residual_elems, residual_loads = node_forces(
        residual_nodes, wide_modulus[1:-2, 1:-2], stiffness
    )
    residual = residual_wide[:, :, 1:-1, 1:-1]
    applied = forces[:, :, 1:-1, 1:-1] + spring * residual

    blur_mass = modulus
    for dim, axis in ((0, "gx"), (1, "gy"), (2, None)):
        extent = modulus.shape[dim]
        count = 1 if axis is None else lax.axis_size(axis)
        places = lax.iota(jnp.int32, extent)
        if axis is not None:
            places = places + lax.axis_index(axis) * extent
        kept = jnp.zeros((extent,), jnp.float32)
        for tap_index, weight in enumerate(blur_weights()):
            shifted = places + 4 - tap_index
            kept = kept + jnp.where((shifted >= 0) & (shifted < extent * count), weight, 0.0)
        shape = [1, 1, 1]
        shape[dim] = extent
        blur_mass = blur_mass * kept.reshape(shape)
    start_elems = start_elems[:, :, 2:-1, 2:-1]
    start_loads = start_loads[:, :, 2:-1, 2:-1]
    residual_elems = residual_elems[:, :, 1:, 1:]
    residual_loads = residual_loads[:, :, 1:, 1:]
    start_energy = jnp.sum(start_elems * start_loads * blur_mass, axis=(1, 2, 3, 4))
    residual_scaled = residual_elems * blur_mass
    cross_energy = jnp.sum(
        residual_scaled[:, None] * start_loads[None, :], axis=(2, 3, 4, 5)
    )
    residual_energy = jnp.sum(
        residual_scaled[:, None] * residual_loads[None, :], axis=(2, 3, 4, 5)
    )
    grams = tree_sum(
        jnp.stack(
            [
                local_gram(residual, residual),
                local_gram(residual, applied),
                cross_energy,
                residual_energy,
                jnp.diag(start_energy),
            ]
        )
    )
    norm_now = grams[0]
    step_alpha = solve_spd(grams[1], norm_now)
    summed = (
        jnp.sum(grams[4])
        + 2.0 * jnp.sum(step_alpha * grams[2])
        + jnp.sum(step_alpha[:, None, :] * grams[3][:, :, None] * step_alpha[None, :, :])
    )
    solution = start_disp + mix_cases(residual, step_alpha)
    node_field = start_nodes[:, :, 2:-1, 2:-1] + mix_cases(
        residual_nodes[:, :, 1:, 1:], step_alpha
    )
    final_modes = corner_modes(node_field)
    final_loads = mode_loads(final_modes, mode_stiffness())
    energy = sum(
        jnp.sum(part * load, axis=(0, 1)) for part, load in zip(final_modes, final_loads)
    )
    stimulus = modulus * energy
    smooth = blur_valid(with_halo(stimulus, (("gx", 0),), 4), 0, size_x)
    smooth = blur_valid(with_halo(smooth, (("gy", 1),), 4), 1, size_y)
    smooth = blur_valid(jnp.pad(smooth, ((0, 0), (0, 0), (4, 4))), 2, size_z)
    mean_stim = summed / (size_x * size_y * size_z * count_x * count_y)
    new_density = jnp.minimum(density * (0.5 + 0.5 * smooth / (mean_stim + mean_eps)), density_cap)
    return (solution, new_density)


def solution(mesh):
    return jax.shard_map(
        on_device,
        mesh=mesh,
        in_specs=(
            P(None, None, "gx", "gy", None),
            P("gx", "gy", None),
            P("gx", "gy", None),
            P("gx", "gy", None, None),
            P("gx", "gy", None, None, None),
        ),
        out_specs=(P(None, None, "gx", "gy", None), P("gx", "gy", None)),
        check_vma=False,
    )
```

```python
import jax
import jax.numpy as jnp
import numpy as np
from jax import lax
from jax.sharding import PartitionSpec as P

spring = 0.1
poisson = 0.3
blur_sigma = 2.0
density_cap = 1.0
mean_eps = 1e-06
highest = lax.Precision.HIGHEST


def from_behind(block, axis, distance):
    devices = range(lax.axis_size(axis))
    route = [(i - distance, i) for i in devices if i - distance in devices]
    return lax.ppermute(block, axis, route)


def with_halo(cells, sides, width):
    for axis, dim in sides:
        count = lax.axis_size(axis)
        ends = count - 1
        head = lax.slice_in_dim(cells, 0, width, axis=dim)
        tail = lax.slice_in_dim(cells, cells.shape[dim] - width, cells.shape[dim], axis=dim)
        cells = jnp.concatenate(
            [
                lax.ppermute(tail, axis, [(i, (i + 1) % count) for i in range(ends)]),
                cells,
                lax.ppermute(head, axis, [((i + 1) % count, i) for i in range(ends)]),
            ],
            axis=dim,
        )
    return cells


def hex_stiffness():
    lame_first = poisson / ((1.0 + poisson) * (1.0 - 2.0 * poisson))
    shear_mod = 1.0 / (2.0 * (1.0 + poisson))
    elastic = np.zeros((6, 6))
    elastic[:3, :3] = lame_first
    for axis_id in range(3):
        elastic[axis_id, axis_id] = lame_first + 2.0 * shear_mod
        elastic[axis_id + 3, axis_id + 3] = shear_mod
    points = [0.5 - 0.5 / np.sqrt(3.0), 0.5 + 0.5 / np.sqrt(3.0)]
    stiffness = np.zeros((24, 24))
    for point_x in points:
        for point_y in points:
            for point_z in points:
                coords = (point_x, point_y, point_z)
                strain = np.zeros((6, 24))
                for corner in range(8):
                    offsets = (corner // 4, corner // 2 % 2, corner % 2)
                    shapes = [
                        coords[axis_id] if offsets[axis_id] == 1 else 1.0 - coords[axis_id]
                        for axis_id in range(3)
                    ]
                    slopes = [1.0 if offsets[axis_id] == 1 else -1.0 for axis_id in range(3)]
                    grad_x = slopes[0] * shapes[1] * shapes[2]
                    grad_y = shapes[0] * slopes[1] * shapes[2]
                    grad_z = shapes[0] * shapes[1] * slopes[2]
                    column = 3 * corner
                    strain[0, column] = grad_x
                    strain[1, column + 1] = grad_y
                    strain[2, column + 2] = grad_z
                    strain[3, column] = grad_y
                    strain[3, column + 1] = grad_x
                    strain[4, column + 1] = grad_z
                    strain[4, column + 2] = grad_y
                    strain[5, column] = grad_z
                    strain[5, column + 2] = grad_x
                stiffness += 0.125 * strain.T @ elastic @ strain
    return stiffness


def blur_weights():
    offsets = np.arange(9) - 4.0
    unscaled = np.exp(-offsets * offsets / (2.0 * blur_sigma * blur_sigma))
    return [float(entry) for entry in unscaled / unscaled.sum()]


def blur_valid(values, axis_id, extent):
    weights = blur_weights()
    summed = weights[0] * lax.slice_in_dim(values, 0, extent, axis=axis_id)
    for tap_index in range(1, 9):
        summed = summed + weights[tap_index] * lax.slice_in_dim(
            values, tap_index, tap_index + extent, axis=axis_id
        )
    return summed


def element_disp(node_field):
    size_x = node_field.shape[1] - 1
    size_y = node_field.shape[2] - 1
    size_z = node_field.shape[3] - 1
    corners = []
    for corner in range(8):
        off_x, off_y, off_z = (corner // 4, corner // 2 % 2, corner % 2)
        corners.append(
            node_field[:, off_x : off_x + size_x, off_y : off_y + size_y, off_z : off_z + size_z]
        )
    return jnp.stack(corners).reshape(24, size_x, size_y, size_z)


def cases_disp(node_field):
    size_x = node_field.shape[2] - 1
    size_y = node_field.shape[3] - 1
    size_z = node_field.shape[4] - 1
    corners = []
    for corner in range(8):
        off_x, off_y, off_z = (corner // 4, corner // 2 % 2, corner % 2)
        corners.append(
            node_field[:, :, off_x : off_x + size_x, off_y : off_y + size_y, off_z : off_z + size_z]
        )
    return jnp.stack(corners, axis=1).reshape(
        (node_field.shape[0], 24, size_x, size_y, size_z)
    )


def element_forces(node_field, modulus, stiffness):
    local_disp = cases_disp(node_field)
    local_force = jnp.einsum("ij,cjabd->ciabd", stiffness, local_disp, precision=highest) * modulus
    local_force = local_force.reshape((node_field.shape[0], 8, 3) + modulus.shape)
    summed = jnp.zeros_like(node_field)
    for corner in range(8):
        off_x, off_y, off_z = (corner // 4, corner // 2 % 2, corner % 2)
        summed = summed + jnp.pad(
            local_force[:, corner],
            ((0, 0), (0, 0), (off_x, 1 - off_x), (off_y, 1 - off_y), (off_z, 1 - off_z)),
        )
    return summed


def element_energy(node_field, stiffness):
    local_disp = cases_disp(node_field)
    local_force = jnp.einsum("ij,cjabd->ciabd", stiffness, local_disp, precision=highest)
    return jnp.sum(local_disp * local_force, axis=(0, 1))


def local_gram(left_field, right_field):
    return jnp.sum(left_field[:, None] * right_field[None, :], axis=(2, 3, 4, 5))


def tree_sum(value):
    for axis in ("gx", "gy"):
        count = lax.axis_size(axis)
        copies = jnp.broadcast_to(value[None], (count,) + value.shape)
        value = jnp.sum(lax.all_to_all(copies, axis, 0, 0, tiled=False), axis=0)
    return value


def mix_cases(field, coeffs):
    return jnp.einsum("kabcd,kj->jabcd", field, coeffs, precision=highest)


def solve_spd(matrix, rhs_matrix):
    factor = jnp.linalg.cholesky(matrix)
    forward = lax.linalg.triangular_solve(factor, rhs_matrix, left_side=True, lower=True)
    return lax.linalg.triangular_solve(
        factor, forward, left_side=True, lower=True, transpose_a=True
    )


def solve_spd_rows(matrix, rhs_matrix):
    factor = jnp.linalg.cholesky(matrix)
    matrix_order = matrix.shape[0]
    forward = []
    for row_index in range(matrix_order):
        partial_sum = rhs_matrix[row_index]
        for col_index in range(row_index):
            partial_sum = partial_sum - factor[row_index, col_index] * forward[col_index]
        forward.append(partial_sum / factor[row_index, row_index])
    backward = [None] * matrix_order
    for row_index in reversed(range(matrix_order)):
        partial_sum = forward[row_index]
        for col_index in range(row_index + 1, matrix_order):
            partial_sum = partial_sum - factor[col_index, row_index] * backward[col_index]
        backward[row_index] = partial_sum / factor[row_index, row_index]
    return jnp.stack(backward)


def pad_upper_z(field):
    return jnp.pad(field, ((0, 0), (0, 0), (0, 0), (0, 0), (0, 1)))


def gather_upper(field):
    from_x = from_behind(field[:, :, :1], "gx", -1)
    widened = jnp.concatenate([field, from_x], axis=2)
    from_y = from_behind(widened[:, :, :, :1], "gy", -1)
    return jnp.concatenate([widened, from_y], axis=3)


def return_lower(forces):
    size_x = forces.shape[2] - 1
    size_y = forces.shape[3] - 1
    to_y = from_behind(forces[:, :, :, size_y:], "gy", 1)
    kept = forces[:, :, :, :size_y]
    kept = jnp.concatenate([kept[:, :, :, :1] + to_y, kept[:, :, :, 1:]], axis=3)
    to_x = from_behind(kept[:, :, size_x:], "gx", 1)
    kept = kept[:, :, :size_x]
    return jnp.concatenate([kept[:, :, :1] + to_x, kept[:, :, 1:]], axis=2)


def corner_modes(node_field):
    found = {(): node_field}
    for dim in (2, 3, 4):
        grown = {}
        for key, cells in found.items():
            low = lax.slice_in_dim(cells, 0, cells.shape[dim] - 1, axis=dim)
            high = lax.slice_in_dim(cells, 1, cells.shape[dim], axis=dim)
            grown[key + (0,)] = high + low
            grown[key + (1,)] = high - low
        found = grown
    return [found[(mode // 4, mode // 2 % 2, mode % 2)] for mode in range(8)]


def mode_stiffness():
    step = np.array([[1.0, 1.0], [-1.0, 1.0]])
    change = np.kron(np.kron(np.kron(step, step), step), np.eye(3))
    return change @ hex_stiffness() @ change.T / 64.0


def mode_loads(modes, table):
    loads = []
    for mode in range(8):
        parts = []
        for comp in range(3):
            total = None
            for other in range(3):
                source = mode ^ (4 >> comp) ^ (4 >> other)
                weight = float(table[3 * mode + comp, 3 * source + other])
                if abs(weight) < 1e-12:
                    continue
                term = weight * modes[source][:, other]
                total = term if total is None else total + term
            parts.append(jnp.zeros_like(modes[mode][:, comp]) if total is None else total)
        loads.append(jnp.stack(parts, axis=1))
    return loads


def halo_both(cells, axis, dim, width):
    count = lax.axis_size(axis)
    head = lax.slice_in_dim(cells, 0, width, axis=dim)
    tail = lax.slice_in_dim(cells, cells.shape[dim] - width, cells.shape[dim], axis=dim)
    below = lax.ppermute(tail, axis, [(i, i + 1) for i in range(count - 1)])
    above = lax.ppermute(head, axis, [(i + 1, i) for i in range(count - 1)])
    return jnp.concatenate([below, cells, above], axis=dim)


def inside_mask(axis, extent, width, total):
    places = np.arange(extent + 2 * width) - width
    own = jnp.asarray(places, jnp.int32) + lax.axis_index(axis) * extent
    return ((own >= 0) & (own < total)).astype(jnp.float32)


def node_forces(node_field, modulus, stiffness):
    local_disp = cases_disp(node_field)
    local_load = jnp.einsum("ij,cjabd->ciabd", stiffness, local_disp, precision=highest)
    local_force = (local_load * modulus).reshape((node_field.shape[0], 8, 3) + modulus.shape)
    summed = jnp.zeros_like(node_field)
    for corner in range(8):
        off_x, off_y, off_z = (corner // 4, corner // 2 % 2, corner % 2)
        summed = summed + jnp.pad(
            local_force[:, corner],
            ((0, 0), (0, 0), (off_x, 1 - off_x), (off_y, 1 - off_y), (off_z, 1 - off_z)),
        )
    return summed[..., :-1], local_disp, local_load


def on_device(start_disp, bone_mask, density, load_nodes, load_forces):
    stiffness = jnp.asarray(hex_stiffness(), jnp.float32)
    modulus = bone_mask.astype(jnp.float32) * density * density
    case_count = start_disp.shape[0]
    size_x = start_disp.shape[2]
    size_y = start_disp.shape[3]
    size_z = start_disp.shape[4]
    count_x = lax.axis_size("gx")
    count_y = lax.axis_size("gy")
    fields = case_count * 3

    slot_ids = jnp.arange(size_x * size_y, dtype=jnp.int32)
    matches = (load_nodes[0, 0][:, :, None] == slot_ids).astype(jnp.float32)
    top_plane = jnp.einsum("cls,ckl->cks", matches, load_forces[0, 0], precision=highest).reshape(
        fields, size_x, size_y
    )
    packed_loads = jnp.pad(top_plane.transpose(1, 2, 0), ((0, 0), (0, 0), (0, size_z - fields)))
    packed = jnp.concatenate(
        [start_disp.reshape(fields, size_x, size_y, size_z), modulus[None], packed_loads[None]],
        axis=0,
    )
    packed = halo_both(halo_both(packed, "gx", 1, 2), "gy", 2, 2)
    wide_start = packed[:fields].reshape(case_count, 3, size_x + 4, size_y + 4, size_z)
    wide_modulus = packed[fields]
    wide_loads = packed[fields + 1, 1:-1, 1:-1, :fields].transpose(2, 0, 1)
    wide_loads = wide_loads.reshape(case_count, 3, size_x + 2, size_y + 2)

    start_nodes = pad_upper_z(wide_start)
    forces, start_elems, start_loads = node_forces(
        start_nodes, wide_modulus[:-1, :-1], stiffness
    )
    applied = forces[:, :, 1:-1, 1:-1] + spring * wide_start[:, :, 1:-1, 1:-1]
    keep = (
        inside_mask("gx", size_x, 1, size_x * count_x)[:, None, None]
        * inside_mask("gy", size_y, 1, size_y * count_y)[None, :, None]
    )
    residual_wide = (
        jnp.concatenate(
            [-applied[..., :-1], (wide_loads - applied[..., -1])[..., None]], axis=4
        )
        * keep
    )

    residual_nodes = pad_upper_z(residual_wide)
    forces, residual_elems, residual_loads = node_forces(
        residual_nodes, wide_modulus[1:-2, 1:-2], stiffness
    )
    residual = residual_wide[:, :, 1:-1, 1:-1]
    applied = forces[:, :, 1:-1, 1:-1] + spring * residual

    blur_mass = modulus
    for dim, axis in ((0, "gx"), (1, "gy"), (2, None)):
        extent = modulus.shape[dim]
        count = 1 if axis is None else lax.axis_size(axis)
        places = lax.iota(jnp.int32, extent)
        if axis is not None:
            places = places + lax.axis_index(axis) * extent
        kept = jnp.zeros((extent,), jnp.float32)
        for tap_index, weight in enumerate(blur_weights()):
            shifted = places + 4 - tap_index
            kept = kept + jnp.where((shifted >= 0) & (shifted < extent * count), weight, 0.0)
        shape = [1, 1, 1]
        shape[dim] = extent
        blur_mass = blur_mass * kept.reshape(shape)
    start_elems = start_elems[:, :, 2:-1, 2:-1]
    start_loads = start_loads[:, :, 2:-1, 2:-1]
    residual_elems = residual_elems[:, :, 1:, 1:]
    residual_loads = residual_loads[:, :, 1:, 1:]
    start_energy = jnp.sum(start_elems * start_loads * blur_mass, axis=(1, 2, 3, 4))
    residual_scaled = residual_elems * blur_mass
    cross_energy = jnp.sum(
        residual_scaled[:, None] * start_loads[None, :], axis=(2, 3, 4, 5)
    )
    residual_energy = jnp.sum(
        residual_scaled[:, None] * residual_loads[None, :], axis=(2, 3, 4, 5)
    )
    grams = tree_sum(
        jnp.stack(
            [
                local_gram(residual, residual),
                local_gram(residual, applied),
                cross_energy,
                residual_energy,
                jnp.diag(start_energy),
            ]
        )
    )
    norm_now = grams[0]
    step_alpha = solve_spd(grams[1], norm_now)
    summed = (
        jnp.sum(grams[4])
        + 2.0 * jnp.sum(step_alpha * grams[2])
        + jnp.sum(step_alpha[:, None, :] * grams[3][:, :, None] * step_alpha[None, :, :])
    )
    solution = start_disp + mix_cases(residual, step_alpha)
    node_field = start_nodes[:, :, 2:-1, 2:-1] + mix_cases(
        residual_nodes[:, :, 1:, 1:], step_alpha
    )
    final_modes = corner_modes(node_field)
    final_loads = mode_loads(final_modes, mode_stiffness())
    energy = sum(
        jnp.sum(part * load, axis=(0, 1)) for part, load in zip(final_modes, final_loads)
    )
    stimulus = modulus * energy
    smooth = blur_valid(with_halo(stimulus, (("gx", 0),), 4), 0, size_x)
    smooth = blur_valid(with_halo(smooth, (("gy", 1),), 4), 1, size_y)
    smooth = blur_valid(jnp.pad(smooth, ((0, 0), (0, 0), (4, 4))), 2, size_z)
    mean_stim = summed / (size_x * size_y * size_z * count_x * count_y)
    new_density = jnp.minimum(density * (0.5 + 0.5 * smooth / (mean_stim + mean_eps)), density_cap)
    return (solution, new_density)


def solution(mesh):
    return jax.shard_map(
        on_device,
        mesh=mesh,
        in_specs=(
            P(None, None, "gx", "gy", None),
            P("gx", "gy", None),
            P("gx", "gy", None),
            P("gx", "gy", None, None),
            P("gx", "gy", None, None, None),
        ),
        out_specs=(P(None, None, "gx", "gy", None), P("gx", "gy", None)),
        check_vma=False,
    )
```
